32 devices in a mesh: grp: 4 (over x, core), ep: 8 (over z, y).
Axes of the slice: x: 2, y: 2, z: 4, core: 2. Of those that a mesh axis runs over, the one named last changes fastest.
Arguments:
- tokens: bfloat16 [2048, 5120], P('ep', 'grp'), may hold values from -6 to 6
- cotangent: bfloat16 [2048, 5120], P('ep', 'grp'), may hold values from -0.59765625 to 0.59765625
- gate_weights: bfloat16 [2048, 6], P('ep'), may hold values from 0.099609375 to 1
- expert_ids: int32 [2048, 6], P('ep'), may hold values from 0 to 159, all different within a row; in each aligned block of 256 rows (0 to 255, 256 to 511, ...) at most 16 rows name the same one
- hot_ids: int32 [2], replicated, may hold values from 8 to 159, as said below
- gate_cold: bfloat16 [8, 5120, 768], P('ep', 'grp'), may hold values from -0.078125 to 0.078125
- up_cold: bfloat16 [8, 5120, 768], P('ep', 'grp'), may hold values from -0.078125 to 0.078125
- down_cold: bfloat16 [8, 768, 5120], P('ep', None, 'grp'), may hold values from -0.21875 to 0.21875
- gate_hot: bfloat16 [2, 5120, 768], P(None, 'grp', 'ep'), may hold values from -0.078125 to 0.078125
- up_hot: bfloat16 [2, 5120, 768], P(None, 'grp', 'ep'), may hold values from -0.078125 to 0.078125
- down_hot: bfloat16 [2, 768, 5120], P(None, 'ep', 'grp'), may hold values from -0.21875 to 0.21875
Outputs:
- grad_gate_cold: bfloat16 [8, 5120, 768], P('ep', 'grp')
- grad_up_cold: bfloat16 [8, 5120, 768], P('ep', 'grp')
- grad_down_cold: bfloat16 [8, 768, 5120], P('ep', None, 'grp')
- grad_gate_hot: float32 [2, 5120, 768], P(None, 'grp', 'ep')
- grad_up_hot: float32 [2, 5120, 768], P(None, 'grp', 'ep')
- grad_down_hot: float32 [2, 768, 5120], P(None, 'ep', 'grp')
- gate_weight_grad: float32 [2048, 6], P('ep')
The draws below stay inside these ranges and needn't reach their ends.
Inputs may be any that keep to these rules, and one draw needn't show every extreme that they name: `expert_ids`: each row names 6 different experts. Among the routes of the 256 tokens of one index of ep (aligned blocks of rows) no expert is named more than 16 times, a bound that some block reaches. `hot_ids`: distinct expert numbers, none below 8; expert 160 - 1 is always among them.
All inputs are finite; a program needn't handle non-finite values.
Results may differ from the reference program's by a relative error of at most 0.02.
Values may be sent and summed in bfloat16 or wider, within the bound.
No kernel may reach another device: no remote copies, remote signals or barrier semaphores. Data moves between devices by JAX's collectives and lax.ppermute only.
A program may use at most 128 MiB of HBM per device.

```python
import math
import jax
import jax.numpy as jnp
import numpy as np
from jax import lax

D = 5120
ROUTED = 160
TOPK = 6
HIDDEN_SIZE = 768
TOK = 256
HOT = 2
CAP = 16
COLD = 8
TOKENS = 2048
N_GRP = 4


def draw_hot_ids(key, part):
    shuffled = jax.random.permutation(jax.random.fold_in(key, 11), ROUTED - COLD - 1)
    others = (shuffled[:HOT - 1] + COLD).astype(jnp.int32)
    listed = jnp.concatenate([jnp.full((1,), ROUTED - 1, jnp.int32), others])
    order = jax.random.permutation(jax.random.fold_in(key, 23), HOT)
    return listed[order].astype(jnp.int32)


def levels(stream_key, shape, cuts, smallest, largest):
    gain = 1.0
    for dim, parts in cuts:
        heights = jax.random.uniform(jax.random.fold_in(jax.random.fold_in(stream_key, 6), dim), (parts,), jnp.float32, smallest / len(cuts), largest / len(cuts))
        gain = gain * jnp.repeat(jnp.exp(heights), shape[dim] // parts).reshape((-1,) + (1,) * (len(shape) - 1 - dim))
    return gain


def routed_block(stream_key, own, number, rows, amount, top, reach, skew):
    order = jax.random.permutation(stream_key, amount)
    packed, common = shares(amount, rows * top, reach, skew, True), shares(amount, rows * top, reach, skew, False)
    places = jnp.arange(amount)

    def named(sizes, turn):
        used = int((sizes > 0).sum())
        fixed = max(1, used // 4)
        shifted = fixed + (places - fixed + turn * (used - fixed)) % max(1, amount - fixed)
        return jnp.zeros((amount,), jnp.int32).at[order[jnp.where(places < fixed, places, shifted)]].set(jnp.asarray(sizes, jnp.int32))

    sizes = jnp.where(number % 4 == 0, named(packed, number // 4), named(common, number - number // 4 - 1))
    mixed = jax.random.permutation(jax.random.fold_in(own, 3), amount)
    giver, sink = mixed[0:amount // 2 * 2:2], mixed[1:amount // 2 * 2:2]
    slack = jnp.minimum(sizes[giver] - 1, reach - sizes[sink]) // 2
    slack = jnp.where((giver == order[0]) | (sink == order[0]) | (sizes[sink] == 0), 0, jnp.maximum(slack, 0))
    shifted = jax.random.randint(jax.random.fold_in(own, 4), (amount // 2,), 0, 1 << 20) % (slack + 1)
    sizes = sizes.at[giver].add(-shifted).at[sink].add(shifted)
    items = jnp.searchsorted(jnp.cumsum(sizes), jnp.arange(rows * top), side="right").astype(jnp.int32)
    table = items.reshape(top, rows).T
    table = table[jax.random.permutation(jax.random.fold_in(own, 1), rows)]
    turn = jax.random.randint(jax.random.fold_in(own, 2), (rows, 1), 0, top)
    return jnp.take_along_axis(table, (jnp.arange(top)[None, :] + turn) % top, axis=1)


def shares(amount, total, bound, skew, full):
    portions = [(1 << 20) // math.isqrt(standing ** skew) + 1 for standing in range(1, amount + 1)]
    largest = bound if full else min(bound, max(-(-total // amount), total * portions[0] // sum(portions)))
    least = 1 if total - largest >= amount - 1 else 0
    counts, spare = [largest] + [least] * (amount - 1), total - largest - least * (amount - 1)
    while spare > 0:
        movable = [i for i in range(1, amount) if counts[i] < largest] or [i for i in range(1, amount) if counts[i] < bound]
        whole, left = sum([portions[i] for i in movable]), spare
        for i in movable:
            more = min(bound - counts[i], max(1, left * portions[i] // whole), spare)
            counts[i] = counts[i] + more
            spare = spare - more
    return np.array(counts)


def bell_draw(key, shape, deviation, limit, split=(), held_as=jnp.bfloat16):
    entries = jax.random.normal(key, shape, jnp.float32) * deviation
    if len(split) > 0:
        entries = levels(key, shape, split, -0.22, 0.18) * entries
    return jnp.clip(entries, min=-limit, max=limit).astype(held_as)


def setup_inputs(seed: int = 0) -> dict:
    arg_keys = jax.random.split(jax.random.key(seed), 12)
    tokens = bell_draw(arg_keys[0], (TOKENS, D), 1.0, 6.0, ((0, 8), (1, 4)))
    cotangent = bell_draw(arg_keys[1], (TOKENS, D), 0.1, 0.59765625, ((0, 8), (1, 4)))
    gate_weights = jnp.clip(jnp.exp(math.log(1.0) - 2.306499 * jax.random.uniform(arg_keys[2], (TOKENS, TOPK), jnp.float32) ** levels(arg_keys[2], (TOKENS, TOPK), ((0, 8),), -0.2, 0.2)), 0.099609375, 1.0).astype(jnp.bfloat16)
    expert_ids_keys = jax.random.split(jax.random.fold_in(arg_keys[3], 1), TOKENS // TOK)
    expert_ids_turns = jax.random.permutation(jax.random.fold_in(arg_keys[3], 3), TOKENS // TOK)
    expert_ids = jax.vmap(lambda own, number: routed_block(jax.random.fold_in(arg_keys[3], 2), own, number, TOK, ROUTED, TOPK, CAP, 2))(expert_ids_keys, expert_ids_turns).reshape((TOKENS, TOPK))
    hot_ids = draw_hot_ids(jax.random.fold_in(arg_keys[11], 71), 0)
    gate_cold = bell_draw(arg_keys[5], (COLD, D, HIDDEN_SIZE), D ** -0.5, 0.078125, ((0, 8), (1, 4)))
    up_cold = bell_draw(arg_keys[6], (COLD, D, HIDDEN_SIZE), D ** -0.5, 0.078125, ((0, 8), (1, 4)))
    down_cold = bell_draw(arg_keys[7], (COLD, HIDDEN_SIZE, D), HIDDEN_SIZE ** -0.5, 0.21875, ((0, 8), (2, 4)))
    gate_hot = bell_draw(arg_keys[8], (HOT, D, HIDDEN_SIZE), D ** -0.5, 0.078125, ((1, 4), (2, 8)))
    up_hot = bell_draw(arg_keys[9], (HOT, D, HIDDEN_SIZE), D ** -0.5, 0.078125, ((1, 4), (2, 8)))
    down_hot = bell_draw(arg_keys[10], (HOT, HIDDEN_SIZE, D), HIDDEN_SIZE ** -0.5, 0.21875, ((1, 8), (2, 4)))
    return {"tokens": tokens, "cotangent": cotangent, "gate_weights": gate_weights, "expert_ids": expert_ids, "hot_ids": hot_ids, "gate_cold": gate_cold, "up_cold": up_cold, "down_cold": down_cold, "gate_hot": gate_hot, "up_hot": up_hot, "down_hot": down_hot}


def sliced_sum(operand, weights):
    groups = N_GRP
    slice_width = operand.shape[1] // groups
    lhs_float = operand.astype(jnp.float32).reshape(operand.shape[0], groups, slice_width)
    rhs_float = weights.astype(jnp.float32).reshape(groups, slice_width, weights.shape[1])
    pieces = jnp.einsum('rgd,gdh->grh', lhs_float, rhs_float)
    rounded = lax.optimization_barrier(pieces.astype(jnp.bfloat16))
    return jnp.sum(rounded.astype(jnp.float32), axis=0)


def expert_rows(feat_rows, cotan_rows, scale_rows, w_gate, w_up, w_down):
    weighted = (scale_rows[:, None] * cotan_rows.astype(jnp.float32)).astype(jnp.bfloat16)
    pre_gate = sliced_sum(feat_rows, w_gate)
    pre_up = sliced_sum(feat_rows, w_up)
    grad_hidden = sliced_sum(weighted, w_down.T)
    sigmoid_gate = jax.nn.sigmoid(pre_gate)
    activated = pre_gate * sigmoid_gate
    hidden = (activated * pre_up).astype(jnp.bfloat16)
    back_gate = (grad_hidden * pre_up * sigmoid_gate * (1.0 + pre_gate * (1.0 - sigmoid_gate))).astype(jnp.bfloat16)
    back_up = (grad_hidden * activated).astype(jnp.bfloat16)
    output_rows = jnp.dot(hidden, w_down, preferred_element_type=jnp.float32)
    route_grads = jnp.sum(output_rows * cotan_rows.astype(jnp.float32), axis=1)
    grad_gate = jnp.dot(feat_rows.T, back_gate, preferred_element_type=jnp.float32)
    grad_up = jnp.dot(feat_rows.T, back_up, preferred_element_type=jnp.float32)
    grad_down = jnp.dot(hidden.T, weighted, preferred_element_type=jnp.float32)
    return grad_gate, grad_up, grad_down, route_grads


def pick_rows(route_mask, row_count, tokens, cotangent, flat_weights):
    picked = jnp.nonzero(route_mask, size=row_count, fill_value=0)[0].astype(jnp.int32)
    usable = jnp.arange(row_count, dtype=jnp.int32) < jnp.sum(route_mask.astype(jnp.int32))
    token_of = picked // TOPK
    feat_rows = jnp.where(usable[:, None], tokens[token_of], jnp.zeros((), tokens.dtype))
    cotan_rows = jnp.where(usable[:, None], cotangent[token_of], jnp.zeros((), cotangent.dtype))
    scale_rows = jnp.where(usable, flat_weights[picked].astype(jnp.float32), jnp.zeros((), jnp.float32))
    return picked, usable, feat_rows, cotan_rows, scale_rows


def reference(tokens, cotangent, gate_weights, expert_ids, hot_ids, gate_cold, up_cold, down_cold, gate_hot, up_hot, down_hot):
    flat_ids = expert_ids.reshape(-1)
    flat_weights = gate_weights.reshape(-1)
    route_total = flat_ids.shape[0]

    def cold_expert(inputs):
        expert, w_gate, w_up, w_down = inputs
        picked, usable, feat_rows, cotan_rows, scale_rows = pick_rows(flat_ids == expert, COLD * CAP, tokens, cotangent, flat_weights)
        grad_gate, grad_up, grad_down, route_grads = expert_rows(feat_rows, cotan_rows, scale_rows, w_gate, w_up, w_down)
        kept = jnp.where(usable, route_grads, jnp.zeros((), route_grads.dtype))
        return grad_gate.astype(jnp.bfloat16), grad_up.astype(jnp.bfloat16), grad_down.astype(jnp.bfloat16), picked, kept

    cold_out = lax.map(cold_expert, (jnp.arange(COLD, dtype=jnp.int32), gate_cold, up_cold, down_cold))
    route_flat = jnp.zeros((route_total,), jnp.float32)
    route_flat = route_flat.at[cold_out[3].reshape(-1)].add(cold_out[4].reshape(-1))

    source_of = jnp.arange(route_total, dtype=jnp.int32) // (TOK * TOPK)
    gate_list, up_list, down_list = [], [], []
    for hot_index in range(HOT):
        w_gate = gate_hot[hot_index]
        w_up = up_hot[hot_index]
        w_down = down_hot[hot_index]
        target = hot_ids[hot_index]

        def per_source(carry, source):
            route_mask = (flat_ids == target) & (source_of == source)
            picked, usable, feat_rows, cotan_rows, scale_rows = pick_rows(route_mask, CAP, tokens, cotangent, flat_weights)
            grad_gate, grad_up, grad_down, route_grads = expert_rows(feat_rows, cotan_rows, scale_rows, w_gate, w_up, w_down)
            rounded = lax.optimization_barrier((grad_gate.astype(jnp.bfloat16), grad_up.astype(jnp.bfloat16), grad_down.astype(jnp.bfloat16)))
            new_carry = (carry[0] + rounded[0].astype(jnp.float32), carry[1] + rounded[1].astype(jnp.float32), carry[2] + rounded[2].astype(jnp.float32))
            kept = jnp.where(usable, route_grads, jnp.zeros((), route_grads.dtype))
            return new_carry, (picked, kept)

        start = (jnp.zeros((D, HIDDEN_SIZE), jnp.float32), jnp.zeros((D, HIDDEN_SIZE), jnp.float32), jnp.zeros((HIDDEN_SIZE, D), jnp.float32))
        totals, scattered = lax.scan(per_source, start, jnp.arange(COLD, dtype=jnp.int32))
        route_flat = route_flat.at[scattered[0].reshape(-1)].add(scattered[1].reshape(-1))
        gate_list.append(totals[0])
        up_list.append(totals[1])
        down_list.append(totals[2])

    gate_weight_grad = route_flat.reshape(TOKENS, TOPK)
    return (cold_out[0], cold_out[1], cold_out[2], jnp.stack(gate_list), jnp.stack(up_list), jnp.stack(down_list), gate_weight_grad)
```

```python
import jax
import jax.numpy as jnp
from jax import lax
from jax.sharding import PartitionSpec as P


def route_table(flat_ids, targets, capacity):
    matches = (flat_ids[:, None] == targets[None, :]).astype(jnp.int32)
    rank_of = jnp.cumsum(matches, axis=0) - 1
    slot_of = jnp.sum(matches * rank_of, axis=1)
    owner_of = jnp.sum(matches * jnp.arange(targets.shape[0], dtype=jnp.int32)[None, :], axis=1)
    usable = jnp.sum(matches, axis=1) > 0
    row_of = owner_of * capacity + slot_of
    rows_total = targets.shape[0] * capacity
    route_map = (row_of[None, :] == jnp.arange(rows_total, dtype=jnp.int32)[:, None]) & usable[
        None, :
    ]
    return route_map.astype(jnp.float32)


def gather_rows(route_map, tokens, cotangent, flat_weights, tok_rows, top_count):
    per_token = jnp.sum(route_map.reshape(route_map.shape[0], tok_rows, top_count), axis=2)
    token_map = per_token.astype(jnp.bfloat16)
    feat_rows = jnp.dot(token_map, tokens, preferred_element_type=jnp.float32).astype(jnp.bfloat16)
    cotan_rows = jnp.dot(token_map, cotangent, preferred_element_type=jnp.float32).astype(
        jnp.bfloat16
    )
    scale_rows = jnp.dot(
        route_map, flat_weights.astype(jnp.float32), precision=lax.Precision.HIGHEST
    )
    return (feat_rows, cotan_rows, scale_rows.astype(jnp.bfloat16))


def swiglu_back(pre_gate, pre_up, grad_hidden):
    sigmoid_gate = jax.nn.sigmoid(pre_gate)
    activated = pre_gate * sigmoid_gate
    hidden = (activated * pre_up).astype(jnp.bfloat16)
    back_gate = (
        grad_hidden * pre_up * sigmoid_gate * (1.0 + pre_gate * (1.0 - sigmoid_gate))
    ).astype(jnp.bfloat16)
    back_up = (grad_hidden * activated).astype(jnp.bfloat16)
    return (hidden, back_gate, back_up)


def body(
    tokens,
    cotangent,
    gate_weights,
    expert_ids,
    hot_ids,
    gate_cold,
    up_cold,
    down_cold,
    gate_hot,
    up_hot,
    down_hot,
):
    tok_rows, slice_width = tokens.shape
    top_count = expert_ids.shape[1]
    cold_count = lax.axis_size("ep")
    hot_count = hot_ids.shape[0]
    capacity = tok_rows // 16
    flat_ids = expert_ids.reshape(-1)
    flat_weights = gate_weights.reshape(-1)
    cold_map = route_table(flat_ids, jnp.arange(cold_count, dtype=jnp.int32), capacity)
    hot_map = route_table(flat_ids, hot_ids, capacity)
    cold_feats, cold_cotan, cold_scale = gather_rows(
        cold_map, tokens, cotangent, flat_weights, tok_rows, top_count
    )
    hot_feats, hot_cotan, hot_scale = gather_rows(
        hot_map, tokens, cotangent, flat_weights, tok_rows, top_count
    )
    outgoing = (
        cold_feats.reshape(cold_count, capacity, slice_width),
        cold_cotan.reshape(cold_count, capacity, slice_width),
        cold_scale.reshape(cold_count, capacity),
    )
    recv_feats, recv_cotan, recv_scale = (
        lax.all_to_all(outgoing[0], "ep", split_axis=0, concat_axis=0, tiled=True),
        lax.all_to_all(outgoing[1], "ep", split_axis=0, concat_axis=0, tiled=True),
        lax.all_to_all(outgoing[2], "ep", split_axis=0, concat_axis=0, tiled=True),
    )
    recv_feats = recv_feats.reshape(-1, slice_width)
    recv_cotan = recv_cotan.reshape(-1, slice_width)
    weighted = (
        recv_scale.reshape(-1).astype(jnp.float32)[:, None] * recv_cotan.astype(jnp.float32)
    ).astype(jnp.bfloat16)
    w_gate = gate_cold[0]
    w_up = up_cold[0]
    w_down = down_cold[0]
    part_gate = jnp.dot(recv_feats, w_gate, preferred_element_type=jnp.float32)
    part_up = jnp.dot(recv_feats, w_up, preferred_element_type=jnp.float32)
    part_hidden = lax.dot_general(
        weighted, w_down, (((1,), (1,)), ((), ())), preferred_element_type=jnp.float32
    )
    pre_gate, pre_up, grad_hidden = (
        lax.psum(part_gate.astype(jnp.bfloat16), "grp").astype(jnp.float32),
        lax.psum(part_up.astype(jnp.bfloat16), "grp").astype(jnp.float32),
        lax.psum(part_hidden.astype(jnp.bfloat16), "grp").astype(jnp.float32),
    )
    hidden, back_gate, back_up = swiglu_back(pre_gate, pre_up, grad_hidden)
    output_slice = jnp.dot(hidden, w_down, preferred_element_type=jnp.float32)
    cold_route = jnp.sum(output_slice * recv_cotan.astype(jnp.float32), axis=1)
    contract_rows = (((0,), (0,)), ((), ()))
    grad_gate_cold = lax.dot_general(
        recv_feats, back_gate, contract_rows, preferred_element_type=jnp.float32
    )
    grad_up_cold = lax.dot_general(
        recv_feats, back_up, contract_rows, preferred_element_type=jnp.float32
    )
    grad_down_cold = lax.dot_general(
        hidden, weighted, contract_rows, preferred_element_type=jnp.float32
    )
    hot_weighted_local = (
        hot_scale.astype(jnp.float32)[:, None] * hot_cotan.astype(jnp.float32)
    ).astype(jnp.bfloat16)
    blocks = lax.axis_size("ep")
    stacked = jnp.stack([hot_feats, hot_cotan, hot_weighted_local])
    all_rows = lax.all_gather(stacked, "ep", axis=1, tiled=False)
    all_rows = all_rows.reshape(3, blocks, hot_count, capacity, slice_width)
    all_rows = jnp.transpose(all_rows, (0, 2, 1, 3, 4)).reshape(
        3, hot_count, blocks * capacity, slice_width
    )
    rows_feat, rows_cot, rows_wt = all_rows[0], all_rows[1], all_rows[2]
    part_gate_hot = jnp.einsum(
        "jrd,jdh->jrh", rows_feat, gate_hot, preferred_element_type=jnp.float32
    )
    part_up_hot = jnp.einsum("jrd,jdh->jrh", rows_feat, up_hot, preferred_element_type=jnp.float32)
    part_hidden_hot = jnp.einsum(
        "jrd,jhd->jrh", rows_wt, down_hot, preferred_element_type=jnp.float32
    )
    cot_down = jnp.einsum("jrd,jhd->jrh", rows_cot, down_hot, preferred_element_type=jnp.float32)
    hot_parts = lax.psum(
        jnp.stack([part_gate_hot, part_up_hot, part_hidden_hot]).astype(jnp.bfloat16), "grp"
    ).astype(jnp.float32)
    hidden_hot, back_gate_hot, back_up_hot = swiglu_back(hot_parts[0], hot_parts[1], hot_parts[2])
    hot_route_part = jnp.sum(hidden_hot.astype(jnp.float32) * cot_down, axis=2)
    hidden_blk = hidden_hot.shape[2]
    feat_b = rows_feat.reshape(hot_count, blocks, capacity, slice_width)
    wt_b = rows_wt.reshape(hot_count, blocks, capacity, slice_width)
    bg_b = back_gate_hot.reshape(hot_count, blocks, capacity, hidden_blk)
    bu_b = back_up_hot.reshape(hot_count, blocks, capacity, hidden_blk)
    hid_b = hidden_hot.reshape(hot_count, blocks, capacity, hidden_blk)
    blk_gate = jnp.einsum("jbcd,jbch->jbdh", feat_b, bg_b, preferred_element_type=jnp.float32)
    blk_up = jnp.einsum("jbcd,jbch->jbdh", feat_b, bu_b, preferred_element_type=jnp.float32)
    blk_down = jnp.einsum("jbch,jbcd->jbhd", hid_b, wt_b, preferred_element_type=jnp.float32)
    grad_gate_hot = jnp.sum(blk_gate.astype(jnp.bfloat16).astype(jnp.float32), axis=1)
    grad_up_hot = jnp.sum(blk_up.astype(jnp.bfloat16).astype(jnp.float32), axis=1)
    grad_down_hot = jnp.sum(blk_down.astype(jnp.bfloat16).astype(jnp.float32), axis=1)
    hot_route_all = lax.psum(hot_route_part, ("grp", "ep"))
    me = lax.axis_index("ep")
    hot_route = lax.dynamic_index_in_dim(
        hot_route_all.reshape(hot_count, blocks, capacity), me, axis=1, keepdims=False
    )
    cold_route = lax.psum(cold_route, "grp")
    cold_back = lax.all_to_all(
        cold_route.reshape(cold_count, capacity), "ep", split_axis=0, concat_axis=0, tiled=True
    )
    route_flat = jnp.dot(cold_back.reshape(-1), cold_map, precision=lax.Precision.HIGHEST)
    route_flat = route_flat + jnp.dot(
        hot_route.reshape(-1), hot_map, precision=lax.Precision.HIGHEST
    )
    gate_weight_grad = route_flat.reshape(tok_rows, top_count)
    return (
        grad_gate_cold[None].astype(jnp.bfloat16),
        grad_up_cold[None].astype(jnp.bfloat16),
        grad_down_cold[None].astype(jnp.bfloat16),
        grad_gate_hot,
        grad_up_hot,
        grad_down_hot,
        gate_weight_grad,
    )


def solution(mesh):
    in_specs = (
        P("ep", "grp"),
        P("ep", "grp"),
        P("ep", None),
        P("ep", None),
        P(),
        P("ep", "grp", None),
        P("ep", "grp", None),
        P("ep", None, "grp"),
        P(None, "grp", "ep"),
        P(None, "grp", "ep"),
        P(None, "ep", "grp"),
    )
    out_specs = (
        P("ep", "grp", None),
        P("ep", "grp", None),
        P("ep", None, "grp"),
        P(None, "grp", "ep"),
        P(None, "grp", "ep"),
        P(None, "ep", "grp"),
        P("ep", None),
    )
    return jax.shard_map(body, mesh=mesh, in_specs=in_specs, out_specs=out_specs, check_vma=False)
```

```python
import jax
import jax.numpy as jnp
from jax import lax
from jax.sharding import PartitionSpec as P


def route_table(flat_ids, targets, capacity):
    matches = (flat_ids[:, None] == targets[None, :]).astype(jnp.int32)
    rank_of = jnp.cumsum(matches, axis=0) - 1
    slot_of = jnp.sum(matches * rank_of, axis=1)
    owner_of = jnp.sum(matches * jnp.arange(targets.shape[0], dtype=jnp.int32)[None, :], axis=1)
    usable = jnp.sum(matches, axis=1) > 0
    row_of = owner_of * capacity + slot_of
    rows_total = targets.shape[0] * capacity
    route_map = (row_of[None, :] == jnp.arange(rows_total, dtype=jnp.int32)[:, None]) & usable[
        None, :
    ]
    return route_map.astype(jnp.float32)


def gather_rows(route_map, tokens, cotangent, flat_weights, tok_rows, top_count):
    per_token = jnp.sum(route_map.reshape(route_map.shape[0], tok_rows, top_count), axis=2)
    token_map = per_token.astype(jnp.bfloat16)
    feat_rows = jnp.dot(token_map, tokens, preferred_element_type=jnp.float32).astype(jnp.bfloat16)
    cotan_rows = jnp.dot(token_map, cotangent, preferred_element_type=jnp.float32).astype(
        jnp.bfloat16
    )
    scale_rows = jnp.dot(
        route_map, flat_weights.astype(jnp.float32), precision=lax.Precision.HIGHEST
    )
    return (feat_rows, cotan_rows, scale_rows.astype(jnp.bfloat16))


def swiglu_back(pre_gate, pre_up, grad_hidden):
    sigmoid_gate = jax.nn.sigmoid(pre_gate)
    activated = pre_gate * sigmoid_gate
    hidden = (activated * pre_up).astype(jnp.bfloat16)
    back_gate = (
        grad_hidden * pre_up * sigmoid_gate * (1.0 + pre_gate * (1.0 - sigmoid_gate))
    ).astype(jnp.bfloat16)
    back_up = (grad_hidden * activated).astype(jnp.bfloat16)
    return (hidden, back_gate, back_up)


def body(
    tokens,
    cotangent,
    gate_weights,
    expert_ids,
    hot_ids,
    gate_cold,
    up_cold,
    down_cold,
    gate_hot,
    up_hot,
    down_hot,
):
    tok_rows, slice_width = tokens.shape
    top_count = expert_ids.shape[1]
    cold_count = lax.axis_size("ep")
    hot_count = hot_ids.shape[0]
    capacity = tok_rows // 16
    flat_ids = expert_ids.reshape(-1)
    flat_weights = gate_weights.reshape(-1)
    cold_map = route_table(flat_ids, jnp.arange(cold_count, dtype=jnp.int32), capacity)
    hot_map = route_table(flat_ids, hot_ids, capacity)
    cold_feats, cold_cotan, cold_scale = gather_rows(
        cold_map, tokens, cotangent, flat_weights, tok_rows, top_count
    )
    hot_feats, hot_cotan, hot_scale = gather_rows(
        hot_map, tokens, cotangent, flat_weights, tok_rows, top_count
    )
    cold_weighted = (
        cold_scale.astype(jnp.float32)[:, None] * cold_cotan.astype(jnp.float32)
    ).astype(jnp.bfloat16)
    outgoing = jnp.stack(
        [
            cold_feats.reshape(cold_count, capacity, slice_width),
            cold_cotan.reshape(cold_count, capacity, slice_width),
            cold_weighted.reshape(cold_count, capacity, slice_width),
        ],
        axis=1,
    )
    received = lax.all_to_all(outgoing, "ep", split_axis=0, concat_axis=0, tiled=True)
    recv_feats = received[:, 0].reshape(-1, slice_width)
    recv_cotan = received[:, 1].reshape(-1, slice_width)
    weighted = received[:, 2].reshape(-1, slice_width)
    w_gate = gate_cold[0]
    w_up = up_cold[0]
    w_down = down_cold[0]
    part_gate = jnp.dot(recv_feats, w_gate, preferred_element_type=jnp.float32)
    part_up = jnp.dot(recv_feats, w_up, preferred_element_type=jnp.float32)
    part_hidden = lax.dot_general(
        weighted, w_down, (((1,), (1,)), ((), ())), preferred_element_type=jnp.float32
    )
    pre_gate, pre_up, grad_hidden = (
        lax.psum(part_gate.astype(jnp.bfloat16), "grp").astype(jnp.float32),
        lax.psum(part_up.astype(jnp.bfloat16), "grp").astype(jnp.float32),
        lax.psum(part_hidden.astype(jnp.bfloat16), "grp").astype(jnp.float32),
    )
    hidden, back_gate, back_up = swiglu_back(pre_gate, pre_up, grad_hidden)
    output_slice = jnp.dot(hidden, w_down, preferred_element_type=jnp.float32)
    cold_route = jnp.sum(output_slice * recv_cotan.astype(jnp.float32), axis=1)
    contract_rows = (((0,), (0,)), ((), ()))
    grad_gate_cold = lax.dot_general(
        recv_feats, back_gate, contract_rows, preferred_element_type=jnp.float32
    )
    grad_up_cold = lax.dot_general(
        recv_feats, back_up, contract_rows, preferred_element_type=jnp.float32
    )
    grad_down_cold = lax.dot_general(
        hidden, weighted, contract_rows, preferred_element_type=jnp.float32
    )
    blocks = lax.axis_size("ep")
    all_rows = lax.all_gather(jnp.stack([hot_feats, hot_cotan]), "ep", axis=1, tiled=False)
    all_rows = all_rows.reshape(2, blocks, hot_count, capacity, slice_width)
    all_rows = jnp.transpose(all_rows, (0, 2, 1, 3, 4)).reshape(
        2, hot_count, blocks * capacity, slice_width
    )
    all_scale = lax.all_gather(hot_scale, "ep", axis=0, tiled=False)
    all_scale = jnp.transpose(all_scale.reshape(blocks, hot_count, capacity), (1, 0, 2))
    rows_feat, rows_cot = all_rows[0], all_rows[1]
    rows_wt = (
        all_scale.reshape(hot_count, blocks * capacity, 1).astype(jnp.float32)
        * rows_cot.astype(jnp.float32)
    ).astype(jnp.bfloat16)
    part_gate_hot = jnp.einsum(
        "jrd,jdh->jrh", rows_feat, gate_hot, preferred_element_type=jnp.float32
    )
    part_up_hot = jnp.einsum("jrd,jdh->jrh", rows_feat, up_hot, preferred_element_type=jnp.float32)
    part_hidden_hot = jnp.einsum(
        "jrd,jhd->jrh", rows_wt, down_hot, preferred_element_type=jnp.float32
    )
    cot_down = jnp.einsum("jrd,jhd->jrh", rows_cot, down_hot, preferred_element_type=jnp.float32)
    hot_parts = lax.psum(
        jnp.stack([part_gate_hot, part_up_hot, part_hidden_hot]).astype(jnp.bfloat16), "grp"
    ).astype(jnp.float32)
    hidden_hot, back_gate_hot, back_up_hot = swiglu_back(hot_parts[0], hot_parts[1], hot_parts[2])
    hot_route_part = jnp.sum(hidden_hot.astype(jnp.float32) * cot_down, axis=2)
    hidden_blk = hidden_hot.shape[2]
    feat_b = rows_feat.reshape(hot_count, blocks, capacity, slice_width)
    wt_b = rows_wt.reshape(hot_count, blocks, capacity, slice_width)
    bg_b = back_gate_hot.reshape(hot_count, blocks, capacity, hidden_blk)
    bu_b = back_up_hot.reshape(hot_count, blocks, capacity, hidden_blk)
    hid_b = hidden_hot.reshape(hot_count, blocks, capacity, hidden_blk)
    blk_gate = jnp.einsum("jbcd,jbch->jbdh", feat_b, bg_b, preferred_element_type=jnp.float32)
    blk_up = jnp.einsum("jbcd,jbch->jbdh", feat_b, bu_b, preferred_element_type=jnp.float32)
    blk_down = jnp.einsum("jbch,jbcd->jbhd", hid_b, wt_b, preferred_element_type=jnp.float32)
    grad_gate_hot = jnp.sum(blk_gate.astype(jnp.bfloat16).astype(jnp.float32), axis=1)
    grad_up_hot = jnp.sum(blk_up.astype(jnp.bfloat16).astype(jnp.float32), axis=1)
    grad_down_hot = jnp.sum(blk_down.astype(jnp.bfloat16).astype(jnp.float32), axis=1)
    route_parts = jnp.concatenate(
        [
            cold_route.reshape(cold_count, 1, capacity),
            jnp.transpose(hot_route_part.reshape(hot_count, blocks, capacity), (1, 0, 2)),
        ],
        axis=1,
    )
    route_parts = lax.psum(route_parts, "grp")
    route_back = lax.all_to_all(route_parts, "ep", split_axis=0, concat_axis=0, tiled=True)
    cold_back = route_back[:, 0, :]
    hot_route = jnp.sum(route_back[:, 1:, :], axis=0)
    route_flat = jnp.dot(cold_back.reshape(-1), cold_map, precision=lax.Precision.HIGHEST)
    route_flat = route_flat + jnp.dot(
        hot_route.reshape(-1), hot_map, precision=lax.Precision.HIGHEST
    )
    gate_weight_grad = route_flat.reshape(tok_rows, top_count)
    return (
        grad_gate_cold[None].astype(jnp.bfloat16),
        grad_up_cold[None].astype(jnp.bfloat16),
        grad_down_cold[None].astype(jnp.bfloat16),
        grad_gate_hot,
        grad_up_hot,
        grad_down_hot,
        gate_weight_grad,
    )


def solution(mesh):
    in_specs = (
        P("ep", "grp"),
        P("ep", "grp"),
        P("ep", None),
        P("ep", None),
        P(),
        P("ep", "grp", None),
        P("ep", "grp", None),
        P("ep", None, "grp"),
        P(None, "grp", "ep"),
        P(None, "grp", "ep"),
        P(None, "ep", "grp"),
    )
    out_specs = (
        P("ep", "grp", None),
        P("ep", "grp", None),
        P("ep", None, "grp"),
        P(None, "grp", "ep"),
        P(None, "grp", "ep"),
        P(None, "ep", "grp"),
        P("ep", None),
    )
    return jax.shard_map(body, mesh=mesh, in_specs=in_specs, out_specs=out_specs, check_vma=False)
```

```python
import jax
import jax.numpy as jnp
from jax import lax
from jax.sharding import PartitionSpec as P


def route_table(flat_ids, targets, capacity):
    matches = (flat_ids[:, None] == targets[None, :]).astype(jnp.int32)
    rank_of = jnp.cumsum(matches, axis=0) - 1
    slot_of = jnp.sum(matches * rank_of, axis=1)
    owner_of = jnp.sum(matches * jnp.arange(targets.shape[0], dtype=jnp.int32)[None, :], axis=1)
    usable = jnp.sum(matches, axis=1) > 0
    row_of = owner_of * capacity + slot_of
    rows_total = targets.shape[0] * capacity
    route_map = (row_of[None, :] == jnp.arange(rows_total, dtype=jnp.int32)[:, None]) & usable[
        None, :
    ]
    return route_map.astype(jnp.float32)


def gather_rows(route_map, tokens, cotangent, flat_weights, tok_rows, top_count):
    per_token = jnp.sum(route_map.reshape(route_map.shape[0], tok_rows, top_count), axis=2)
    token_map = per_token.astype(jnp.bfloat16)
    feat_rows = jnp.dot(token_map, tokens, preferred_element_type=jnp.float32).astype(jnp.bfloat16)
    cotan_rows = jnp.dot(token_map, cotangent, preferred_element_type=jnp.float32).astype(
        jnp.bfloat16
    )
    scale_rows = jnp.dot(
        route_map, flat_weights.astype(jnp.float32), precision=lax.Precision.HIGHEST
    )
    return (feat_rows, cotan_rows, scale_rows.astype(jnp.bfloat16))


def swiglu_back(pre_gate, pre_up, grad_hidden):
    sigmoid_gate = jax.nn.sigmoid(pre_gate)
    activated = pre_gate * sigmoid_gate
    hidden = (activated * pre_up).astype(jnp.bfloat16)
    back_gate = (
        grad_hidden * pre_up * sigmoid_gate * (1.0 + pre_gate * (1.0 - sigmoid_gate))
    ).astype(jnp.bfloat16)
    back_up = (grad_hidden * activated).astype(jnp.bfloat16)
    return (hidden, back_gate, back_up)


def grp_sum_f32(x, axis_name):
    size = lax.axis_size(axis_name)
    if size & (size - 1):
        return lax.psum(x, axis_name)
    bit = 1
    while bit < size:
        partner = [(i, i ^ bit) for i in range(size)]
        x = x + lax.ppermute(x, axis_name, partner)
        bit *= 2
    return x


def body(
    tokens,
    cotangent,
    gate_weights,
    expert_ids,
    hot_ids,
    gate_cold,
    up_cold,
    down_cold,
    gate_hot,
    up_hot,
    down_hot,
):
    tok_rows, slice_width = tokens.shape
    top_count = expert_ids.shape[1]
    cold_count = lax.axis_size("ep")
    hot_count = hot_ids.shape[0]
    capacity = tok_rows // 16
    flat_ids = expert_ids.reshape(-1)
    flat_weights = gate_weights.reshape(-1)
    cold_map = route_table(flat_ids, jnp.arange(cold_count, dtype=jnp.int32), capacity)
    hot_map = route_table(flat_ids, hot_ids, capacity)
    hot_feats, hot_cotan, hot_scale = gather_rows(
        hot_map, tokens, cotangent, flat_weights, tok_rows, top_count
    )
    hot_rows = hot_count * capacity
    scale_lines = -(-hot_rows // slice_width)
    scale_lines = -(-scale_lines // 8) * 8
    scale_block = jnp.pad(hot_scale, (0, scale_lines * slice_width - hot_rows)).reshape(
        scale_lines, slice_width
    )
    blocks = lax.axis_size("ep")
    gathered = lax.all_gather(
        jnp.concatenate([hot_feats, hot_cotan, scale_block], axis=0), "ep", axis=0, tiled=False
    )
    cold_feats, cold_cotan, cold_scale = gather_rows(
        cold_map, tokens, cotangent, flat_weights, tok_rows, top_count
    )
    cold_weighted = (
        cold_scale.astype(jnp.float32)[:, None] * cold_cotan.astype(jnp.float32)
    ).astype(jnp.bfloat16)
    outgoing = jnp.stack(
        [
            cold_feats.reshape(cold_count, capacity, slice_width),
            cold_cotan.reshape(cold_count, capacity, slice_width),
            cold_weighted.reshape(cold_count, capacity, slice_width),
        ],
        axis=1,
    )
    received = lax.all_to_all(outgoing, "ep", split_axis=0, concat_axis=0, tiled=True)
    recv_feats = received[:, 0].reshape(-1, slice_width)
    recv_cotan = received[:, 1].reshape(-1, slice_width)
    weighted = received[:, 2].reshape(-1, slice_width)
    w_gate = gate_cold[0]
    w_up = up_cold[0]
    w_down = down_cold[0]
    part_gate = jnp.dot(recv_feats, w_gate, preferred_element_type=jnp.float32)
    part_up = jnp.dot(recv_feats, w_up, preferred_element_type=jnp.float32)
    part_hidden = lax.dot_general(
        weighted, w_down, (((1,), (1,)), ((), ())), preferred_element_type=jnp.float32
    )
    pre_gate, pre_up, grad_hidden = (
        lax.psum(part_gate.astype(jnp.bfloat16), "grp").astype(jnp.float32),
        lax.psum(part_up.astype(jnp.bfloat16), "grp").astype(jnp.float32),
        lax.psum(part_hidden.astype(jnp.bfloat16), "grp").astype(jnp.float32),
    )
    hidden, back_gate, back_up = swiglu_back(pre_gate, pre_up, grad_hidden)
    output_slice = jnp.dot(hidden, w_down, preferred_element_type=jnp.float32)
    cold_route = jnp.sum(output_slice * recv_cotan.astype(jnp.float32), axis=1)
    contract_rows = (((0,), (0,)), ((), ()))
    grad_gate_cold = lax.dot_general(
        recv_feats, back_gate, contract_rows, preferred_element_type=jnp.float32
    )
    grad_up_cold = lax.dot_general(
        recv_feats, back_up, contract_rows, preferred_element_type=jnp.float32
    )
    grad_down_cold = lax.dot_general(
        hidden, weighted, contract_rows, preferred_element_type=jnp.float32
    )
    all_rows = gathered[:, : 2 * hot_rows].reshape(blocks, 2, hot_count, capacity, slice_width)
    all_rows = jnp.transpose(all_rows, (1, 2, 0, 3, 4)).reshape(
        2, hot_count, blocks * capacity, slice_width
    )
    all_scale = gathered[:, 2 * hot_rows :].reshape(blocks, -1)[:, :hot_rows]
    all_scale = jnp.transpose(all_scale.reshape(blocks, hot_count, capacity), (1, 0, 2))
    rows_feat, rows_cot = all_rows[0], all_rows[1]
    rows_wt = (
        all_scale.reshape(hot_count, blocks * capacity, 1).astype(jnp.float32)
        * rows_cot.astype(jnp.float32)
    ).astype(jnp.bfloat16)
    part_gate_hot = jnp.einsum(
        "jrd,jdh->jrh", rows_feat, gate_hot, preferred_element_type=jnp.float32
    )
    part_up_hot = jnp.einsum("jrd,jdh->jrh", rows_feat, up_hot, preferred_element_type=jnp.float32)
    part_hidden_hot = jnp.einsum(
        "jrd,jhd->jrh", rows_wt, down_hot, preferred_element_type=jnp.float32
    )
    cot_down = jnp.einsum("jrd,jhd->jrh", rows_cot, down_hot, preferred_element_type=jnp.float32)
    hot_parts = lax.psum(
        jnp.stack([part_gate_hot, part_up_hot, part_hidden_hot]).astype(jnp.bfloat16), "grp"
    ).astype(jnp.float32)
    hidden_hot, back_gate_hot, back_up_hot = swiglu_back(hot_parts[0], hot_parts[1], hot_parts[2])
    hot_route_part = jnp.sum(hidden_hot.astype(jnp.float32) * cot_down, axis=2)
    hidden_blk = hidden_hot.shape[2]
    feat_b = rows_feat.reshape(hot_count, blocks, capacity, slice_width)
    wt_b = rows_wt.reshape(hot_count, blocks, capacity, slice_width)
    bg_b = back_gate_hot.reshape(hot_count, blocks, capacity, hidden_blk)
    bu_b = back_up_hot.reshape(hot_count, blocks, capacity, hidden_blk)
    hid_b = hidden_hot.reshape(hot_count, blocks, capacity, hidden_blk)
    blk_gate = jnp.einsum("jbcd,jbch->jbdh", feat_b, bg_b, preferred_element_type=jnp.float32)
    blk_up = jnp.einsum("jbcd,jbch->jbdh", feat_b, bu_b, preferred_element_type=jnp.float32)
    blk_down = jnp.einsum("jbch,jbcd->jbhd", hid_b, wt_b, preferred_element_type=jnp.float32)
    grad_gate_hot = jnp.sum(blk_gate.astype(jnp.bfloat16).astype(jnp.float32), axis=1)
    grad_up_hot = jnp.sum(blk_up.astype(jnp.bfloat16).astype(jnp.float32), axis=1)
    grad_down_hot = jnp.sum(blk_down.astype(jnp.bfloat16).astype(jnp.float32), axis=1)
    route_parts = jnp.concatenate(
        [
            cold_route.reshape(cold_count, 1, capacity),
            jnp.transpose(hot_route_part.reshape(hot_count, blocks, capacity), (1, 0, 2)),
        ],
        axis=1,
    )
    route_parts = grp_sum_f32(route_parts, "grp")
    route_back = lax.all_to_all(route_parts, "ep", split_axis=0, concat_axis=0, tiled=True)
    cold_back = route_back[:, 0, :]
    hot_route = jnp.sum(route_back[:, 1:, :], axis=0)
    route_flat = jnp.dot(cold_back.reshape(-1), cold_map, precision=lax.Precision.HIGHEST)
    route_flat = route_flat + jnp.dot(
        hot_route.reshape(-1), hot_map, precision=lax.Precision.HIGHEST
    )
    gate_weight_grad = route_flat.reshape(tok_rows, top_count)
    return (
        grad_gate_cold[None].astype(jnp.bfloat16),
        grad_up_cold[None].astype(jnp.bfloat16),
        grad_down_cold[None].astype(jnp.bfloat16),
        grad_gate_hot,
        grad_up_hot,
        grad_down_hot,
        gate_weight_grad,
    )


def solution(mesh):
    in_specs = (
        P("ep", "grp"),
        P("ep", "grp"),
        P("ep", None),
        P("ep", None),
        P(),
        P("ep", "grp", None),
        P("ep", "grp", None),
        P("ep", None, "grp"),
        P(None, "grp", "ep"),
        P(None, "grp", "ep"),
        P(None, "ep", "grp"),
    )
    out_specs = (
        P("ep", "grp", None),
        P("ep", "grp", None),
        P("ep", None, "grp"),
        P(None, "grp", "ep"),
        P(None, "grp", "ep"),
        P(None, "ep", "grp"),
        P("ep", None),
    )
    return jax.shard_map(body, mesh=mesh, in_specs=in_specs, out_specs=out_specs, check_vma=False)
```

```python
import jax
import jax.numpy as jnp
from jax import lax
from jax.sharding import PartitionSpec as P


def route_table(flat_ids, targets, capacity):
    matches = (flat_ids[:, None] == targets[None, :]).astype(jnp.int32)
    rank_of = jnp.cumsum(matches, axis=0) - 1
    slot_of = jnp.sum(matches * rank_of, axis=1)
    owner_of = jnp.sum(matches * jnp.arange(targets.shape[0], dtype=jnp.int32)[None, :], axis=1)
    usable = jnp.sum(matches, axis=1) > 0
    row_of = owner_of * capacity + slot_of
    rows_total = targets.shape[0] * capacity
    route_map = (row_of[None, :] == jnp.arange(rows_total, dtype=jnp.int32)[:, None]) & usable[
        None, :
    ]
    return route_map.astype(jnp.float32)


def gather_rows(route_map, tokens, cotangent, flat_weights, tok_rows, top_count):
    per_token = jnp.sum(route_map.reshape(route_map.shape[0], tok_rows, top_count), axis=2)
    token_map = per_token.astype(jnp.bfloat16)
    feat_rows = jnp.dot(token_map, tokens, preferred_element_type=jnp.float32).astype(jnp.bfloat16)
    cotan_rows = jnp.dot(token_map, cotangent, preferred_element_type=jnp.float32).astype(
        jnp.bfloat16
    )
    scale_rows = jnp.dot(
        route_map, flat_weights.astype(jnp.float32), precision=lax.Precision.HIGHEST
    )
    return (feat_rows, cotan_rows, scale_rows.astype(jnp.bfloat16))


def swiglu_back(pre_gate, pre_up, grad_hidden):
    sigmoid_gate = jax.nn.sigmoid(pre_gate)
    activated = pre_gate * sigmoid_gate
    hidden = (activated * pre_up).astype(jnp.bfloat16)
    back_gate = (
        grad_hidden * pre_up * sigmoid_gate * (1.0 + pre_gate * (1.0 - sigmoid_gate))
    ).astype(jnp.bfloat16)
    back_up = (grad_hidden * activated).astype(jnp.bfloat16)
    return (hidden, back_gate, back_up)


def grp_sum_f32(x, axis_name):
    size = lax.axis_size(axis_name)
    if size & (size - 1):
        return lax.psum(x, axis_name)
    bit = 1
    while bit < size:
        partner = [(i, i ^ bit) for i in range(size)]
        x = x + lax.ppermute(x, axis_name, partner)
        bit *= 2
    return x


def grp_sum_rounded(parts, axes, axis_name):
    size = lax.axis_size(axis_name)
    rounded = [p.astype(jnp.bfloat16) for p in parts]
    if size == 1:
        return [r.astype(jnp.float32) for r in rounded]
    if size & (size - 1) or any(p.shape[a] % 2 for p, a in zip(parts, axes)):
        return [lax.psum(r, axis_name).astype(jnp.float32) for r in rounded]
    half_of = [p.shape[a] // 2 for p, a in zip(parts, axes)]
    core = lax.axis_index(axis_name) % 2
    keep = [
        lax.dynamic_slice_in_dim(r, core * h, h, axis=a) for r, h, a in zip(rounded, half_of, axes)
    ]
    send = [
        lax.dynamic_slice_in_dim(r, (1 - core) * h, h, axis=a)
        for r, h, a in zip(rounded, half_of, axes)
    ]
    swap = [(i, i ^ 1) for i in range(size)]
    got = lax.ppermute(send, axis_name, swap)
    sums = [k.astype(jnp.float32) + g.astype(jnp.float32) for k, g in zip(keep, got)]
    bit = 2
    while bit < size:
        partner = [(i, i ^ bit) for i in range(size)]
        mine = [s.astype(jnp.bfloat16) for s in sums]
        got = lax.ppermute(mine, axis_name, partner)
        sums = [m.astype(jnp.float32) + g.astype(jnp.float32) for m, g in zip(mine, got)]
        bit *= 2
    other = lax.ppermute(sums, axis_name, swap)
    full = []
    for s, o, a in zip(sums, other, axes):
        pair = jnp.stack([s, o])
        first = lax.dynamic_index_in_dim(pair, core, axis=0, keepdims=False)
        second = lax.dynamic_index_in_dim(pair, 1 - core, axis=0, keepdims=False)
        full.append(jnp.concatenate([first, second], axis=a))
    return full


def body(
    tokens,
    cotangent,
    gate_weights,
    expert_ids,
    hot_ids,
    gate_cold,
    up_cold,
    down_cold,
    gate_hot,
    up_hot,
    down_hot,
):
    tok_rows, slice_width = tokens.shape
    top_count = expert_ids.shape[1]
    cold_count = lax.axis_size("ep")
    hot_count = hot_ids.shape[0]
    capacity = tok_rows // 16
    flat_ids = expert_ids.reshape(-1)
    flat_weights = gate_weights.reshape(-1)
    cold_map = route_table(flat_ids, jnp.arange(cold_count, dtype=jnp.int32), capacity)
    hot_map = route_table(flat_ids, hot_ids, capacity)
    hot_feats, hot_cotan, hot_scale = gather_rows(
        hot_map, tokens, cotangent, flat_weights, tok_rows, top_count
    )
    hot_rows = hot_count * capacity
    scale_lines = -(-hot_rows // slice_width)
    scale_lines = -(-scale_lines // 8) * 8
    scale_block = jnp.pad(hot_scale, (0, scale_lines * slice_width - hot_rows)).reshape(
        scale_lines, slice_width
    )
    blocks = lax.axis_size("ep")
    gathered = lax.all_gather(
        jnp.concatenate([hot_feats, hot_cotan, scale_block], axis=0), "ep", axis=0, tiled=False
    )
    cold_feats, cold_cotan, cold_scale = gather_rows(
        cold_map, tokens, cotangent, flat_weights, tok_rows, top_count
    )
    cold_lines = -(-capacity // slice_width)
    cold_lines = -(-cold_lines // 8) * 8
    cold_scale_block = jnp.pad(
        cold_scale.reshape(cold_count, capacity),
        ((0, 0), (0, cold_lines * slice_width - capacity)),
    ).reshape(cold_count, cold_lines, slice_width)
    outgoing = jnp.concatenate(
        [
            cold_feats.reshape(cold_count, capacity, slice_width),
            cold_cotan.reshape(cold_count, capacity, slice_width),
            cold_scale_block,
        ],
        axis=1,
    )
    received = lax.all_to_all(outgoing, "ep", split_axis=0, concat_axis=0, tiled=True)
    recv_feats = received[:, :capacity].reshape(-1, slice_width)
    recv_cotan = received[:, capacity : 2 * capacity].reshape(-1, slice_width)
    recv_scale = received[:, 2 * capacity :].reshape(cold_count, -1)[:, :capacity]
    weighted = (
        recv_scale.reshape(-1, 1).astype(jnp.float32) * recv_cotan.astype(jnp.float32)
    ).astype(jnp.bfloat16)
    w_gate = gate_cold[0]
    w_up = up_cold[0]
    w_down = down_cold[0]
    part_gate = jnp.dot(recv_feats, w_gate, preferred_element_type=jnp.float32)
    part_up = jnp.dot(recv_feats, w_up, preferred_element_type=jnp.float32)
    part_hidden = lax.dot_general(
        weighted, w_down, (((1,), (1,)), ((), ())), preferred_element_type=jnp.float32
    )
    all_rows = gathered[:, : 2 * hot_rows].reshape(blocks, 2, hot_count, capacity, slice_width)
    all_rows = jnp.transpose(all_rows, (1, 2, 0, 3, 4)).reshape(
        2, hot_count, blocks * capacity, slice_width
    )
    all_scale = gathered[:, 2 * hot_rows :].reshape(blocks, -1)[:, :hot_rows]
    all_scale = jnp.transpose(all_scale.reshape(blocks, hot_count, capacity), (1, 0, 2))
    rows_feat, rows_cot = all_rows[0], all_rows[1]
    rows_wt = (
        all_scale.reshape(hot_count, blocks * capacity, 1).astype(jnp.float32)
        * rows_cot.astype(jnp.float32)
    ).astype(jnp.bfloat16)
    part_gate_hot = jnp.einsum(
        "jrd,jdh->jrh", rows_feat, gate_hot, preferred_element_type=jnp.float32
    )
    part_up_hot = jnp.einsum("jrd,jdh->jrh", rows_feat, up_hot, preferred_element_type=jnp.float32)
    part_hidden_hot = jnp.einsum(
        "jrd,jhd->jrh", rows_wt, down_hot, preferred_element_type=jnp.float32
    )
    cot_down = jnp.einsum("jrd,jhd->jrh", rows_cot, down_hot, preferred_element_type=jnp.float32)
    (pre_gate, pre_up, grad_hidden, pre_gate_hot, pre_up_hot, grad_hidden_hot) = grp_sum_rounded(
        [part_gate, part_up, part_hidden, part_gate_hot, part_up_hot, part_hidden_hot],
        [0, 0, 0, 1, 1, 1],
        "grp",
    )
    hidden, back_gate, back_up = swiglu_back(pre_gate, pre_up, grad_hidden)
    output_slice = jnp.dot(hidden, w_down, preferred_element_type=jnp.float32)
    cold_route = jnp.sum(output_slice * recv_cotan.astype(jnp.float32), axis=1)
    contract_rows = (((0,), (0,)), ((), ()))
    grad_gate_cold = lax.dot_general(
        recv_feats, back_gate, contract_rows, preferred_element_type=jnp.float32
    )
    grad_up_cold = lax.dot_general(
        recv_feats, back_up, contract_rows, preferred_element_type=jnp.float32
    )
    grad_down_cold = lax.dot_general(
        hidden, weighted, contract_rows, preferred_element_type=jnp.float32
    )
    hidden_hot, back_gate_hot, back_up_hot = swiglu_back(pre_gate_hot, pre_up_hot, grad_hidden_hot)
    hot_route_part = jnp.sum(hidden_hot.astype(jnp.float32) * cot_down, axis=2)
    hidden_blk = hidden_hot.shape[2]
    feat_b = rows_feat.reshape(hot_count, blocks, capacity, slice_width)
    wt_b = rows_wt.reshape(hot_count, blocks, capacity, slice_width)
    bg_b = back_gate_hot.reshape(hot_count, blocks, capacity, hidden_blk)
    bu_b = back_up_hot.reshape(hot_count, blocks, capacity, hidden_blk)
    hid_b = hidden_hot.reshape(hot_count, blocks, capacity, hidden_blk)
    blk_gate = jnp.einsum("jbcd,jbch->jbdh", feat_b, bg_b, preferred_element_type=jnp.float32)
    blk_up = jnp.einsum("jbcd,jbch->jbdh", feat_b, bu_b, preferred_element_type=jnp.float32)
    blk_down = jnp.einsum("jbch,jbcd->jbhd", hid_b, wt_b, preferred_element_type=jnp.float32)
    grad_gate_hot = jnp.sum(blk_gate.astype(jnp.bfloat16).astype(jnp.float32), axis=1)
    grad_up_hot = jnp.sum(blk_up.astype(jnp.bfloat16).astype(jnp.float32), axis=1)
    grad_down_hot = jnp.sum(blk_down.astype(jnp.bfloat16).astype(jnp.float32), axis=1)
    route_parts = jnp.concatenate(
        [
            cold_route.reshape(cold_count, 1, capacity),
            jnp.transpose(hot_route_part.reshape(hot_count, blocks, capacity), (1, 0, 2)),
        ],
        axis=1,
    )
    route_parts = grp_sum_f32(route_parts, "grp")
    route_back = lax.all_to_all(route_parts, "ep", split_axis=0, concat_axis=0, tiled=True)
    cold_back = route_back[:, 0, :]
    hot_route = jnp.sum(route_back[:, 1:, :], axis=0)
    route_flat = jnp.dot(cold_back.reshape(-1), cold_map, precision=lax.Precision.HIGHEST)
    route_flat = route_flat + jnp.dot(
        hot_route.reshape(-1), hot_map, precision=lax.Precision.HIGHEST
    )
    gate_weight_grad = route_flat.reshape(tok_rows, top_count)
    return (
        grad_gate_cold[None].astype(jnp.bfloat16),
        grad_up_cold[None].astype(jnp.bfloat16),
        grad_down_cold[None].astype(jnp.bfloat16),
        grad_gate_hot,
        grad_up_hot,
        grad_down_hot,
        gate_weight_grad,
    )


def solution(mesh):
    in_specs = (
        P("ep", "grp"),
        P("ep", "grp"),
        P("ep", None),
        P("ep", None),
        P(),
        P("ep", "grp", None),
        P("ep", "grp", None),
        P("ep", None, "grp"),
        P(None, "grp", "ep"),
        P(None, "grp", "ep"),
        P(None, "ep", "grp"),
    )
    out_specs = (
        P("ep", "grp", None),
        P("ep", "grp", None),
        P("ep", None, "grp"),
        P(None, "grp", "ep"),
        P(None, "grp", "ep"),
        P(None, "ep", "grp"),
        P("ep", None),
    )
    return jax.shard_map(body, mesh=mesh, in_specs=in_specs, out_specs=out_specs, check_vma=False)
```

```python
import jax
import jax.numpy as jnp
from jax import lax
from jax.sharding import PartitionSpec as P


def token_table(expert_ids, targets, capacity):
    hit = expert_ids[:, :, None] == targets[None, None, :]
    tok_hit = jnp.any(hit, axis=1)
    rank = jnp.cumsum(tok_hit.astype(jnp.int32), axis=0) - 1
    slots = jnp.arange(capacity, dtype=jnp.int32)
    sel = (rank[None, :, :] == slots[:, None, None]) & tok_hit[None, :, :]
    return hit, sel


def gather_rows(hit, sel, tokens, cotangent, gate_weights):
    count, capacity = sel.shape[2], sel.shape[0]
    token_map = jnp.transpose(sel, (2, 0, 1)).reshape(count * capacity, -1).astype(jnp.bfloat16)
    feat_rows = jnp.dot(token_map, tokens, preferred_element_type=jnp.float32).astype(jnp.bfloat16)
    cotan_rows = jnp.dot(token_map, cotangent, preferred_element_type=jnp.float32).astype(
        jnp.bfloat16
    )
    per_token = jnp.sum(
        jnp.where(hit, gate_weights.astype(jnp.float32)[:, :, None], 0.0), axis=1
    )
    scale = jnp.sum(jnp.where(sel, per_token[None, :, :], 0.0), axis=1)
    return feat_rows, cotan_rows, jnp.transpose(scale).reshape(-1).astype(jnp.bfloat16)


def scatter_routes(hit, sel, values):
    per_token = jnp.sum(jnp.where(sel, jnp.transpose(values)[:, None, :], 0.0), axis=0)
    return jnp.sum(jnp.where(hit, per_token[:, None, :], 0.0), axis=2)


def swiglu_back(pre_gate, pre_up, grad_hidden):
    sigmoid_gate = jax.nn.sigmoid(pre_gate)
    activated = pre_gate * sigmoid_gate
    hidden = (activated * pre_up).astype(jnp.bfloat16)
    back_gate = (
        grad_hidden * pre_up * sigmoid_gate * (1.0 + pre_gate * (1.0 - sigmoid_gate))
    ).astype(jnp.bfloat16)
    back_up = (grad_hidden * activated).astype(jnp.bfloat16)
    return (hidden, back_gate, back_up)


def grp_sum_f32(x, axis_name):
    size = lax.axis_size(axis_name)
    if size & (size - 1):
        return lax.psum(x, axis_name)
    bit = 1
    while bit < size:
        partner = [(i, i ^ bit) for i in range(size)]
        x = x + lax.ppermute(x, axis_name, partner)
        bit *= 2
    return x


def grp_sum_rounded(parts, axes, axis_name):
    size = lax.axis_size(axis_name)
    rounded = [p.astype(jnp.bfloat16) for p in parts]
    if size == 1:
        return [r.astype(jnp.float32) for r in rounded]
    if size & (size - 1) or any(p.shape[a] % 2 for p, a in zip(parts, axes)):
        return [lax.psum(r, axis_name).astype(jnp.float32) for r in rounded]
    half_of = [p.shape[a] // 2 for p, a in zip(parts, axes)]
    core = lax.axis_index(axis_name) % 2
    keep = [
        lax.dynamic_slice_in_dim(r, core * h, h, axis=a) for r, h, a in zip(rounded, half_of, axes)
    ]
    send = [
        lax.dynamic_slice_in_dim(r, (1 - core) * h, h, axis=a)
        for r, h, a in zip(rounded, half_of, axes)
    ]
    swap = [(i, i ^ 1) for i in range(size)]
    got = lax.ppermute(send, axis_name, swap)
    sums = [k.astype(jnp.float32) + g.astype(jnp.float32) for k, g in zip(keep, got)]
    bit = 2
    while bit < size:
        partner = [(i, i ^ bit) for i in range(size)]
        mine = [s.astype(jnp.bfloat16) for s in sums]
        got = lax.ppermute(mine, axis_name, partner)
        sums = [m.astype(jnp.float32) + g.astype(jnp.float32) for m, g in zip(mine, got)]
        bit *= 2
    other = lax.ppermute(sums, axis_name, swap)
    full = []
    for s, o, a in zip(sums, other, axes):
        pair = jnp.stack([s, o])
        first = lax.dynamic_index_in_dim(pair, core, axis=0, keepdims=False)
        second = lax.dynamic_index_in_dim(pair, 1 - core, axis=0, keepdims=False)
        full.append(jnp.concatenate([first, second], axis=a))
    return full


def body(
    tokens,
    cotangent,
    gate_weights,
    expert_ids,
    hot_ids,
    gate_cold,
    up_cold,
    down_cold,
    gate_hot,
    up_hot,
    down_hot,
):
    tok_rows, slice_width = tokens.shape
    top_count = expert_ids.shape[1]
    cold_count = lax.axis_size("ep")
    blocks = lax.axis_size("ep")
    hot_count = hot_ids.shape[0]
    capacity = tok_rows // 16
    hot_hit, hot_sel = token_table(expert_ids, hot_ids, capacity)
    hot_feats, hot_cotan, hot_scale = gather_rows(hot_hit, hot_sel, tokens, cotangent, gate_weights)
    hot_rows = hot_count * capacity
    scale_lines = -(-hot_rows // slice_width)
    scale_lines = -(-scale_lines // 8) * 8
    scale_block = jnp.pad(hot_scale, (0, scale_lines * slice_width - hot_rows)).reshape(
        scale_lines, slice_width
    )
    hot_outgoing = jnp.concatenate([hot_feats, hot_cotan, scale_block], axis=0)
    cold_hit, cold_sel = token_table(
        expert_ids, jnp.arange(cold_count, dtype=jnp.int32), capacity
    )
    cold_feats, cold_cotan, cold_scale = gather_rows(
        cold_hit, cold_sel, tokens, cotangent, gate_weights
    )
    cold_lines = -(-capacity // slice_width)
    cold_lines = -(-cold_lines // 8) * 8
    cold_scale_block = jnp.pad(
        cold_scale.reshape(cold_count, capacity),
        ((0, 0), (0, cold_lines * slice_width - capacity)),
    ).reshape(cold_count, cold_lines, slice_width)
    outgoing = jnp.concatenate(
        [
            cold_feats.reshape(cold_count, capacity, slice_width),
            cold_cotan.reshape(cold_count, capacity, slice_width),
            cold_scale_block,
        ],
        axis=1,
    )
    hot_outgoing, outgoing = lax.optimization_barrier((hot_outgoing, outgoing))
    gathered = lax.all_gather(hot_outgoing, "ep", axis=0, tiled=False)
    received = lax.all_to_all(outgoing, "ep", split_axis=0, concat_axis=0, tiled=True)
    recv_feats = received[:, :capacity].reshape(-1, slice_width)
    recv_cotan = received[:, capacity : 2 * capacity].reshape(-1, slice_width)
    recv_scale = received[:, 2 * capacity :].reshape(cold_count, -1)[:, :capacity]
    weighted = (
        recv_scale.reshape(-1, 1).astype(jnp.float32) * recv_cotan.astype(jnp.float32)
    ).astype(jnp.bfloat16)
    w_gate = gate_cold[0]
    w_up = up_cold[0]
    w_down = down_cold[0]
    part_gate = jnp.dot(recv_feats, w_gate, preferred_element_type=jnp.float32)
    part_up = jnp.dot(recv_feats, w_up, preferred_element_type=jnp.float32)
    part_hidden = lax.dot_general(
        weighted, w_down, (((1,), (1,)), ((), ())), preferred_element_type=jnp.float32
    )
    pre_gate, pre_up, grad_hidden = grp_sum_rounded(
        [part_gate, part_up, part_hidden], [0, 0, 0], "grp"
    )
    hidden, back_gate, back_up = swiglu_back(pre_gate, pre_up, grad_hidden)
    output_slice = jnp.dot(hidden, w_down, preferred_element_type=jnp.float32)
    cold_route = jnp.sum(output_slice * recv_cotan.astype(jnp.float32), axis=1)
    cold_route = grp_sum_f32(cold_route.reshape(cold_count, capacity), "grp")
    cold_back = lax.all_to_all(cold_route, "ep", split_axis=0, concat_axis=0, tiled=True)
    contract_rows = (((0,), (0,)), ((), ()))
    grad_gate_cold = lax.dot_general(
        recv_feats, back_gate, contract_rows, preferred_element_type=jnp.float32
    )
    grad_up_cold = lax.dot_general(
        recv_feats, back_up, contract_rows, preferred_element_type=jnp.float32
    )
    grad_down_cold = lax.dot_general(
        hidden, weighted, contract_rows, preferred_element_type=jnp.float32
    )
    all_rows = gathered[:, : 2 * hot_rows].reshape(blocks, 2, hot_count, capacity, slice_width)
    all_rows = jnp.transpose(all_rows, (1, 2, 0, 3, 4)).reshape(
        2, hot_count, blocks * capacity, slice_width
    )
    all_scale = gathered[:, 2 * hot_rows :].reshape(blocks, -1)[:, :hot_rows]
    all_scale = jnp.transpose(all_scale.reshape(blocks, hot_count, capacity), (1, 0, 2))
    rows_feat, rows_cot = all_rows[0], all_rows[1]
    rows_wt = (
        all_scale.reshape(hot_count, blocks * capacity, 1).astype(jnp.float32)
        * rows_cot.astype(jnp.float32)
    ).astype(jnp.bfloat16)
    part_gate_hot = jnp.einsum(
        "jrd,jdh->jrh", rows_feat, gate_hot, preferred_element_type=jnp.float32
    )
    part_up_hot = jnp.einsum("jrd,jdh->jrh", rows_feat, up_hot, preferred_element_type=jnp.float32)
    part_hidden_hot = jnp.einsum(
        "jrd,jhd->jrh", rows_wt, down_hot, preferred_element_type=jnp.float32
    )
    part_cot_hot = jnp.einsum(
        "jrd,jhd->jrh", rows_cot, down_hot, preferred_element_type=jnp.float32
    )
    pre_gate_hot, pre_up_hot, grad_hidden_hot, cot_down = grp_sum_rounded(
        [part_gate_hot, part_up_hot, part_hidden_hot, part_cot_hot], [1, 1, 1, 1], "grp"
    )
    hidden_hot, back_gate_hot, back_up_hot = swiglu_back(pre_gate_hot, pre_up_hot, grad_hidden_hot)
    hot_route_part = jnp.sum(hidden_hot.astype(jnp.float32) * cot_down, axis=2)
    hot_back = lax.all_to_all(
        jnp.transpose(hot_route_part.reshape(hot_count, blocks, capacity), (1, 0, 2)),
        "ep",
        split_axis=0,
        concat_axis=0,
        tiled=True,
    )
    hot_route = jnp.sum(hot_back, axis=0)
    hidden_blk = hidden_hot.shape[2]
    feat_b = rows_feat.reshape(hot_count, blocks, capacity, slice_width)
    wt_b = rows_wt.reshape(hot_count, blocks, capacity, slice_width)
    bg_b = back_gate_hot.reshape(hot_count, blocks, capacity, hidden_blk)
    bu_b = back_up_hot.reshape(hot_count, blocks, capacity, hidden_blk)
    hid_b = hidden_hot.reshape(hot_count, blocks, capacity, hidden_blk)
    blk_gate = jnp.einsum("jbcd,jbch->jbdh", feat_b, bg_b, preferred_element_type=jnp.float32)
    blk_up = jnp.einsum("jbcd,jbch->jbdh", feat_b, bu_b, preferred_element_type=jnp.float32)
    blk_down = jnp.einsum("jbch,jbcd->jbhd", hid_b, wt_b, preferred_element_type=jnp.float32)
    grad_gate_hot = jnp.sum(blk_gate.astype(jnp.bfloat16).astype(jnp.float32), axis=1)
    grad_up_hot = jnp.sum(blk_up.astype(jnp.bfloat16).astype(jnp.float32), axis=1)
    grad_down_hot = jnp.sum(blk_down.astype(jnp.bfloat16).astype(jnp.float32), axis=1)
    gate_weight_grad = scatter_routes(cold_hit, cold_sel, cold_back) + scatter_routes(
        hot_hit, hot_sel, hot_route
    )
    return (
        grad_gate_cold[None].astype(jnp.bfloat16),
        grad_up_cold[None].astype(jnp.bfloat16),
        grad_down_cold[None].astype(jnp.bfloat16),
        grad_gate_hot,
        grad_up_hot,
        grad_down_hot,
        gate_weight_grad,
    )


def solution(mesh):
    in_specs = (
        P("ep", "grp"),
        P("ep", "grp"),
        P("ep", None),
        P("ep", None),
        P(),
        P("ep", "grp", None),
        P("ep", "grp", None),
        P("ep", None, "grp"),
        P(None, "grp", "ep"),
        P(None, "grp", "ep"),
        P(None, "ep", "grp"),
    )
    out_specs = (
        P("ep", "grp", None),
        P("ep", "grp", None),
        P("ep", None, "grp"),
        P(None, "grp", "ep"),
        P(None, "grp", "ep"),
        P(None, "ep", "grp"),
        P("ep", None),
    )
    return jax.shard_map(body, mesh=mesh, in_specs=in_specs, out_specs=out_specs, check_vma=False)
```

```python
import jax
import jax.numpy as jnp
from jax import lax
from jax.sharding import PartitionSpec as P


def token_table(expert_ids, targets, capacity):
    hit = expert_ids.T[:, None, :] == targets[None, :, None]
    tok_hit = jnp.any(hit, axis=0)
    rank = jnp.cumsum(tok_hit.astype(jnp.int32), axis=1) - 1
    slots = jnp.arange(capacity, dtype=jnp.int32)
    sel = (rank[:, None, :] == slots[None, :, None]) & tok_hit[:, None, :]
    return hit, sel


def gather_rows(hit, sel, tokens, cotangent, gate_weights):
    count, capacity = sel.shape[0], sel.shape[1]
    token_map = sel.reshape(count * capacity, -1).astype(jnp.bfloat16)
    feat_rows = jnp.dot(token_map, tokens, preferred_element_type=jnp.float32).astype(jnp.bfloat16)
    cotan_rows = jnp.dot(token_map, cotangent, preferred_element_type=jnp.float32).astype(
        jnp.bfloat16
    )
    per_token = jnp.sum(
        jnp.where(hit, gate_weights.T.astype(jnp.float32)[:, None, :], 0.0), axis=0
    )
    scale = jnp.sum(jnp.where(sel, per_token[:, None, :], 0.0), axis=2)
    return feat_rows, cotan_rows, scale.reshape(-1).astype(jnp.bfloat16)


def scatter_routes(hit, sel, values):
    per_token = jnp.sum(jnp.where(sel, values[:, :, None], 0.0), axis=1)
    return jnp.sum(jnp.where(hit, per_token[None, :, :], 0.0), axis=1).T


def shift_exchange(chunks, axis_name, sign):
    size = lax.axis_size(axis_name)
    moved = [chunks[0]]
    for k in range(1, size):
        perm = [(i, (i + sign * k) % size) for i in range(size)]
        moved.append(lax.ppermute(chunks[k], axis_name, perm))
    return jnp.stack(moved)


def swiglu_back(pre_gate, pre_up, grad_hidden):
    sigmoid_gate = jax.nn.sigmoid(pre_gate)
    activated = pre_gate * sigmoid_gate
    hidden = (activated * pre_up).astype(jnp.bfloat16)
    back_gate = (
        grad_hidden * pre_up * sigmoid_gate * (1.0 + pre_gate * (1.0 - sigmoid_gate))
    ).astype(jnp.bfloat16)
    back_up = (grad_hidden * activated).astype(jnp.bfloat16)
    return (hidden, back_gate, back_up)


def grp_sum_f32(x, axis_name):
    size = lax.axis_size(axis_name)
    if size & (size - 1):
        return lax.psum(x, axis_name)
    bit = 1
    while bit < size:
        partner = [(i, i ^ bit) for i in range(size)]
        x = x + lax.ppermute(x, axis_name, partner)
        bit *= 2
    return x


def grp_sum_rounded(parts, axes, axis_name):
    size = lax.axis_size(axis_name)
    rounded = [p.astype(jnp.bfloat16) for p in parts]
    if size == 1:
        return [r.astype(jnp.float32) for r in rounded]
    if size & (size - 1) or any(p.shape[a] % 2 for p, a in zip(parts, axes)):
        return [lax.psum(r, axis_name).astype(jnp.float32) for r in rounded]
    half_of = [p.shape[a] // 2 for p, a in zip(parts, axes)]
    core = lax.axis_index(axis_name) % 2
    keep = [
        lax.dynamic_slice_in_dim(r, core * h, h, axis=a) for r, h, a in zip(rounded, half_of, axes)
    ]
    send = [
        lax.dynamic_slice_in_dim(r, (1 - core) * h, h, axis=a)
        for r, h, a in zip(rounded, half_of, axes)
    ]
    swap = [(i, i ^ 1) for i in range(size)]
    got = lax.ppermute(send, axis_name, swap)
    sums = [k.astype(jnp.float32) + g.astype(jnp.float32) for k, g in zip(keep, got)]
    bit = 2
    while bit < size:
        partner = [(i, i ^ bit) for i in range(size)]
        mine = [s.astype(jnp.bfloat16) for s in sums]
        got = lax.ppermute(mine, axis_name, partner)
        sums = [m.astype(jnp.float32) + g.astype(jnp.float32) for m, g in zip(mine, got)]
        bit *= 2
    other = lax.ppermute(sums, axis_name, swap)
    full = []
    for s, o, a in zip(sums, other, axes):
        pair = jnp.stack([s, o])
        first = lax.dynamic_index_in_dim(pair, core, axis=0, keepdims=False)
        second = lax.dynamic_index_in_dim(pair, 1 - core, axis=0, keepdims=False)
        full.append(jnp.concatenate([first, second], axis=a))
    return full


def body(
    tokens,
    cotangent,
    gate_weights,
    expert_ids,
    hot_ids,
    gate_cold,
    up_cold,
    down_cold,
    gate_hot,
    up_hot,
    down_hot,
):
    tok_rows, slice_width = tokens.shape
    top_count = expert_ids.shape[1]
    cold_count = lax.axis_size("ep")
    blocks = lax.axis_size("ep")
    hot_count = hot_ids.shape[0]
    capacity = tok_rows // 16
    hot_hit, hot_sel = token_table(expert_ids, hot_ids, capacity)
    hot_feats, hot_cotan, hot_scale = gather_rows(hot_hit, hot_sel, tokens, cotangent, gate_weights)
    hot_rows = hot_count * capacity
    scale_lines = -(-hot_rows // slice_width)
    scale_lines = -(-scale_lines // 8) * 8
    scale_block = jnp.pad(hot_scale, (0, scale_lines * slice_width - hot_rows)).reshape(
        scale_lines, slice_width
    )
    hot_outgoing = jnp.concatenate([hot_feats, hot_cotan, scale_block], axis=0)
    cold_targets = (lax.axis_index("ep") + jnp.arange(cold_count, dtype=jnp.int32)) % cold_count
    cold_hit, cold_sel = token_table(expert_ids, cold_targets, capacity)
    cold_feats, cold_cotan, cold_scale = gather_rows(
        cold_hit, cold_sel, tokens, cotangent, gate_weights
    )
    cold_lines = -(-capacity // slice_width)
    cold_lines = -(-cold_lines // 8) * 8
    cold_scale_block = jnp.pad(
        cold_scale.reshape(cold_count, capacity),
        ((0, 0), (0, cold_lines * slice_width - capacity)),
    ).reshape(cold_count, cold_lines, slice_width)
    outgoing = jnp.concatenate(
        [
            cold_feats.reshape(cold_count, capacity, slice_width),
            cold_cotan.reshape(cold_count, capacity, slice_width),
            cold_scale_block,
        ],
        axis=1,
    )
    gathered = lax.all_gather(hot_outgoing, "ep", axis=0, tiled=False)
    received = shift_exchange(outgoing, "ep", 1)
    recv_feats = received[:, :capacity].reshape(-1, slice_width)
    recv_cotan = received[:, capacity : 2 * capacity].reshape(-1, slice_width)
    recv_scale = received[:, 2 * capacity :].reshape(cold_count, -1)[:, :capacity]
    weighted = (
        recv_scale.reshape(-1, 1).astype(jnp.float32) * recv_cotan.astype(jnp.float32)
    ).astype(jnp.bfloat16)
    w_gate = gate_cold[0]
    w_up = up_cold[0]
    w_down = down_cold[0]
    part_gate = jnp.dot(recv_feats, w_gate, preferred_element_type=jnp.float32)
    part_up = jnp.dot(recv_feats, w_up, preferred_element_type=jnp.float32)
    part_hidden = lax.dot_general(
        weighted, w_down, (((1,), (1,)), ((), ())), preferred_element_type=jnp.float32
    )
    pre_gate, pre_up, grad_hidden = grp_sum_rounded(
        [part_gate, part_up, part_hidden], [0, 0, 0], "grp"
    )
    hidden, back_gate, back_up = swiglu_back(pre_gate, pre_up, grad_hidden)
    output_slice = jnp.dot(hidden, w_down, preferred_element_type=jnp.float32)
    cold_route = jnp.sum(output_slice * recv_cotan.astype(jnp.float32), axis=1)
    cold_route = grp_sum_f32(cold_route.reshape(cold_count, capacity), "grp")
    cold_back = shift_exchange(cold_route, "ep", -1)
    contract_rows = (((0,), (0,)), ((), ()))
    grad_gate_cold = lax.dot_general(
        recv_feats, back_gate, contract_rows, preferred_element_type=jnp.float32
    )
    grad_up_cold = lax.dot_general(
        recv_feats, back_up, contract_rows, preferred_element_type=jnp.float32
    )
    grad_down_cold = lax.dot_general(
        hidden, weighted, contract_rows, preferred_element_type=jnp.float32
    )
    all_rows = gathered[:, : 2 * hot_rows].reshape(blocks, 2, hot_count, capacity, slice_width)
    all_rows = jnp.transpose(all_rows, (1, 2, 0, 3, 4)).reshape(
        2, hot_count, blocks * capacity, slice_width
    )
    all_scale = gathered[:, 2 * hot_rows :].reshape(blocks, -1)[:, :hot_rows]
    all_scale = jnp.transpose(all_scale.reshape(blocks, hot_count, capacity), (1, 0, 2))
    rows_feat, rows_cot = all_rows[0], all_rows[1]
    rows_wt = (
        all_scale.reshape(hot_count, blocks * capacity, 1).astype(jnp.float32)
        * rows_cot.astype(jnp.float32)
    ).astype(jnp.bfloat16)
    part_gate_hot = jnp.einsum(
        "jrd,jdh->jrh", rows_feat, gate_hot, preferred_element_type=jnp.float32
    )
    part_up_hot = jnp.einsum("jrd,jdh->jrh", rows_feat, up_hot, preferred_element_type=jnp.float32)
    part_hidden_hot = jnp.einsum(
        "jrd,jhd->jrh", rows_wt, down_hot, preferred_element_type=jnp.float32
    )
    part_cot_hot = jnp.einsum(
        "jrd,jhd->jrh", rows_cot, down_hot, preferred_element_type=jnp.float32
    )
    pre_gate_hot, pre_up_hot, grad_hidden_hot, cot_down = grp_sum_rounded(
        [part_gate_hot, part_up_hot, part_hidden_hot, part_cot_hot], [1, 1, 1, 1], "grp"
    )
    hidden_hot, back_gate_hot, back_up_hot = swiglu_back(pre_gate_hot, pre_up_hot, grad_hidden_hot)
    hot_route_part = jnp.sum(hidden_hot.astype(jnp.float32) * cot_down, axis=2)
    hot_back = lax.all_to_all(
        jnp.transpose(hot_route_part.reshape(hot_count, blocks, capacity), (1, 0, 2)),
        "ep",
        split_axis=0,
        concat_axis=0,
        tiled=True,
    )
    hot_route = jnp.sum(hot_back, axis=0)
    hidden_blk = hidden_hot.shape[2]
    feat_b = rows_feat.reshape(hot_count, blocks, capacity, slice_width)
    wt_b = rows_wt.reshape(hot_count, blocks, capacity, slice_width)
    bg_b = back_gate_hot.reshape(hot_count, blocks, capacity, hidden_blk)
    bu_b = back_up_hot.reshape(hot_count, blocks, capacity, hidden_blk)
    hid_b = hidden_hot.reshape(hot_count, blocks, capacity, hidden_blk)
    blk_gate = jnp.einsum("jbcd,jbch->jbdh", feat_b, bg_b, preferred_element_type=jnp.float32)
    blk_up = jnp.einsum("jbcd,jbch->jbdh", feat_b, bu_b, preferred_element_type=jnp.float32)
    blk_down = jnp.einsum("jbch,jbcd->jbhd", hid_b, wt_b, preferred_element_type=jnp.float32)
    grad_gate_hot = jnp.sum(blk_gate.astype(jnp.bfloat16).astype(jnp.float32), axis=1)
    grad_up_hot = jnp.sum(blk_up.astype(jnp.bfloat16).astype(jnp.float32), axis=1)
    grad_down_hot = jnp.sum(blk_down.astype(jnp.bfloat16).astype(jnp.float32), axis=1)
    gate_weight_grad = scatter_routes(cold_hit, cold_sel, cold_back) + scatter_routes(
        hot_hit, hot_sel, hot_route
    )
    return (
        grad_gate_cold[None].astype(jnp.bfloat16),
        grad_up_cold[None].astype(jnp.bfloat16),
        grad_down_cold[None].astype(jnp.bfloat16),
        grad_gate_hot,
        grad_up_hot,
        grad_down_hot,
        gate_weight_grad,
    )


def solution(mesh):
    in_specs = (
        P("ep", "grp"),
        P("ep", "grp"),
        P("ep", None),
        P("ep", None),
        P(),
        P("ep", "grp", None),
        P("ep", "grp", None),
        P("ep", None, "grp"),
        P(None, "grp", "ep"),
        P(None, "grp", "ep"),
        P(None, "ep", "grp"),
    )
    out_specs = (
        P("ep", "grp", None),
        P("ep", "grp", None),
        P("ep", None, "grp"),
        P(None, "grp", "ep"),
        P(None, "grp", "ep"),
        P(None, "ep", "grp"),
        P("ep", None),
    )
    return jax.shard_map(body, mesh=mesh, in_specs=in_specs, out_specs=out_specs, check_vma=False)
```

```python
import jax
import jax.numpy as jnp
from jax import lax
from jax.sharding import PartitionSpec as P


def route_table(flat_ids, targets, capacity):
    matches = (flat_ids[:, None] == targets[None, :]).astype(jnp.int32)
    rank_of = jnp.cumsum(matches, axis=0) - 1
    slot_of = jnp.sum(matches * rank_of, axis=1)
    owner_of = jnp.sum(matches * jnp.arange(targets.shape[0], dtype=jnp.int32)[None, :], axis=1)
    usable = jnp.sum(matches, axis=1) > 0
    row_of = owner_of * capacity + slot_of
    rows_total = targets.shape[0] * capacity
    route_map = (row_of[None, :] == jnp.arange(rows_total, dtype=jnp.int32)[:, None]) & usable[
        None, :
    ]
    return route_map.astype(jnp.float32)


def gather_rows(route_map, tokens, cotangent, flat_weights, tok_rows, top_count):
    per_token = jnp.sum(route_map.reshape(route_map.shape[0], tok_rows, top_count), axis=2)
    token_map = per_token.astype(jnp.bfloat16)
    feat_rows = jnp.dot(token_map, tokens, preferred_element_type=jnp.float32).astype(jnp.bfloat16)
    cotan_rows = jnp.dot(token_map, cotangent, preferred_element_type=jnp.float32).astype(
        jnp.bfloat16
    )
    scale_rows = jnp.dot(
        route_map, flat_weights.astype(jnp.float32), precision=lax.Precision.HIGHEST
    )
    return (feat_rows, cotan_rows, scale_rows.astype(jnp.bfloat16))


def swiglu_back(pre_gate, pre_up, grad_hidden):
    sigmoid_gate = jax.nn.sigmoid(pre_gate)
    activated = pre_gate * sigmoid_gate
    hidden = (activated * pre_up).astype(jnp.bfloat16)
    back_gate = (
        grad_hidden * pre_up * sigmoid_gate * (1.0 + pre_gate * (1.0 - sigmoid_gate))
    ).astype(jnp.bfloat16)
    back_up = (grad_hidden * activated).astype(jnp.bfloat16)
    return (hidden, back_gate, back_up)


def grp_sum_f32(x, axis_name):
    size = lax.axis_size(axis_name)
    if size & (size - 1):
        return lax.psum(x, axis_name)
    bit = 1
    while bit < size:
        partner = [(i, i ^ bit) for i in range(size)]
        x = x + lax.ppermute(x, axis_name, partner)
        bit *= 2
    return x


def grp_sum_rounded(parts, axes, axis_name):
    size = lax.axis_size(axis_name)
    rounded = [p.astype(jnp.bfloat16) for p in parts]
    if size == 1:
        return [r.astype(jnp.float32) for r in rounded]
    if size & (size - 1) or any(p.shape[a] % 2 for p, a in zip(parts, axes)):
        return [lax.psum(r, axis_name).astype(jnp.float32) for r in rounded]
    half_of = [p.shape[a] // 2 for p, a in zip(parts, axes)]
    core = lax.axis_index(axis_name) % 2
    keep = [
        lax.dynamic_slice_in_dim(r, core * h, h, axis=a) for r, h, a in zip(rounded, half_of, axes)
    ]
    send = [
        lax.dynamic_slice_in_dim(r, (1 - core) * h, h, axis=a)
        for r, h, a in zip(rounded, half_of, axes)
    ]
    swap = [(i, i ^ 1) for i in range(size)]
    got = lax.ppermute(send, axis_name, swap)
    sums = [k.astype(jnp.float32) + g.astype(jnp.float32) for k, g in zip(keep, got)]
    bit = 2
    while bit < size:
        partner = [(i, i ^ bit) for i in range(size)]
        mine = [s.astype(jnp.bfloat16) for s in sums]
        got = lax.ppermute(mine, axis_name, partner)
        sums = [m.astype(jnp.float32) + g.astype(jnp.float32) for m, g in zip(mine, got)]
        bit *= 2
    other = lax.ppermute(sums, axis_name, swap)
    full = []
    for s, o, a in zip(sums, other, axes):
        pair = jnp.stack([s, o])
        first = lax.dynamic_index_in_dim(pair, core, axis=0, keepdims=False)
        second = lax.dynamic_index_in_dim(pair, 1 - core, axis=0, keepdims=False)
        full.append(jnp.concatenate([first, second], axis=a))
    return full


def body(
    tokens,
    cotangent,
    gate_weights,
    expert_ids,
    hot_ids,
    gate_cold,
    up_cold,
    down_cold,
    gate_hot,
    up_hot,
    down_hot,
):
    tok_rows, slice_width = tokens.shape
    top_count = expert_ids.shape[1]
    cold_count = lax.axis_size("ep")
    hot_count = hot_ids.shape[0]
    capacity = tok_rows // 16
    flat_ids = expert_ids.reshape(-1)
    flat_weights = gate_weights.reshape(-1)
    cold_map = route_table(flat_ids, jnp.arange(cold_count, dtype=jnp.int32), capacity)
    hot_map = route_table(flat_ids, hot_ids, capacity)
    hot_feats, hot_cotan, hot_scale = gather_rows(
        hot_map, tokens, cotangent, flat_weights, tok_rows, top_count
    )
    hot_rows = hot_count * capacity
    scale_lines = -(-hot_rows // slice_width)
    scale_lines = -(-scale_lines // 8) * 8
    scale_block = jnp.pad(hot_scale, (0, scale_lines * slice_width - hot_rows)).reshape(
        scale_lines, slice_width
    )
    blocks = lax.axis_size("ep")
    gathered = lax.all_gather(
        jnp.concatenate([hot_feats, hot_cotan, scale_block], axis=0), "ep", axis=0, tiled=False
    )
    cold_feats, cold_cotan, cold_scale = gather_rows(
        cold_map, tokens, cotangent, flat_weights, tok_rows, top_count
    )
    cold_lines = -(-capacity // slice_width)
    cold_lines = -(-cold_lines // 8) * 8
    cold_scale_block = jnp.pad(
        cold_scale.reshape(cold_count, capacity),
        ((0, 0), (0, cold_lines * slice_width - capacity)),
    ).reshape(cold_count, cold_lines, slice_width)
    outgoing = jnp.concatenate(
        [
            cold_feats.reshape(cold_count, capacity, slice_width),
            cold_cotan.reshape(cold_count, capacity, slice_width),
            cold_scale_block,
        ],
        axis=1,
    )
    received = lax.all_to_all(outgoing, "ep", split_axis=0, concat_axis=0, tiled=True)
    recv_feats = received[:, :capacity].reshape(-1, slice_width)
    recv_cotan = received[:, capacity : 2 * capacity].reshape(-1, slice_width)
    recv_scale = received[:, 2 * capacity :].reshape(cold_count, -1)[:, :capacity]
    weighted = (
        recv_scale.reshape(-1, 1).astype(jnp.float32) * recv_cotan.astype(jnp.float32)
    ).astype(jnp.bfloat16)
    w_gate = gate_cold[0]
    w_up = up_cold[0]
    w_down = down_cold[0]
    part_gate = jnp.dot(recv_feats, w_gate, preferred_element_type=jnp.float32)
    part_up = jnp.dot(recv_feats, w_up, preferred_element_type=jnp.float32)
    part_hidden = lax.dot_general(
        weighted, w_down, (((1,), (1,)), ((), ())), preferred_element_type=jnp.float32
    )
    all_rows = gathered[:, : 2 * hot_rows].reshape(blocks, 2, hot_count, capacity, slice_width)
    all_rows = jnp.transpose(all_rows, (1, 2, 0, 3, 4)).reshape(
        2, hot_count, blocks * capacity, slice_width
    )
    all_scale = gathered[:, 2 * hot_rows :].reshape(blocks, -1)[:, :hot_rows]
    all_scale = jnp.transpose(all_scale.reshape(blocks, hot_count, capacity), (1, 0, 2))
    rows_feat, rows_cot = all_rows[0], all_rows[1]
    rows_wt = (
        all_scale.reshape(hot_count, blocks * capacity, 1).astype(jnp.float32)
        * rows_cot.astype(jnp.float32)
    ).astype(jnp.bfloat16)
    part_gate_hot = jnp.einsum(
        "jrd,jdh->jrh", rows_feat, gate_hot, preferred_element_type=jnp.float32
    )
    part_up_hot = jnp.einsum("jrd,jdh->jrh", rows_feat, up_hot, preferred_element_type=jnp.float32)
    part_hidden_hot = jnp.einsum(
        "jrd,jhd->jrh", rows_wt, down_hot, preferred_element_type=jnp.float32
    )
    part_cot_hot = jnp.einsum(
        "jrd,jhd->jrh", rows_cot, down_hot, preferred_element_type=jnp.float32
    )
    part_cot = lax.dot_general(
        recv_cotan, w_down, (((1,), (1,)), ((), ())), preferred_element_type=jnp.float32
    )
    (
        pre_gate,
        pre_up,
        grad_hidden,
        cold_cot_down,
        pre_gate_hot,
        pre_up_hot,
        grad_hidden_hot,
        cot_down,
    ) = grp_sum_rounded(
        [
            part_gate,
            part_up,
            part_hidden,
            part_cot,
            part_gate_hot,
            part_up_hot,
            part_hidden_hot,
            part_cot_hot,
        ],
        [0, 0, 0, 0, 1, 1, 1, 1],
        "grp",
    )
    hidden, back_gate, back_up = swiglu_back(pre_gate, pre_up, grad_hidden)
    cold_route = jnp.sum(hidden.astype(jnp.float32) * cold_cot_down, axis=1)
    contract_rows = (((0,), (0,)), ((), ()))
    grad_gate_cold = lax.dot_general(
        recv_feats, back_gate, contract_rows, preferred_element_type=jnp.float32
    )
    grad_up_cold = lax.dot_general(
        recv_feats, back_up, contract_rows, preferred_element_type=jnp.float32
    )
    grad_down_cold = lax.dot_general(
        hidden, weighted, contract_rows, preferred_element_type=jnp.float32
    )
    hidden_hot, back_gate_hot, back_up_hot = swiglu_back(pre_gate_hot, pre_up_hot, grad_hidden_hot)
    hot_route_part = jnp.sum(hidden_hot.astype(jnp.float32) * cot_down, axis=2)
    hidden_blk = hidden_hot.shape[2]
    feat_b = rows_feat.reshape(hot_count, blocks, capacity, slice_width)
    wt_b = rows_wt.reshape(hot_count, blocks, capacity, slice_width)
    bg_b = back_gate_hot.reshape(hot_count, blocks, capacity, hidden_blk)
    bu_b = back_up_hot.reshape(hot_count, blocks, capacity, hidden_blk)
    hid_b = hidden_hot.reshape(hot_count, blocks, capacity, hidden_blk)
    blk_gate = jnp.einsum("jbcd,jbch->jbdh", feat_b, bg_b, preferred_element_type=jnp.float32)
    blk_up = jnp.einsum("jbcd,jbch->jbdh", feat_b, bu_b, preferred_element_type=jnp.float32)
    blk_down = jnp.einsum("jbch,jbcd->jbhd", hid_b, wt_b, preferred_element_type=jnp.float32)
    grad_gate_hot = jnp.sum(blk_gate.astype(jnp.bfloat16).astype(jnp.float32), axis=1)
    grad_up_hot = jnp.sum(blk_up.astype(jnp.bfloat16).astype(jnp.float32), axis=1)
    grad_down_hot = jnp.sum(blk_down.astype(jnp.bfloat16).astype(jnp.float32), axis=1)
    route_parts = jnp.concatenate(
        [
            cold_route.reshape(cold_count, 1, capacity),
            jnp.transpose(hot_route_part.reshape(hot_count, blocks, capacity), (1, 0, 2)),
        ],
        axis=1,
    )
    route_back = lax.all_to_all(route_parts, "ep", split_axis=0, concat_axis=0, tiled=True)
    cold_back = route_back[:, 0, :]
    hot_route = jnp.sum(route_back[:, 1:, :], axis=0)
    route_flat = jnp.dot(cold_back.reshape(-1), cold_map, precision=lax.Precision.HIGHEST)
    route_flat = route_flat + jnp.dot(
        hot_route.reshape(-1), hot_map, precision=lax.Precision.HIGHEST
    )
    gate_weight_grad = route_flat.reshape(tok_rows, top_count)
    return (
        grad_gate_cold[None].astype(jnp.bfloat16),
        grad_up_cold[None].astype(jnp.bfloat16),
        grad_down_cold[None].astype(jnp.bfloat16),
        grad_gate_hot,
        grad_up_hot,
        grad_down_hot,
        gate_weight_grad,
    )


def solution(mesh):
    in_specs = (
        P("ep", "grp"),
        P("ep", "grp"),
        P("ep", None),
        P("ep", None),
        P(),
        P("ep", "grp", None),
        P("ep", "grp", None),
        P("ep", None, "grp"),
        P(None, "grp", "ep"),
        P(None, "grp", "ep"),
        P(None, "ep", "grp"),
    )
    out_specs = (
        P("ep", "grp", None),
        P("ep", "grp", None),
        P("ep", None, "grp"),
        P(None, "grp", "ep"),
        P(None, "grp", "ep"),
        P(None, "ep", "grp"),
        P("ep", None),
    )
    return jax.shard_map(body, mesh=mesh, in_specs=in_specs, out_specs=out_specs, check_vma=False)
```

```python
import jax
import jax.numpy as jnp
from jax import lax
from jax.sharding import PartitionSpec as P


def token_table(expert_ids, targets, capacity):
    hit = expert_ids.T[:, None, :] == targets[None, :, None]
    tok_hit = jnp.any(hit, axis=0)
    rank = jnp.cumsum(tok_hit.astype(jnp.int32), axis=1) - 1
    slots = jnp.arange(capacity, dtype=jnp.int32)
    sel = (rank[:, None, :] == slots[None, :, None]) & tok_hit[:, None, :]
    return hit, sel


def gather_rows(hit, sel, tokens, cotangent, gate_weights):
    count, capacity = sel.shape[0], sel.shape[1]
    token_map = sel.reshape(count * capacity, -1).astype(jnp.bfloat16)
    feat_rows = jnp.dot(token_map, tokens, preferred_element_type=jnp.float32).astype(jnp.bfloat16)
    cotan_rows = jnp.dot(token_map, cotangent, preferred_element_type=jnp.float32).astype(
        jnp.bfloat16
    )
    per_token = jnp.sum(
        jnp.where(hit, gate_weights.T.astype(jnp.float32)[:, None, :], 0.0), axis=0
    )
    scale = jnp.sum(jnp.where(sel, per_token[:, None, :], 0.0), axis=2)
    return feat_rows, cotan_rows, scale.reshape(-1).astype(jnp.bfloat16)


def scatter_routes(hit, sel, values):
    per_token = jnp.sum(jnp.where(sel, values[:, :, None], 0.0), axis=1)
    return jnp.sum(jnp.where(hit, per_token[None, :, :], 0.0), axis=1).T


def swiglu_back(pre_gate, pre_up, grad_hidden):
    sigmoid_gate = jax.nn.sigmoid(pre_gate)
    activated = pre_gate * sigmoid_gate
    hidden = (activated * pre_up).astype(jnp.bfloat16)
    back_gate = (
        grad_hidden * pre_up * sigmoid_gate * (1.0 + pre_gate * (1.0 - sigmoid_gate))
    ).astype(jnp.bfloat16)
    back_up = (grad_hidden * activated).astype(jnp.bfloat16)
    return (hidden, back_gate, back_up)


def grp_sum_f32(x, axis_name):
    size = lax.axis_size(axis_name)
    if size & (size - 1):
        return lax.psum(x, axis_name)
    bit = 1
    while bit < size:
        partner = [(i, i ^ bit) for i in range(size)]
        x = x + lax.ppermute(x, axis_name, partner)
        bit *= 2
    return x


def grp_sum_rounded(parts, axes, axis_name):
    size = lax.axis_size(axis_name)
    rounded = [p.astype(jnp.bfloat16) for p in parts]
    if size == 1:
        return [r.astype(jnp.float32) for r in rounded]
    if size & (size - 1) or any(p.shape[a] % 2 for p, a in zip(parts, axes)):
        return [lax.psum(r, axis_name).astype(jnp.float32) for r in rounded]
    first_core = lax.axis_index(axis_name) % 2 == 0
    halves = [jnp.split(r, 2, axis=a) for r, a in zip(rounded, axes)]
    keep = [jnp.where(first_core, lo, hi) for lo, hi in halves]
    send = [jnp.where(first_core, hi, lo) for lo, hi in halves]
    swap = [(i, i ^ 1) for i in range(size)]
    got = lax.ppermute(send, axis_name, swap)
    sums = [k.astype(jnp.float32) + g.astype(jnp.float32) for k, g in zip(keep, got)]
    bit = 2
    while bit < size:
        partner = [(i, i ^ bit) for i in range(size)]
        mine = [s.astype(jnp.bfloat16) for s in sums]
        got = lax.ppermute(mine, axis_name, partner)
        sums = [m.astype(jnp.float32) + g.astype(jnp.float32) for m, g in zip(mine, got)]
        bit *= 2
    other = lax.ppermute(sums, axis_name, swap)
    full = []
    for s, o, a in zip(sums, other, axes):
        first = jnp.where(first_core, s, o)
        second = jnp.where(first_core, o, s)
        full.append(jnp.concatenate([first, second], axis=a))
    return full


def body(
    tokens,
    cotangent,
    gate_weights,
    expert_ids,
    hot_ids,
    gate_cold,
    up_cold,
    down_cold,
    gate_hot,
    up_hot,
    down_hot,
):
    tok_rows, slice_width = tokens.shape
    top_count = expert_ids.shape[1]
    cold_count = lax.axis_size("ep")
    hot_count = hot_ids.shape[0]
    capacity = tok_rows // 16
    hot_hit, hot_sel = token_table(expert_ids, hot_ids, capacity)
    hot_feats, hot_cotan, hot_scale = gather_rows(hot_hit, hot_sel, tokens, cotangent, gate_weights)
    hot_rows = hot_count * capacity
    scale_lines = -(-hot_rows // slice_width)
    scale_lines = -(-scale_lines // 8) * 8
    scale_block = jnp.pad(hot_scale, (0, scale_lines * slice_width - hot_rows)).reshape(
        scale_lines, slice_width
    )
    blocks = lax.axis_size("ep")
    gathered = lax.all_gather(
        jnp.concatenate([hot_feats, hot_cotan, scale_block], axis=0), "ep", axis=0, tiled=False
    )
    cold_hit, cold_sel = token_table(
        expert_ids, jnp.arange(cold_count, dtype=jnp.int32), capacity
    )
    cold_feats, cold_cotan, cold_scale = gather_rows(
        cold_hit, cold_sel, tokens, cotangent, gate_weights
    )
    cold_lines = -(-capacity // slice_width)
    cold_lines = -(-cold_lines // 8) * 8
    cold_scale_block = jnp.pad(
        cold_scale.reshape(cold_count, capacity),
        ((0, 0), (0, cold_lines * slice_width - capacity)),
    ).reshape(cold_count, cold_lines, slice_width)
    outgoing = jnp.concatenate(
        [
            cold_feats.reshape(cold_count, capacity, slice_width),
            cold_cotan.reshape(cold_count, capacity, slice_width),
            cold_scale_block,
        ],
        axis=1,
    )
    received = lax.all_to_all(outgoing, "ep", split_axis=0, concat_axis=0, tiled=True)
    recv_feats = received[:, :capacity].reshape(-1, slice_width)
    recv_cotan = received[:, capacity : 2 * capacity].reshape(-1, slice_width)
    recv_scale = received[:, 2 * capacity :].reshape(cold_count, -1)[:, :capacity]
    weighted = (
        recv_scale.reshape(-1, 1).astype(jnp.float32) * recv_cotan.astype(jnp.float32)
    ).astype(jnp.bfloat16)
    w_gate = gate_cold[0]
    w_up = up_cold[0]
    w_down = down_cold[0]
    part_gate = jnp.dot(recv_feats, w_gate, preferred_element_type=jnp.float32)
    part_up = jnp.dot(recv_feats, w_up, preferred_element_type=jnp.float32)
    part_hidden = lax.dot_general(
        weighted, w_down, (((1,), (1,)), ((), ())), preferred_element_type=jnp.float32
    )
    all_rows = gathered[:, : 2 * hot_rows].reshape(blocks, 2, hot_count, capacity, slice_width)
    all_rows = jnp.transpose(all_rows, (1, 2, 0, 3, 4)).reshape(
        2, hot_count, blocks * capacity, slice_width
    )
    all_scale = gathered[:, 2 * hot_rows :].reshape(blocks, -1)[:, :hot_rows]
    all_scale = jnp.transpose(all_scale.reshape(blocks, hot_count, capacity), (1, 0, 2))
    rows_feat, rows_cot = all_rows[0], all_rows[1]
    rows_wt = (
        all_scale.reshape(hot_count, blocks * capacity, 1).astype(jnp.float32)
        * rows_cot.astype(jnp.float32)
    ).astype(jnp.bfloat16)
    part_gate_hot = jnp.einsum(
        "jrd,jdh->jrh", rows_feat, gate_hot, preferred_element_type=jnp.float32
    )
    part_up_hot = jnp.einsum("jrd,jdh->jrh", rows_feat, up_hot, preferred_element_type=jnp.float32)
    part_hidden_hot = jnp.einsum(
        "jrd,jhd->jrh", rows_wt, down_hot, preferred_element_type=jnp.float32
    )
    cot_down = jnp.einsum("jrd,jhd->jrh", rows_cot, down_hot, preferred_element_type=jnp.float32)
    (pre_gate, pre_up, grad_hidden, pre_gate_hot, pre_up_hot, grad_hidden_hot) = grp_sum_rounded(
        [part_gate, part_up, part_hidden, part_gate_hot, part_up_hot, part_hidden_hot],
        [0, 0, 0, 1, 1, 1],
        "grp",
    )
    hidden, back_gate, back_up = swiglu_back(pre_gate, pre_up, grad_hidden)
    output_slice = jnp.dot(hidden, w_down, preferred_element_type=jnp.float32)
    cold_route = jnp.sum(output_slice * recv_cotan.astype(jnp.float32), axis=1)
    contract_rows = (((0,), (0,)), ((), ()))
    grad_gate_cold = lax.dot_general(
        recv_feats, back_gate, contract_rows, preferred_element_type=jnp.float32
    )
    grad_up_cold = lax.dot_general(
        recv_feats, back_up, contract_rows, preferred_element_type=jnp.float32
    )
    grad_down_cold = lax.dot_general(
        hidden, weighted, contract_rows, preferred_element_type=jnp.float32
    )
    hidden_hot, back_gate_hot, back_up_hot = swiglu_back(pre_gate_hot, pre_up_hot, grad_hidden_hot)
    hot_route_part = jnp.sum(hidden_hot.astype(jnp.float32) * cot_down, axis=2)
    hidden_blk = hidden_hot.shape[2]
    feat_b = rows_feat.reshape(hot_count, blocks, capacity, slice_width)
    wt_b = rows_wt.reshape(hot_count, blocks, capacity, slice_width)
    bg_b = back_gate_hot.reshape(hot_count, blocks, capacity, hidden_blk)
    bu_b = back_up_hot.reshape(hot_count, blocks, capacity, hidden_blk)
    hid_b = hidden_hot.reshape(hot_count, blocks, capacity, hidden_blk)
    blk_gate = jnp.einsum("jbcd,jbch->jbdh", feat_b, bg_b, preferred_element_type=jnp.float32)
    blk_up = jnp.einsum("jbcd,jbch->jbdh", feat_b, bu_b, preferred_element_type=jnp.float32)
    blk_down = jnp.einsum("jbch,jbcd->jbhd", hid_b, wt_b, preferred_element_type=jnp.float32)
    grad_gate_hot = jnp.sum(blk_gate.astype(jnp.bfloat16).astype(jnp.float32), axis=1)
    grad_up_hot = jnp.sum(blk_up.astype(jnp.bfloat16).astype(jnp.float32), axis=1)
    grad_down_hot = jnp.sum(blk_down.astype(jnp.bfloat16).astype(jnp.float32), axis=1)
    route_parts = jnp.concatenate(
        [
            cold_route.reshape(cold_count, 1, capacity),
            jnp.transpose(hot_route_part.reshape(hot_count, blocks, capacity), (1, 0, 2)),
        ],
        axis=1,
    )
    route_parts = grp_sum_f32(route_parts, "grp")
    route_back = lax.all_to_all(route_parts, "ep", split_axis=0, concat_axis=0, tiled=True)
    cold_back = route_back[:, 0, :]
    hot_route = jnp.sum(route_back[:, 1:, :], axis=0)
    gate_weight_grad = scatter_routes(cold_hit, cold_sel, cold_back) + scatter_routes(
        hot_hit, hot_sel, hot_route
    )
    return (
        grad_gate_cold[None].astype(jnp.bfloat16),
        grad_up_cold[None].astype(jnp.bfloat16),
        grad_down_cold[None].astype(jnp.bfloat16),
        grad_gate_hot,
        grad_up_hot,
        grad_down_hot,
        gate_weight_grad,
    )


def solution(mesh):
    in_specs = (
        P("ep", "grp"),
        P("ep", "grp"),
        P("ep", None),
        P("ep", None),
        P(),
        P("ep", "grp", None),
        P("ep", "grp", None),
        P("ep", None, "grp"),
        P(None, "grp", "ep"),
        P(None, "grp", "ep"),
        P(None, "ep", "grp"),
    )
    out_specs = (
        P("ep", "grp", None),
        P("ep", "grp", None),
        P("ep", None, "grp"),
        P(None, "grp", "ep"),
        P(None, "grp", "ep"),
        P(None, "ep", "grp"),
        P("ep", None),
    )
    return jax.shard_map(body, mesh=mesh, in_specs=in_specs, out_specs=out_specs, check_vma=False)
```

```python
import jax
import jax.numpy as jnp
from jax import lax
from jax.sharding import PartitionSpec as P


def token_table(expert_ids, targets, capacity):
    hit = expert_ids.T[:, None, :] == targets[None, :, None]
    tok_hit = jnp.any(hit, axis=0)
    rank = jnp.cumsum(tok_hit.astype(jnp.int32), axis=1) - 1
    slots = jnp.arange(capacity, dtype=jnp.int32)
    sel = (rank[:, None, :] == slots[None, :, None]) & tok_hit[:, None, :]
    return hit, sel


def gather_rows(hit, sel, tokens, cotangent, gate_weights):
    count, capacity = sel.shape[0], sel.shape[1]
    token_map = sel.reshape(count * capacity, -1).astype(jnp.bfloat16)
    feat_rows = jnp.dot(token_map, tokens, preferred_element_type=jnp.float32).astype(jnp.bfloat16)
    cotan_rows = jnp.dot(token_map, cotangent, preferred_element_type=jnp.float32).astype(
        jnp.bfloat16
    )
    per_token = jnp.sum(
        jnp.where(hit, gate_weights.T.astype(jnp.float32)[:, None, :], 0.0), axis=0
    )
    scale = jnp.sum(jnp.where(sel, per_token[:, None, :], 0.0), axis=2)
    return feat_rows, cotan_rows, scale.reshape(-1).astype(jnp.bfloat16)


def scatter_routes(hit, sel, values):
    per_token = jnp.sum(jnp.where(sel, values[:, :, None], 0.0), axis=1)
    return jnp.sum(jnp.where(hit, per_token[None, :, :], 0.0), axis=1).T


def swiglu_back(pre_gate, pre_up, grad_hidden):
    sigmoid_gate = jax.nn.sigmoid(pre_gate)
    activated = pre_gate * sigmoid_gate
    hidden = (activated * pre_up).astype(jnp.bfloat16)
    back_gate = (
        grad_hidden * pre_up * sigmoid_gate * (1.0 + pre_gate * (1.0 - sigmoid_gate))
    ).astype(jnp.bfloat16)
    back_up = (grad_hidden * activated).astype(jnp.bfloat16)
    return (hidden, back_gate, back_up)


def grp_sum_f32(x, axis_name):
    size = lax.axis_size(axis_name)
    if size & (size - 1):
        return lax.psum(x, axis_name)
    bit = 1
    while bit < size:
        partner = [(i, i ^ bit) for i in range(size)]
        x = x + lax.ppermute(x, axis_name, partner)
        bit *= 2
    return x


def grp_sum_rounded(parts, axes, axis_name):
    size = lax.axis_size(axis_name)
    rounded = [p.astype(jnp.bfloat16) for p in parts]
    if size == 1:
        return [r.astype(jnp.float32) for r in rounded]
    if size & (size - 1) or any(p.shape[a] % 2 for p, a in zip(parts, axes)):
        return [lax.psum(r, axis_name).astype(jnp.float32) for r in rounded]
    first_core = lax.axis_index(axis_name) % 2 == 0
    halves = [jnp.split(r, 2, axis=a) for r, a in zip(rounded, axes)]
    keep = [jnp.where(first_core, lo, hi) for lo, hi in halves]
    send = [jnp.where(first_core, hi, lo) for lo, hi in halves]
    swap = [(i, i ^ 1) for i in range(size)]
    got = lax.ppermute(send, axis_name, swap)
    sums = [k.astype(jnp.float32) + g.astype(jnp.float32) for k, g in zip(keep, got)]
    bit = 2
    while bit < size:
        partner = [(i, i ^ bit) for i in range(size)]
        mine = [s.astype(jnp.bfloat16) for s in sums]
        got = lax.ppermute(mine, axis_name, partner)
        sums = [m.astype(jnp.float32) + g.astype(jnp.float32) for m, g in zip(mine, got)]
        bit *= 2
    other = lax.ppermute(sums, axis_name, swap)
    full = []
    for s, o, a in zip(sums, other, axes):
        first = jnp.where(first_core, s, o)
        second = jnp.where(first_core, o, s)
        full.append(jnp.concatenate([first, second], axis=a))
    return full


def body(
    tokens,
    cotangent,
    gate_weights,
    expert_ids,
    hot_ids,
    gate_cold,
    up_cold,
    down_cold,
    gate_hot,
    up_hot,
    down_hot,
):
    tok_rows, slice_width = tokens.shape
    top_count = expert_ids.shape[1]
    cold_count = lax.axis_size("ep")
    hot_count = hot_ids.shape[0]
    capacity = tok_rows // 16
    hot_hit, hot_sel = token_table(expert_ids, hot_ids, capacity)
    hot_feats, hot_cotan, hot_scale = gather_rows(hot_hit, hot_sel, tokens, cotangent, gate_weights)
    hot_rows = hot_count * capacity
    scale_lines = -(-hot_rows // slice_width)
    scale_lines = -(-scale_lines // 8) * 8
    scale_block = jnp.pad(hot_scale, (0, scale_lines * slice_width - hot_rows)).reshape(
        scale_lines, slice_width
    )
    blocks = lax.axis_size("ep")
    hot_outgoing = jnp.concatenate([hot_feats, hot_cotan, scale_block], axis=0)
    hot_outgoing, expert_ids, tokens, cotangent, gate_weights = lax.optimization_barrier(
        (hot_outgoing, expert_ids, tokens, cotangent, gate_weights)
    )
    gathered = lax.all_gather(hot_outgoing, "ep", axis=0, tiled=False)
    cold_hit, cold_sel = token_table(
        expert_ids, jnp.arange(cold_count, dtype=jnp.int32), capacity
    )
    cold_feats, cold_cotan, cold_scale = gather_rows(
        cold_hit, cold_sel, tokens, cotangent, gate_weights
    )
    cold_lines = -(-capacity // slice_width)
    cold_lines = -(-cold_lines // 8) * 8
    cold_scale_block = jnp.pad(
        cold_scale.reshape(cold_count, capacity),
        ((0, 0), (0, cold_lines * slice_width - capacity)),
    ).reshape(cold_count, cold_lines, slice_width)
    outgoing = jnp.concatenate(
        [
            cold_feats.reshape(cold_count, capacity, slice_width),
            cold_cotan.reshape(cold_count, capacity, slice_width),
            cold_scale_block,
        ],
        axis=1,
    )
    received = lax.all_to_all(outgoing, "ep", split_axis=0, concat_axis=0, tiled=True)
    recv_feats = received[:, :capacity].reshape(-1, slice_width)
    recv_cotan = received[:, capacity : 2 * capacity].reshape(-1, slice_width)
    recv_scale = received[:, 2 * capacity :].reshape(cold_count, -1)[:, :capacity]
    weighted = (
        recv_scale.reshape(-1, 1).astype(jnp.float32) * recv_cotan.astype(jnp.float32)
    ).astype(jnp.bfloat16)
    w_gate = gate_cold[0]
    w_up = up_cold[0]
    w_down = down_cold[0]
    part_gate = jnp.dot(recv_feats, w_gate, preferred_element_type=jnp.float32)
    part_up = jnp.dot(recv_feats, w_up, preferred_element_type=jnp.float32)
    part_hidden = lax.dot_general(
        weighted, w_down, (((1,), (1,)), ((), ())), preferred_element_type=jnp.float32
    )
    all_rows = gathered[:, : 2 * hot_rows].reshape(blocks, 2, hot_count, capacity, slice_width)
    all_rows = jnp.transpose(all_rows, (1, 2, 0, 3, 4)).reshape(
        2, hot_count, blocks * capacity, slice_width
    )
    all_scale = gathered[:, 2 * hot_rows :].reshape(blocks, -1)[:, :hot_rows]
    all_scale = jnp.transpose(all_scale.reshape(blocks, hot_count, capacity), (1, 0, 2))
    rows_feat, rows_cot = all_rows[0], all_rows[1]
    rows_wt = (
        all_scale.reshape(hot_count, blocks * capacity, 1).astype(jnp.float32)
        * rows_cot.astype(jnp.float32)
    ).astype(jnp.bfloat16)
    part_gate_hot = jnp.einsum(
        "jrd,jdh->jrh", rows_feat, gate_hot, preferred_element_type=jnp.float32
    )
    part_up_hot = jnp.einsum("jrd,jdh->jrh", rows_feat, up_hot, preferred_element_type=jnp.float32)
    part_hidden_hot = jnp.einsum(
        "jrd,jhd->jrh", rows_wt, down_hot, preferred_element_type=jnp.float32
    )
    part_cot_hot = jnp.einsum(
        "jrd,jhd->jrh", rows_cot, down_hot, preferred_element_type=jnp.float32
    )
    pre_gate, pre_up, grad_hidden = grp_sum_rounded(
        [part_gate, part_up, part_hidden], [0, 0, 0], "grp"
    )
    pre_gate_hot, pre_up_hot, grad_hidden_hot, cot_down = grp_sum_rounded(
        [part_gate_hot, part_up_hot, part_hidden_hot, part_cot_hot], [1, 1, 1, 1], "grp"
    )
    hidden, back_gate, back_up = swiglu_back(pre_gate, pre_up, grad_hidden)
    output_slice = jnp.dot(hidden, w_down, preferred_element_type=jnp.float32)
    cold_route = jnp.sum(output_slice * recv_cotan.astype(jnp.float32), axis=1)
    cold_route = grp_sum_f32(cold_route.reshape(cold_count, 1, capacity), "grp")
    contract_rows = (((0,), (0,)), ((), ()))
    grad_gate_cold = lax.dot_general(
        recv_feats, back_gate, contract_rows, preferred_element_type=jnp.float32
    )
    grad_up_cold = lax.dot_general(
        recv_feats, back_up, contract_rows, preferred_element_type=jnp.float32
    )
    grad_down_cold = lax.dot_general(
        hidden, weighted, contract_rows, preferred_element_type=jnp.float32
    )
    hidden_hot, back_gate_hot, back_up_hot = swiglu_back(pre_gate_hot, pre_up_hot, grad_hidden_hot)
    hot_route_part = jnp.sum(hidden_hot.astype(jnp.float32) * cot_down, axis=2)
    hidden_blk = hidden_hot.shape[2]
    feat_b = rows_feat.reshape(hot_count, blocks, capacity, slice_width)
    wt_b = rows_wt.reshape(hot_count, blocks, capacity, slice_width)
    bg_b = back_gate_hot.reshape(hot_count, blocks, capacity, hidden_blk)
    bu_b = back_up_hot.reshape(hot_count, blocks, capacity, hidden_blk)
    hid_b = hidden_hot.reshape(hot_count, blocks, capacity, hidden_blk)
    blk_gate = jnp.einsum("jbcd,jbch->jbdh", feat_b, bg_b, preferred_element_type=jnp.float32)
    blk_up = jnp.einsum("jbcd,jbch->jbdh", feat_b, bu_b, preferred_element_type=jnp.float32)
    blk_down = jnp.einsum("jbch,jbcd->jbhd", hid_b, wt_b, preferred_element_type=jnp.float32)
    grad_gate_hot = jnp.sum(blk_gate.astype(jnp.bfloat16).astype(jnp.float32), axis=1)
    grad_up_hot = jnp.sum(blk_up.astype(jnp.bfloat16).astype(jnp.float32), axis=1)
    grad_down_hot = jnp.sum(blk_down.astype(jnp.bfloat16).astype(jnp.float32), axis=1)
    route_parts = jnp.concatenate(
        [
            cold_route,
            jnp.transpose(hot_route_part.reshape(hot_count, blocks, capacity), (1, 0, 2)),
        ],
        axis=1,
    )
    route_back = lax.all_to_all(route_parts, "ep", split_axis=0, concat_axis=0, tiled=True)
    cold_back = route_back[:, 0, :]
    hot_route = jnp.sum(route_back[:, 1:, :], axis=0)
    gate_weight_grad = scatter_routes(cold_hit, cold_sel, cold_back) + scatter_routes(
        hot_hit, hot_sel, hot_route
    )
    return (
        grad_gate_cold[None].astype(jnp.bfloat16),
        grad_up_cold[None].astype(jnp.bfloat16),
        grad_down_cold[None].astype(jnp.bfloat16),
        grad_gate_hot,
        grad_up_hot,
        grad_down_hot,
        gate_weight_grad,
    )


def solution(mesh):
    in_specs = (
        P("ep", "grp"),
        P("ep", "grp"),
        P("ep", None),
        P("ep", None),
        P(),
        P("ep", "grp", None),
        P("ep", "grp", None),
        P("ep", None, "grp"),
        P(None, "grp", "ep"),
        P(None, "grp", "ep"),
        P(None, "ep", "grp"),
    )
    out_specs = (
        P("ep", "grp", None),
        P("ep", "grp", None),
        P("ep", None, "grp"),
        P(None, "grp", "ep"),
        P(None, "grp", "ep"),
        P(None, "ep", "grp"),
        P("ep", None),
    )
    return jax.shard_map(body, mesh=mesh, in_specs=in_specs, out_specs=out_specs, check_vma=False)
```

```python
import jax
import jax.numpy as jnp
from jax import lax
from jax.sharding import PartitionSpec as P


def token_table(expert_ids, targets, capacity):
    hit = expert_ids.T[:, None, :] == targets[None, :, None]
    tok_hit = jnp.any(hit, axis=0)
    rank = jnp.cumsum(tok_hit.astype(jnp.int32), axis=1) - 1
    slots = jnp.arange(capacity, dtype=jnp.int32)
    sel = (rank[:, None, :] == slots[None, :, None]) & tok_hit[:, None, :]
    return hit, sel


def gather_rows(hit, sel, tokens, cotangent, gate_weights):
    count, capacity = sel.shape[0], sel.shape[1]
    token_map = sel.reshape(count * capacity, -1).astype(jnp.bfloat16)
    feat_rows = jnp.dot(token_map, tokens, preferred_element_type=jnp.float32).astype(jnp.bfloat16)
    cotan_rows = jnp.dot(token_map, cotangent, preferred_element_type=jnp.float32).astype(
        jnp.bfloat16
    )
    per_token = jnp.sum(
        jnp.where(hit, gate_weights.T.astype(jnp.float32)[:, None, :], 0.0), axis=0
    )
    scale = jnp.sum(jnp.where(sel, per_token[:, None, :], 0.0), axis=2)
    return feat_rows, cotan_rows, scale.reshape(-1).astype(jnp.bfloat16)


def scatter_routes(hit, sel, values):
    per_token = jnp.sum(jnp.where(sel, values[:, :, None], 0.0), axis=1)
    return jnp.sum(jnp.where(hit, per_token[None, :, :], 0.0), axis=1).T


def swiglu_back(pre_gate, pre_up, grad_hidden):
    sigmoid_gate = jax.nn.sigmoid(pre_gate)
    activated = pre_gate * sigmoid_gate
    hidden = (activated * pre_up).astype(jnp.bfloat16)
    back_gate = (
        grad_hidden * pre_up * sigmoid_gate * (1.0 + pre_gate * (1.0 - sigmoid_gate))
    ).astype(jnp.bfloat16)
    back_up = (grad_hidden * activated).astype(jnp.bfloat16)
    return (hidden, back_gate, back_up)


def grp_sum_f32(x, axis_name):
    size = lax.axis_size(axis_name)
    if size & (size - 1):
        return lax.psum(x, axis_name)
    bit = 1
    while bit < size:
        partner = [(i, i ^ bit) for i in range(size)]
        x = x + lax.ppermute(x, axis_name, partner)
        bit *= 2
    return x


def grp_sum_rounded(parts, axes, axis_name):
    size = lax.axis_size(axis_name)
    rounded = [p.astype(jnp.bfloat16) for p in parts]
    if size == 1:
        return [r.astype(jnp.float32) for r in rounded]
    if size & (size - 1) or any(p.shape[a] % 2 for p, a in zip(parts, axes)):
        return [lax.psum(r, axis_name).astype(jnp.float32) for r in rounded]
    first_core = lax.axis_index(axis_name) % 2 == 0
    halves = [jnp.split(r, 2, axis=a) for r, a in zip(rounded, axes)]
    keep = [jnp.where(first_core, lo, hi) for lo, hi in halves]
    send = [jnp.where(first_core, hi, lo) for lo, hi in halves]
    swap = [(i, i ^ 1) for i in range(size)]
    got = lax.ppermute(send, axis_name, swap)
    sums = [k.astype(jnp.float32) + g.astype(jnp.float32) for k, g in zip(keep, got)]
    bit = 2
    while bit < size:
        partner = [(i, i ^ bit) for i in range(size)]
        mine = [s.astype(jnp.bfloat16) for s in sums]
        got = lax.ppermute(mine, axis_name, partner)
        sums = [m.astype(jnp.float32) + g.astype(jnp.float32) for m, g in zip(mine, got)]
        bit *= 2
    other = lax.ppermute(sums, axis_name, swap)
    full = []
    for s, o, a in zip(sums, other, axes):
        first = jnp.where(first_core, s, o)
        second = jnp.where(first_core, o, s)
        full.append(jnp.concatenate([first, second], axis=a))
    return full


def body(
    tokens,
    cotangent,
    gate_weights,
    expert_ids,
    hot_ids,
    gate_cold,
    up_cold,
    down_cold,
    gate_hot,
    up_hot,
    down_hot,
):
    tok_rows, slice_width = tokens.shape
    top_count = expert_ids.shape[1]
    cold_count = lax.axis_size("ep")
    hot_count = hot_ids.shape[0]
    capacity = tok_rows // 16
    hot_hit, hot_sel = token_table(expert_ids, hot_ids, capacity)
    hot_feats, hot_cotan, hot_scale = gather_rows(hot_hit, hot_sel, tokens, cotangent, gate_weights)
    hot_rows = hot_count * capacity
    scale_lines = -(-hot_rows // slice_width)
    scale_lines = -(-scale_lines // 8) * 8
    scale_block = jnp.pad(hot_scale, (0, scale_lines * slice_width - hot_rows)).reshape(
        scale_lines, slice_width
    )
    blocks = lax.axis_size("ep")
    hot_outgoing = jnp.concatenate([hot_feats, hot_cotan, scale_block], axis=0)
    hot_outgoing, expert_ids, tokens, cotangent, gate_weights = lax.optimization_barrier(
        (hot_outgoing, expert_ids, tokens, cotangent, gate_weights)
    )
    gathered = lax.all_gather(hot_outgoing, "ep", axis=0, tiled=False)
    cold_hit, cold_sel = token_table(
        expert_ids, jnp.arange(cold_count, dtype=jnp.int32), capacity
    )
    cold_feats, cold_cotan, cold_scale = gather_rows(
        cold_hit, cold_sel, tokens, cotangent, gate_weights
    )
    cold_lines = -(-capacity // slice_width)
    cold_lines = -(-cold_lines // 8) * 8
    cold_scale_block = jnp.pad(
        cold_scale.reshape(cold_count, capacity),
        ((0, 0), (0, cold_lines * slice_width - capacity)),
    ).reshape(cold_count, cold_lines, slice_width)
    outgoing = jnp.concatenate(
        [
            cold_feats.reshape(cold_count, capacity, slice_width),
            cold_cotan.reshape(cold_count, capacity, slice_width),
            cold_scale_block,
        ],
        axis=1,
    )
    received = lax.all_to_all(outgoing, "ep", split_axis=0, concat_axis=0, tiled=True)
    recv_feats = received[:, :capacity].reshape(-1, slice_width)
    recv_cotan = received[:, capacity : 2 * capacity].reshape(-1, slice_width)
    recv_scale = received[:, 2 * capacity :].reshape(cold_count, -1)[:, :capacity]
    weighted = (
        recv_scale.reshape(-1, 1).astype(jnp.float32) * recv_cotan.astype(jnp.float32)
    ).astype(jnp.bfloat16)
    w_gate = gate_cold[0]
    w_up = up_cold[0]
    w_down = down_cold[0]
    part_gate = jnp.dot(recv_feats, w_gate, preferred_element_type=jnp.float32)
    part_up = jnp.dot(recv_feats, w_up, preferred_element_type=jnp.float32)
    part_hidden = lax.dot_general(
        weighted, w_down, (((1,), (1,)), ((), ())), preferred_element_type=jnp.float32
    )
    all_rows = gathered[:, : 2 * hot_rows].reshape(blocks, 2, hot_count, capacity, slice_width)
    all_rows = jnp.transpose(all_rows, (1, 2, 0, 3, 4)).reshape(
        2, hot_count, blocks * capacity, slice_width
    )
    all_scale = gathered[:, 2 * hot_rows :].reshape(blocks, -1)[:, :hot_rows]
    all_scale = jnp.transpose(all_scale.reshape(blocks, hot_count, capacity), (1, 0, 2))
    rows_feat, rows_cot = all_rows[0], all_rows[1]
    rows_wt = (
        all_scale.reshape(hot_count, blocks * capacity, 1).astype(jnp.float32)
        * rows_cot.astype(jnp.float32)
    ).astype(jnp.bfloat16)
    part_gate_hot = jnp.einsum(
        "jrd,jdh->jrh", rows_feat, gate_hot, preferred_element_type=jnp.float32
    )
    part_up_hot = jnp.einsum("jrd,jdh->jrh", rows_feat, up_hot, preferred_element_type=jnp.float32)
    part_hidden_hot = jnp.einsum(
        "jrd,jhd->jrh", rows_wt, down_hot, preferred_element_type=jnp.float32
    )
    part_cot_hot = jnp.einsum(
        "jrd,jhd->jrh", rows_cot, down_hot, preferred_element_type=jnp.float32
    )
    (cold_sums,) = grp_sum_rounded([jnp.stack([part_gate, part_up, part_hidden])], [1], "grp")
    pre_gate, pre_up, grad_hidden = cold_sums[0], cold_sums[1], cold_sums[2]
    (hot_sums,) = grp_sum_rounded(
        [jnp.stack([part_gate_hot, part_up_hot, part_hidden_hot, part_cot_hot])], [2], "grp"
    )
    pre_gate_hot, pre_up_hot, grad_hidden_hot, cot_down = (
        hot_sums[0],
        hot_sums[1],
        hot_sums[2],
        hot_sums[3],
    )
    hidden, back_gate, back_up = swiglu_back(pre_gate, pre_up, grad_hidden)
    output_slice = jnp.dot(hidden, w_down, preferred_element_type=jnp.float32)
    cold_route = jnp.sum(output_slice * recv_cotan.astype(jnp.float32), axis=1)
    cold_route = grp_sum_f32(cold_route.reshape(cold_count, 1, capacity), "grp")
    contract_rows = (((0,), (0,)), ((), ()))
    grad_gate_cold = lax.dot_general(
        recv_feats, back_gate, contract_rows, preferred_element_type=jnp.float32
    )
    grad_up_cold = lax.dot_general(
        recv_feats, back_up, contract_rows, preferred_element_type=jnp.float32
    )
    grad_down_cold = lax.dot_general(
        hidden, weighted, contract_rows, preferred_element_type=jnp.float32
    )
    hidden_hot, back_gate_hot, back_up_hot = swiglu_back(pre_gate_hot, pre_up_hot, grad_hidden_hot)
    hot_route_part = jnp.sum(hidden_hot.astype(jnp.float32) * cot_down, axis=2)
    hidden_blk = hidden_hot.shape[2]
    feat_b = rows_feat.reshape(hot_count, blocks, capacity, slice_width)
    wt_b = rows_wt.reshape(hot_count, blocks, capacity, slice_width)
    bg_b = back_gate_hot.reshape(hot_count, blocks, capacity, hidden_blk)
    bu_b = back_up_hot.reshape(hot_count, blocks, capacity, hidden_blk)
    hid_b = hidden_hot.reshape(hot_count, blocks, capacity, hidden_blk)
    blk_gate = jnp.einsum("jbcd,jbch->jbdh", feat_b, bg_b, preferred_element_type=jnp.float32)
    blk_up = jnp.einsum("jbcd,jbch->jbdh", feat_b, bu_b, preferred_element_type=jnp.float32)
    blk_down = jnp.einsum("jbch,jbcd->jbhd", hid_b, wt_b, preferred_element_type=jnp.float32)
    grad_gate_hot = jnp.sum(blk_gate.astype(jnp.bfloat16).astype(jnp.float32), axis=1)
    grad_up_hot = jnp.sum(blk_up.astype(jnp.bfloat16).astype(jnp.float32), axis=1)
    grad_down_hot = jnp.sum(blk_down.astype(jnp.bfloat16).astype(jnp.float32), axis=1)
    route_parts = jnp.concatenate(
        [
            cold_route,
            jnp.transpose(hot_route_part.reshape(hot_count, blocks, capacity), (1, 0, 2)),
        ],
        axis=1,
    )
    route_back = lax.all_to_all(route_parts, "ep", split_axis=0, concat_axis=0, tiled=True)
    cold_back = route_back[:, 0, :]
    hot_route = jnp.sum(route_back[:, 1:, :], axis=0)
    gate_weight_grad = scatter_routes(
        jnp.concatenate([cold_hit, hot_hit], axis=1),
        jnp.concatenate([cold_sel, hot_sel], axis=0),
        jnp.concatenate([cold_back, hot_route], axis=0),
    )
    return (
        grad_gate_cold[None].astype(jnp.bfloat16),
        grad_up_cold[None].astype(jnp.bfloat16),
        grad_down_cold[None].astype(jnp.bfloat16),
        grad_gate_hot,
        grad_up_hot,
        grad_down_hot,
        gate_weight_grad,
    )


def solution(mesh):
    in_specs = (
        P("ep", "grp"),
        P("ep", "grp"),
        P("ep", None),
        P("ep", None),
        P(),
        P("ep", "grp", None),
        P("ep", "grp", None),
        P("ep", None, "grp"),
        P(None, "grp", "ep"),
        P(None, "grp", "ep"),
        P(None, "ep", "grp"),
    )
    out_specs = (
        P("ep", "grp", None),
        P("ep", "grp", None),
        P("ep", None, "grp"),
        P(None, "grp", "ep"),
        P(None, "grp", "ep"),
        P(None, "ep", "grp"),
        P("ep", None),
    )
    return jax.shard_map(body, mesh=mesh, in_specs=in_specs, out_specs=out_specs, check_vma=False)
```

```python
import jax
import jax.numpy as jnp
from jax import lax
from jax.sharding import PartitionSpec as P


def token_table(expert_ids, targets, capacity):
    hit = expert_ids.T[:, None, :] == targets[None, :, None]
    tok_hit = jnp.any(hit, axis=0)
    rank = jnp.cumsum(tok_hit.astype(jnp.int32), axis=1) - 1
    slots = jnp.arange(capacity, dtype=jnp.int32)
    sel = (rank[:, None, :] == slots[None, :, None]) & tok_hit[:, None, :]
    return hit, sel


def gather_rows(hit, sel, tokens, cotangent, gate_weights):
    count, capacity = sel.shape[0], sel.shape[1]
    token_map = sel.reshape(count * capacity, -1).astype(jnp.bfloat16)
    feat_rows = jnp.dot(token_map, tokens, preferred_element_type=jnp.float32).astype(jnp.bfloat16)
    cotan_rows = jnp.dot(token_map, cotangent, preferred_element_type=jnp.float32).astype(
        jnp.bfloat16
    )
    per_token = jnp.sum(
        jnp.where(hit, gate_weights.T.astype(jnp.float32)[:, None, :], 0.0), axis=0
    )
    scale = jnp.sum(jnp.where(sel, per_token[:, None, :], 0.0), axis=2)
    return feat_rows, cotan_rows, scale.reshape(-1).astype(jnp.bfloat16)


def scatter_routes(hit, sel, values):
    per_token = jnp.sum(jnp.where(sel, values[:, :, None], 0.0), axis=1)
    return jnp.sum(jnp.where(hit, per_token[None, :, :], 0.0), axis=1).T


def swiglu_back(pre_gate, pre_up, grad_hidden):
    sigmoid_gate = jax.nn.sigmoid(pre_gate)
    activated = pre_gate * sigmoid_gate
    hidden = (activated * pre_up).astype(jnp.bfloat16)
    back_gate = (
        grad_hidden * pre_up * sigmoid_gate * (1.0 + pre_gate * (1.0 - sigmoid_gate))
    ).astype(jnp.bfloat16)
    back_up = (grad_hidden * activated).astype(jnp.bfloat16)
    return (hidden, back_gate, back_up)


def grp_sum_f32(x, axis_name):
    size = lax.axis_size(axis_name)
    if size & (size - 1):
        return lax.psum(x, axis_name)
    bit = 1
    while bit < size:
        partner = [(i, i ^ bit) for i in range(size)]
        x = x + lax.ppermute(x, axis_name, partner)
        bit *= 2
    return x


def grp_sum_rounded(parts, axes, axis_name):
    size = lax.axis_size(axis_name)
    rounded = [p.astype(jnp.bfloat16) for p in parts]
    if size == 1:
        return [r.astype(jnp.float32) for r in rounded]
    if size & (size - 1) or any(p.shape[a] % 2 for p, a in zip(parts, axes)):
        return [lax.psum(r, axis_name).astype(jnp.float32) for r in rounded]
    first_core = lax.axis_index(axis_name) % 2 == 0
    halves = [jnp.split(r, 2, axis=a) for r, a in zip(rounded, axes)]
    keep = [jnp.where(first_core, lo, hi) for lo, hi in halves]
    send = [jnp.where(first_core, hi, lo) for lo, hi in halves]
    swap = [(i, i ^ 1) for i in range(size)]
    got = lax.ppermute(send, axis_name, swap)
    sums = [k.astype(jnp.float32) + g.astype(jnp.float32) for k, g in zip(keep, got)]
    bit = 2
    while bit < size:
        partner = [(i, i ^ bit) for i in range(size)]
        mine = [s.astype(jnp.bfloat16) for s in sums]
        got = lax.ppermute(mine, axis_name, partner)
        sums = [m.astype(jnp.float32) + g.astype(jnp.float32) for m, g in zip(mine, got)]
        bit *= 2
    other = lax.ppermute(sums, axis_name, swap)
    full = []
    for s, o, a in zip(sums, other, axes):
        first = jnp.where(first_core, s, o)
        second = jnp.where(first_core, o, s)
        full.append(jnp.concatenate([first, second], axis=a))
    return full


def body(
    tokens,
    cotangent,
    gate_weights,
    expert_ids,
    hot_ids,
    gate_cold,
    up_cold,
    down_cold,
    gate_hot,
    up_hot,
    down_hot,
):
    tok_rows, slice_width = tokens.shape
    top_count = expert_ids.shape[1]
    cold_count = lax.axis_size("ep")
    hot_count = hot_ids.shape[0]
    capacity = tok_rows // 16
    hot_hit, hot_sel = token_table(expert_ids, hot_ids, capacity)
    hot_feats, hot_cotan, hot_scale = gather_rows(hot_hit, hot_sel, tokens, cotangent, gate_weights)
    hot_rows = hot_count * capacity
    scale_lines = -(-hot_rows // slice_width)
    scale_lines = -(-scale_lines // 8) * 8
    scale_block = jnp.pad(hot_scale, (0, scale_lines * slice_width - hot_rows)).reshape(
        scale_lines, slice_width
    )
    blocks = lax.axis_size("ep")
    hot_outgoing = jnp.concatenate([hot_feats, hot_cotan, scale_block], axis=0)
    hot_outgoing, expert_ids, tokens, cotangent, gate_weights = lax.optimization_barrier(
        (hot_outgoing, expert_ids, tokens, cotangent, gate_weights)
    )
    gathered = lax.all_gather(hot_outgoing, "ep", axis=0, tiled=False)
    cold_hit, cold_sel = token_table(
        expert_ids, jnp.arange(cold_count, dtype=jnp.int32), capacity
    )
    cold_feats, cold_cotan, cold_scale = gather_rows(
        cold_hit, cold_sel, tokens, cotangent, gate_weights
    )
    cold_lines = -(-capacity // slice_width)
    cold_lines = -(-cold_lines // 8) * 8
    cold_scale_block = jnp.pad(
        cold_scale.reshape(cold_count, capacity),
        ((0, 0), (0, cold_lines * slice_width - capacity)),
    ).reshape(cold_count, cold_lines, slice_width)
    outgoing = jnp.concatenate(
        [
            cold_feats.reshape(cold_count, capacity, slice_width),
            cold_cotan.reshape(cold_count, capacity, slice_width),
            cold_scale_block,
        ],
        axis=1,
    )
    received = lax.all_to_all(outgoing, "ep", split_axis=0, concat_axis=0, tiled=True)
    recv_feats = received[:, :capacity].reshape(-1, slice_width)
    recv_cotan = received[:, capacity : 2 * capacity].reshape(-1, slice_width)
    recv_scale = received[:, 2 * capacity :].reshape(cold_count, -1)[:, :capacity]
    weighted = (
        recv_scale.reshape(-1, 1).astype(jnp.float32) * recv_cotan.astype(jnp.float32)
    ).astype(jnp.bfloat16)
    w_gate = gate_cold[0]
    w_up = up_cold[0]
    w_down = down_cold[0]
    part_gate = jnp.dot(recv_feats, w_gate, preferred_element_type=jnp.float32)
    part_up = jnp.dot(recv_feats, w_up, preferred_element_type=jnp.float32)
    part_hidden = lax.dot_general(
        weighted, w_down, (((1,), (1,)), ((), ())), preferred_element_type=jnp.float32
    )
    all_rows = gathered[:, : 2 * hot_rows].reshape(blocks, 2, hot_count, capacity, slice_width)
    all_rows = jnp.transpose(all_rows, (1, 2, 0, 3, 4)).reshape(
        2, hot_count, blocks * capacity, slice_width
    )
    all_scale = gathered[:, 2 * hot_rows :].reshape(blocks, -1)[:, :hot_rows]
    all_scale = jnp.transpose(all_scale.reshape(blocks, hot_count, capacity), (1, 0, 2))
    rows_feat, rows_cot = all_rows[0], all_rows[1]
    rows_wt = (
        all_scale.reshape(hot_count, blocks * capacity, 1).astype(jnp.float32)
        * rows_cot.astype(jnp.float32)
    ).astype(jnp.bfloat16)
    part_gate_hot = jnp.einsum(
        "jrd,jdh->jrh", rows_feat, gate_hot, preferred_element_type=jnp.float32
    )
    part_up_hot = jnp.einsum("jrd,jdh->jrh", rows_feat, up_hot, preferred_element_type=jnp.float32)
    part_hidden_hot = jnp.einsum(
        "jrd,jhd->jrh", rows_wt, down_hot, preferred_element_type=jnp.float32
    )
    part_cot_hot = jnp.einsum(
        "jrd,jhd->jrh", rows_cot, down_hot, preferred_element_type=jnp.float32
    )
    pre_gate, pre_up, grad_hidden = grp_sum_rounded(
        [part_gate, part_up, part_hidden], [0, 0, 0], "grp"
    )
    pre_gate_hot, pre_up_hot, grad_hidden_hot, cot_down = grp_sum_rounded(
        [part_gate_hot, part_up_hot, part_hidden_hot, part_cot_hot], [1, 1, 1, 1], "grp"
    )
    hidden, back_gate, back_up = swiglu_back(pre_gate, pre_up, grad_hidden)
    output_slice = jnp.dot(hidden, w_down, preferred_element_type=jnp.float32)
    cold_route = jnp.sum(output_slice * recv_cotan.astype(jnp.float32), axis=1)
    cold_route = grp_sum_f32(cold_route.reshape(cold_count, 1, capacity), "grp")
    contract_rows = (((0,), (0,)), ((), ()))
    grad_gate_cold = lax.dot_general(
        recv_feats, back_gate, contract_rows, preferred_element_type=jnp.float32
    )
    grad_up_cold = lax.dot_general(
        recv_feats, back_up, contract_rows, preferred_element_type=jnp.float32
    )
    grad_down_cold = lax.dot_general(
        hidden, weighted, contract_rows, preferred_element_type=jnp.float32
    )
    hidden_hot, back_gate_hot, back_up_hot = swiglu_back(pre_gate_hot, pre_up_hot, grad_hidden_hot)
    hot_route_part = jnp.sum(hidden_hot.astype(jnp.float32) * cot_down, axis=2)
    grad_gate_hot = jnp.einsum(
        "jrd,jrh->jdh", rows_feat, back_gate_hot, preferred_element_type=jnp.float32
    )
    grad_up_hot = jnp.einsum("jrd,jrh->jdh", rows_feat, back_up_hot, preferred_element_type=jnp.float32)
    grad_down_hot = jnp.einsum(
        "jrh,jrd->jhd", hidden_hot, rows_wt, preferred_element_type=jnp.float32
    )
    route_parts = jnp.concatenate(
        [
            cold_route,
            jnp.transpose(hot_route_part.reshape(hot_count, blocks, capacity), (1, 0, 2)),
        ],
        axis=1,
    )
    route_back = lax.all_to_all(route_parts, "ep", split_axis=0, concat_axis=0, tiled=True)
    cold_back = route_back[:, 0, :]
    hot_route = jnp.sum(route_back[:, 1:, :], axis=0)
    gate_weight_grad = scatter_routes(
        jnp.concatenate([cold_hit, hot_hit], axis=1),
        jnp.concatenate([cold_sel, hot_sel], axis=0),
        jnp.concatenate([cold_back, hot_route], axis=0),
    )
    return (
        grad_gate_cold[None].astype(jnp.bfloat16),
        grad_up_cold[None].astype(jnp.bfloat16),
        grad_down_cold[None].astype(jnp.bfloat16),
        grad_gate_hot,
        grad_up_hot,
        grad_down_hot,
        gate_weight_grad,
    )


def solution(mesh):
    in_specs = (
        P("ep", "grp"),
        P("ep", "grp"),
        P("ep", None),
        P("ep", None),
        P(),
        P("ep", "grp", None),
        P("ep", "grp", None),
        P("ep", None, "grp"),
        P(None, "grp", "ep"),
        P(None, "grp", "ep"),
        P(None, "ep", "grp"),
    )
    out_specs = (
        P("ep", "grp", None),
        P("ep", "grp", None),
        P("ep", None, "grp"),
        P(None, "grp", "ep"),
        P(None, "grp", "ep"),
        P(None, "ep", "grp"),
        P("ep", None),
    )
    return jax.shard_map(body, mesh=mesh, in_specs=in_specs, out_specs=out_specs, check_vma=False)
```

```python
import jax
import jax.numpy as jnp
from jax import lax
from jax.sharding import PartitionSpec as P


def token_table(expert_ids, targets, capacity):
    hit = expert_ids.T[:, None, :] == targets[None, :, None]
    tok_hit = jnp.any(hit, axis=0)
    rank = jnp.cumsum(tok_hit.astype(jnp.int32), axis=1) - 1
    slots = jnp.arange(capacity, dtype=jnp.int32)
    sel = (rank[:, None, :] == slots[None, :, None]) & tok_hit[:, None, :]
    return hit, sel


def gather_rows(hit, sel, tokens, cotangent, gate_weights):
    count, capacity = sel.shape[0], sel.shape[1]
    token_map = sel.reshape(count * capacity, -1).astype(jnp.bfloat16)
    feat_rows = jnp.dot(token_map, tokens, preferred_element_type=jnp.float32).astype(jnp.bfloat16)
    cotan_rows = jnp.dot(token_map, cotangent, preferred_element_type=jnp.float32).astype(
        jnp.bfloat16
    )
    per_token = jnp.sum(
        jnp.where(hit, gate_weights.T.astype(jnp.float32)[:, None, :], 0.0), axis=0
    )
    scale = jnp.sum(jnp.where(sel, per_token[:, None, :], 0.0), axis=2)
    return feat_rows, cotan_rows, scale.reshape(-1).astype(jnp.bfloat16)


def scatter_routes(hit, sel, values):
    per_token = jnp.sum(jnp.where(sel, values[:, :, None], 0.0), axis=1)
    return jnp.sum(jnp.where(hit, per_token[None, :, :], 0.0), axis=1).T


def swiglu_back(pre_gate, pre_up, grad_hidden):
    sigmoid_gate = jax.nn.sigmoid(pre_gate)
    activated = pre_gate * sigmoid_gate
    hidden = (activated * pre_up).astype(jnp.bfloat16)
    back_gate = (
        grad_hidden * pre_up * sigmoid_gate * (1.0 + pre_gate * (1.0 - sigmoid_gate))
    ).astype(jnp.bfloat16)
    back_up = (grad_hidden * activated).astype(jnp.bfloat16)
    return (hidden, back_gate, back_up)


def grp_sum_f32(x, axis_name):
    size = lax.axis_size(axis_name)
    if size & (size - 1):
        return lax.psum(x, axis_name)
    bit = 1
    while bit < size:
        partner = [(i, i ^ bit) for i in range(size)]
        x = x + lax.ppermute(x, axis_name, partner)
        bit *= 2
    return x


def grp_sum_doubling(parts, axis_name):
    size = lax.axis_size(axis_name)
    mine = [p.astype(jnp.bfloat16) for p in parts]
    if size & (size - 1):
        return [lax.psum(r, axis_name).astype(jnp.float32) for r in mine]
    sums = [r.astype(jnp.float32) for r in mine]
    bit = 1
    while bit < size:
        partner = [(i, i ^ bit) for i in range(size)]
        got = lax.ppermute(mine, axis_name, partner)
        sums = [m.astype(jnp.float32) + g.astype(jnp.float32) for m, g in zip(mine, got)]
        mine = [s.astype(jnp.bfloat16) for s in sums]
        bit *= 2
    return sums


def grp_sum_rounded(parts, axes, axis_name):
    size = lax.axis_size(axis_name)
    rounded = [p.astype(jnp.bfloat16) for p in parts]
    if size == 1:
        return [r.astype(jnp.float32) for r in rounded]
    if size & (size - 1) or any(p.shape[a] % 2 for p, a in zip(parts, axes)):
        return [lax.psum(r, axis_name).astype(jnp.float32) for r in rounded]
    first_core = lax.axis_index(axis_name) % 2 == 0
    halves = [jnp.split(r, 2, axis=a) for r, a in zip(rounded, axes)]
    keep = [jnp.where(first_core, lo, hi) for lo, hi in halves]
    send = [jnp.where(first_core, hi, lo) for lo, hi in halves]
    swap = [(i, i ^ 1) for i in range(size)]
    got = lax.ppermute(send, axis_name, swap)
    sums = [k.astype(jnp.float32) + g.astype(jnp.float32) for k, g in zip(keep, got)]
    bit = 2
    while bit < size:
        partner = [(i, i ^ bit) for i in range(size)]
        mine = [s.astype(jnp.bfloat16) for s in sums]
        got = lax.ppermute(mine, axis_name, partner)
        sums = [m.astype(jnp.float32) + g.astype(jnp.float32) for m, g in zip(mine, got)]
        bit *= 2
    other = lax.ppermute(sums, axis_name, swap)
    full = []
    for s, o, a in zip(sums, other, axes):
        first = jnp.where(first_core, s, o)
        second = jnp.where(first_core, o, s)
        full.append(jnp.concatenate([first, second], axis=a))
    return full


def body(
    tokens,
    cotangent,
    gate_weights,
    expert_ids,
    hot_ids,
    gate_cold,
    up_cold,
    down_cold,
    gate_hot,
    up_hot,
    down_hot,
):
    tok_rows, slice_width = tokens.shape
    top_count = expert_ids.shape[1]
    cold_count = lax.axis_size("ep")
    hot_count = hot_ids.shape[0]
    capacity = tok_rows // 16
    hot_hit, hot_sel = token_table(expert_ids, hot_ids, capacity)
    hot_feats, hot_cotan, hot_scale = gather_rows(hot_hit, hot_sel, tokens, cotangent, gate_weights)
    hot_rows = hot_count * capacity
    scale_lines = -(-hot_rows // slice_width)
    scale_lines = -(-scale_lines // 8) * 8
    scale_block = jnp.pad(hot_scale, (0, scale_lines * slice_width - hot_rows)).reshape(
        scale_lines, slice_width
    )
    blocks = lax.axis_size("ep")
    hot_outgoing = jnp.concatenate([hot_feats, hot_cotan, scale_block], axis=0)
    hot_outgoing, expert_ids, tokens, cotangent, gate_weights = lax.optimization_barrier(
        (hot_outgoing, expert_ids, tokens, cotangent, gate_weights)
    )
    gathered = lax.all_gather(hot_outgoing, "ep", axis=0, tiled=False)
    cold_hit, cold_sel = token_table(
        expert_ids, jnp.arange(cold_count, dtype=jnp.int32), capacity
    )
    cold_feats, cold_cotan, cold_scale = gather_rows(
        cold_hit, cold_sel, tokens, cotangent, gate_weights
    )
    cold_lines = -(-capacity // slice_width)
    cold_lines = -(-cold_lines // 8) * 8
    cold_scale_block = jnp.pad(
        cold_scale.reshape(cold_count, capacity),
        ((0, 0), (0, cold_lines * slice_width - capacity)),
    ).reshape(cold_count, cold_lines, slice_width)
    outgoing = jnp.concatenate(
        [
            cold_feats.reshape(cold_count, capacity, slice_width),
            cold_cotan.reshape(cold_count, capacity, slice_width),
            cold_scale_block,
        ],
        axis=1,
    )
    received = lax.all_to_all(outgoing, "ep", split_axis=0, concat_axis=0, tiled=True)
    recv_feats = received[:, :capacity].reshape(-1, slice_width)
    recv_cotan = received[:, capacity : 2 * capacity].reshape(-1, slice_width)
    recv_scale = received[:, 2 * capacity :].reshape(cold_count, -1)[:, :capacity]
    weighted = (
        recv_scale.reshape(-1, 1).astype(jnp.float32) * recv_cotan.astype(jnp.float32)
    ).astype(jnp.bfloat16)
    w_gate = gate_cold[0]
    w_up = up_cold[0]
    w_down = down_cold[0]
    part_gate = jnp.dot(recv_feats, w_gate, preferred_element_type=jnp.float32)
    part_up = jnp.dot(recv_feats, w_up, preferred_element_type=jnp.float32)
    part_hidden = lax.dot_general(
        weighted, w_down, (((1,), (1,)), ((), ())), preferred_element_type=jnp.float32
    )
    all_rows = gathered[:, : 2 * hot_rows].reshape(blocks, 2, hot_count, capacity, slice_width)
    all_rows = jnp.transpose(all_rows, (1, 2, 0, 3, 4)).reshape(
        2, hot_count, blocks * capacity, slice_width
    )
    all_scale = gathered[:, 2 * hot_rows :].reshape(blocks, -1)[:, :hot_rows]
    all_scale = jnp.transpose(all_scale.reshape(blocks, hot_count, capacity), (1, 0, 2))
    rows_feat, rows_cot = all_rows[0], all_rows[1]
    rows_wt = (
        all_scale.reshape(hot_count, blocks * capacity, 1).astype(jnp.float32)
        * rows_cot.astype(jnp.float32)
    ).astype(jnp.bfloat16)
    part_gate_hot = jnp.einsum(
        "jrd,jdh->jrh", rows_feat, gate_hot, preferred_element_type=jnp.float32
    )
    part_up_hot = jnp.einsum("jrd,jdh->jrh", rows_feat, up_hot, preferred_element_type=jnp.float32)
    part_hidden_hot = jnp.einsum(
        "jrd,jhd->jrh", rows_wt, down_hot, preferred_element_type=jnp.float32
    )
    part_cot_hot = jnp.einsum(
        "jrd,jhd->jrh", rows_cot, down_hot, preferred_element_type=jnp.float32
    )
    pre_gate, pre_up, grad_hidden = grp_sum_rounded(
        [part_gate, part_up, part_hidden], [0, 0, 0], "grp"
    )
    pre_gate_hot, pre_up_hot, grad_hidden_hot, cot_down = grp_sum_doubling(
        [part_gate_hot, part_up_hot, part_hidden_hot, part_cot_hot], "grp"
    )
    hidden, back_gate, back_up = swiglu_back(pre_gate, pre_up, grad_hidden)
    output_slice = jnp.dot(hidden, w_down, preferred_element_type=jnp.float32)
    cold_route = jnp.sum(output_slice * recv_cotan.astype(jnp.float32), axis=1)
    cold_route = grp_sum_f32(cold_route.reshape(cold_count, 1, capacity), "grp")
    contract_rows = (((0,), (0,)), ((), ()))
    grad_gate_cold = lax.dot_general(
        recv_feats, back_gate, contract_rows, preferred_element_type=jnp.float32
    )
    grad_up_cold = lax.dot_general(
        recv_feats, back_up, contract_rows, preferred_element_type=jnp.float32
    )
    grad_down_cold = lax.dot_general(
        hidden, weighted, contract_rows, preferred_element_type=jnp.float32
    )
    hidden_hot, back_gate_hot, back_up_hot = swiglu_back(pre_gate_hot, pre_up_hot, grad_hidden_hot)
    hot_route_part = jnp.sum(hidden_hot.astype(jnp.float32) * cot_down, axis=2)
    grad_gate_hot = jnp.einsum(
        "jrd,jrh->jdh", rows_feat, back_gate_hot, preferred_element_type=jnp.float32
    )
    grad_up_hot = jnp.einsum("jrd,jrh->jdh", rows_feat, back_up_hot, preferred_element_type=jnp.float32)
    grad_down_hot = jnp.einsum(
        "jrh,jrd->jhd", hidden_hot, rows_wt, preferred_element_type=jnp.float32
    )
    route_parts = jnp.concatenate(
        [
            cold_route,
            jnp.transpose(hot_route_part.reshape(hot_count, blocks, capacity), (1, 0, 2)),
        ],
        axis=1,
    )
    route_back = lax.all_to_all(route_parts, "ep", split_axis=0, concat_axis=0, tiled=True)
    cold_back = route_back[:, 0, :]
    hot_route = jnp.sum(route_back[:, 1:, :], axis=0)
    gate_weight_grad = scatter_routes(
        jnp.concatenate([cold_hit, hot_hit], axis=1),
        jnp.concatenate([cold_sel, hot_sel], axis=0),
        jnp.concatenate([cold_back, hot_route], axis=0),
    )
    return (
        grad_gate_cold[None].astype(jnp.bfloat16),
        grad_up_cold[None].astype(jnp.bfloat16),
        grad_down_cold[None].astype(jnp.bfloat16),
        grad_gate_hot,
        grad_up_hot,
        grad_down_hot,
        gate_weight_grad,
    )


def solution(mesh):
    in_specs = (
        P("ep", "grp"),
        P("ep", "grp"),
        P("ep", None),
        P("ep", None),
        P(),
        P("ep", "grp", None),
        P("ep", "grp", None),
        P("ep", None, "grp"),
        P(None, "grp", "ep"),
        P(None, "grp", "ep"),
        P(None, "ep", "grp"),
    )
    out_specs = (
        P("ep", "grp", None),
        P("ep", "grp", None),
        P("ep", None, "grp"),
        P(None, "grp", "ep"),
        P(None, "grp", "ep"),
        P(None, "ep", "grp"),
        P("ep", None),
    )
    return jax.shard_map(body, mesh=mesh, in_specs=in_specs, out_specs=out_specs, check_vma=False)
```

```python
import jax
import jax.numpy as jnp
from jax import lax
from jax.sharding import PartitionSpec as P


def token_table(expert_ids, targets, capacity):
    hit = expert_ids.T[:, None, :] == targets[None, :, None]
    tok_hit = jnp.any(hit, axis=0)
    rank = jnp.cumsum(tok_hit.astype(jnp.int32), axis=1) - 1
    slots = jnp.arange(capacity, dtype=jnp.int32)
    sel = (rank[:, None, :] == slots[None, :, None]) & tok_hit[:, None, :]
    return hit, sel


def gather_rows(hit, sel, tokens, cotangent, gate_weights):
    count, capacity = sel.shape[0], sel.shape[1]
    token_map = sel.reshape(count * capacity, -1).astype(jnp.bfloat16)
    feat_rows = jnp.dot(token_map, tokens, preferred_element_type=jnp.float32).astype(jnp.bfloat16)
    cotan_rows = jnp.dot(token_map, cotangent, preferred_element_type=jnp.float32).astype(
        jnp.bfloat16
    )
    per_token = jnp.sum(
        jnp.where(hit, gate_weights.T.astype(jnp.float32)[:, None, :], 0.0), axis=0
    )
    scale = jnp.sum(jnp.where(sel, per_token[:, None, :], 0.0), axis=2)
    return feat_rows, cotan_rows, scale.reshape(-1).astype(jnp.bfloat16)


def scatter_routes(hit, sel, values):
    per_token = jnp.sum(jnp.where(sel, values[:, :, None], 0.0), axis=1)
    return jnp.sum(jnp.where(hit, per_token[None, :, :], 0.0), axis=1).T


def swiglu_back(pre_gate, pre_up, grad_hidden):
    sigmoid_gate = jax.nn.sigmoid(pre_gate)
    activated = pre_gate * sigmoid_gate
    hidden = (activated * pre_up).astype(jnp.bfloat16)
    back_gate = (
        grad_hidden * pre_up * sigmoid_gate * (1.0 + pre_gate * (1.0 - sigmoid_gate))
    ).astype(jnp.bfloat16)
    back_up = (grad_hidden * activated).astype(jnp.bfloat16)
    return (hidden, back_gate, back_up)


def grp_sum_f32(x, axis_name):
    size = lax.axis_size(axis_name)
    if size & (size - 1):
        return lax.psum(x, axis_name)
    bit = 1
    while bit < size:
        partner = [(i, i ^ bit) for i in range(size)]
        x = x + lax.ppermute(x, axis_name, partner)
        bit *= 2
    return x


def grp_sum_doubling(parts, axis_name):
    size = lax.axis_size(axis_name)
    mine = [p.astype(jnp.bfloat16) for p in parts]
    if size & (size - 1):
        return [lax.psum(r, axis_name).astype(jnp.float32) for r in mine]
    sums = [r.astype(jnp.float32) for r in mine]
    bit = 1
    while bit < size:
        partner = [(i, i ^ bit) for i in range(size)]
        got = lax.ppermute(mine, axis_name, partner)
        sums = [m.astype(jnp.float32) + g.astype(jnp.float32) for m, g in zip(mine, got)]
        mine = [s.astype(jnp.bfloat16) for s in sums]
        bit *= 2
    return sums


def grp_sum_rounded(parts, axes, axis_name):
    size = lax.axis_size(axis_name)
    rounded = [p.astype(jnp.bfloat16) for p in parts]
    if size == 1:
        return [r.astype(jnp.float32) for r in rounded]
    if size & (size - 1) or any(p.shape[a] % 2 for p, a in zip(parts, axes)):
        return [lax.psum(r, axis_name).astype(jnp.float32) for r in rounded]
    first_core = lax.axis_index(axis_name) % 2 == 0
    halves = [jnp.split(r, 2, axis=a) for r, a in zip(rounded, axes)]
    keep = [jnp.where(first_core, lo, hi) for lo, hi in halves]
    send = [jnp.where(first_core, hi, lo) for lo, hi in halves]
    swap = [(i, i ^ 1) for i in range(size)]
    got = lax.ppermute(send, axis_name, swap)
    sums = [k.astype(jnp.float32) + g.astype(jnp.float32) for k, g in zip(keep, got)]
    bit = 2
    while bit < size:
        partner = [(i, i ^ bit) for i in range(size)]
        mine = [s.astype(jnp.bfloat16) for s in sums]
        got = lax.ppermute(mine, axis_name, partner)
        sums = [m.astype(jnp.float32) + g.astype(jnp.float32) for m, g in zip(mine, got)]
        bit *= 2
    other = lax.ppermute(sums, axis_name, swap)
    full = []
    for s, o, a in zip(sums, other, axes):
        first = jnp.where(first_core, s, o)
        second = jnp.where(first_core, o, s)
        full.append(jnp.concatenate([first, second], axis=a))
    return full


def body(
    tokens,
    cotangent,
    gate_weights,
    expert_ids,
    hot_ids,
    gate_cold,
    up_cold,
    down_cold,
    gate_hot,
    up_hot,
    down_hot,
):
    tok_rows, slice_width = tokens.shape
    top_count = expert_ids.shape[1]
    cold_count = lax.axis_size("ep")
    hot_count = hot_ids.shape[0]
    capacity = tok_rows // 16
    blocks = lax.axis_size("ep")
    targets = jnp.concatenate([jnp.arange(cold_count, dtype=jnp.int32), hot_ids])
    all_hit, all_sel = token_table(expert_ids, targets, capacity)
    feats_all, cotan_all, scale_all = gather_rows(all_hit, all_sel, tokens, cotangent, gate_weights)
    cold_total = cold_count * capacity
    hot_feats, hot_cotan, hot_scale = (
        feats_all[cold_total:],
        cotan_all[cold_total:],
        scale_all[cold_total:],
    )
    cold_feats, cold_cotan, cold_scale = (
        feats_all[:cold_total],
        cotan_all[:cold_total],
        scale_all[:cold_total],
    )
    hot_rows = hot_count * capacity
    scale_lines = -(-hot_rows // slice_width)
    scale_lines = -(-scale_lines // 8) * 8
    scale_block = jnp.pad(hot_scale, (0, scale_lines * slice_width - hot_rows)).reshape(
        scale_lines, slice_width
    )
    hot_outgoing = jnp.concatenate([hot_feats, hot_cotan, scale_block], axis=0)
    gathered = lax.all_gather(hot_outgoing, "ep", axis=0, tiled=False)
    cold_lines = -(-capacity // slice_width)
    cold_lines = -(-cold_lines // 8) * 8
    cold_scale_block = jnp.pad(
        cold_scale.reshape(cold_count, capacity),
        ((0, 0), (0, cold_lines * slice_width - capacity)),
    ).reshape(cold_count, cold_lines, slice_width)
    outgoing = jnp.concatenate(
        [
            cold_feats.reshape(cold_count, capacity, slice_width),
            cold_cotan.reshape(cold_count, capacity, slice_width),
            cold_scale_block,
        ],
        axis=1,
    )
    received = lax.all_to_all(outgoing, "ep", split_axis=0, concat_axis=0, tiled=True)
    recv_feats = received[:, :capacity].reshape(-1, slice_width)
    recv_cotan = received[:, capacity : 2 * capacity].reshape(-1, slice_width)
    recv_scale = received[:, 2 * capacity :].reshape(cold_count, -1)[:, :capacity]
    weighted = (
        recv_scale.reshape(-1, 1).astype(jnp.float32) * recv_cotan.astype(jnp.float32)
    ).astype(jnp.bfloat16)
    w_gate = gate_cold[0]
    w_up = up_cold[0]
    w_down = down_cold[0]
    part_gate = jnp.dot(recv_feats, w_gate, preferred_element_type=jnp.float32)
    part_up = jnp.dot(recv_feats, w_up, preferred_element_type=jnp.float32)
    part_hidden = lax.dot_general(
        weighted, w_down, (((1,), (1,)), ((), ())), preferred_element_type=jnp.float32
    )
    all_rows = gathered[:, : 2 * hot_rows].reshape(blocks, 2, hot_count, capacity, slice_width)
    all_rows = jnp.transpose(all_rows, (1, 2, 0, 3, 4)).reshape(
        2, hot_count, blocks * capacity, slice_width
    )
    all_scale = gathered[:, 2 * hot_rows :].reshape(blocks, -1)[:, :hot_rows]
    all_scale = jnp.transpose(all_scale.reshape(blocks, hot_count, capacity), (1, 0, 2))
    rows_feat, rows_cot = all_rows[0], all_rows[1]
    rows_wt = (
        all_scale.reshape(hot_count, blocks * capacity, 1).astype(jnp.float32)
        * rows_cot.astype(jnp.float32)
    ).astype(jnp.bfloat16)
    part_gate_hot = jnp.einsum(
        "jrd,jdh->jrh", rows_feat, gate_hot, preferred_element_type=jnp.float32
    )
    part_up_hot = jnp.einsum("jrd,jdh->jrh", rows_feat, up_hot, preferred_element_type=jnp.float32)
    part_hidden_hot = jnp.einsum(
        "jrd,jhd->jrh", rows_wt, down_hot, preferred_element_type=jnp.float32
    )
    part_cot_hot = jnp.einsum(
        "jrd,jhd->jrh", rows_cot, down_hot, preferred_element_type=jnp.float32
    )
    pre_gate, pre_up, grad_hidden = grp_sum_rounded(
        [part_gate, part_up, part_hidden], [0, 0, 0], "grp"
    )
    pre_gate_hot, pre_up_hot, grad_hidden_hot, cot_down = grp_sum_doubling(
        [part_gate_hot, part_up_hot, part_hidden_hot, part_cot_hot], "grp"
    )
    hidden, back_gate, back_up = swiglu_back(pre_gate, pre_up, grad_hidden)
    output_slice = jnp.dot(hidden, w_down, preferred_element_type=jnp.float32)
    cold_route = jnp.sum(output_slice * recv_cotan.astype(jnp.float32), axis=1)
    cold_route = grp_sum_f32(cold_route.reshape(cold_count, 1, capacity), "grp")
    contract_rows = (((0,), (0,)), ((), ()))
    grad_gate_cold = lax.dot_general(
        recv_feats, back_gate, contract_rows, preferred_element_type=jnp.float32
    )
    grad_up_cold = lax.dot_general(
        recv_feats, back_up, contract_rows, preferred_element_type=jnp.float32
    )
    grad_down_cold = lax.dot_general(
        hidden, weighted, contract_rows, preferred_element_type=jnp.float32
    )
    hidden_hot, back_gate_hot, back_up_hot = swiglu_back(pre_gate_hot, pre_up_hot, grad_hidden_hot)
    hot_route_part = jnp.sum(hidden_hot.astype(jnp.float32) * cot_down, axis=2)
    grad_gate_hot = jnp.einsum(
        "jrd,jrh->jdh", rows_feat, back_gate_hot, preferred_element_type=jnp.float32
    )
    grad_up_hot = jnp.einsum("jrd,jrh->jdh", rows_feat, back_up_hot, preferred_element_type=jnp.float32)
    grad_down_hot = jnp.einsum(
        "jrh,jrd->jhd", hidden_hot, rows_wt, preferred_element_type=jnp.float32
    )
    route_parts = jnp.concatenate(
        [
            cold_route,
            jnp.transpose(hot_route_part.reshape(hot_count, blocks, capacity), (1, 0, 2)),
        ],
        axis=1,
    )
    route_back = lax.all_to_all(route_parts, "ep", split_axis=0, concat_axis=0, tiled=True)
    cold_back = route_back[:, 0, :]
    hot_route = jnp.sum(route_back[:, 1:, :], axis=0)
    gate_weight_grad = scatter_routes(
        all_hit, all_sel, jnp.concatenate([cold_back, hot_route], axis=0)
    )
    return (
        grad_gate_cold[None].astype(jnp.bfloat16),
        grad_up_cold[None].astype(jnp.bfloat16),
        grad_down_cold[None].astype(jnp.bfloat16),
        grad_gate_hot,
        grad_up_hot,
        grad_down_hot,
        gate_weight_grad,
    )


def solution(mesh):
    in_specs = (
        P("ep", "grp"),
        P("ep", "grp"),
        P("ep", None),
        P("ep", None),
        P(),
        P("ep", "grp", None),
        P("ep", "grp", None),
        P("ep", None, "grp"),
        P(None, "grp", "ep"),
        P(None, "grp", "ep"),
        P(None, "ep", "grp"),
    )
    out_specs = (
        P("ep", "grp", None),
        P("ep", "grp", None),
        P("ep", None, "grp"),
        P(None, "grp", "ep"),
        P(None, "grp", "ep"),
        P(None, "ep", "grp"),
        P("ep", None),
    )
    return jax.shard_map(body, mesh=mesh, in_specs=in_specs, out_specs=out_specs, check_vma=False)
```

```python
import jax
import jax.numpy as jnp
from jax import lax
from jax.sharding import PartitionSpec as P


def token_table(expert_ids, targets, capacity):
    hit = expert_ids.T[:, None, :] == targets[None, :, None]
    tok_hit = jnp.any(hit, axis=0)
    rank = jnp.cumsum(tok_hit.astype(jnp.int32), axis=1) - 1
    slots = jnp.arange(capacity, dtype=jnp.int32)
    sel = (rank[:, None, :] == slots[None, :, None]) & tok_hit[:, None, :]
    return hit, sel


def gather_rows(hit, sel, tokens, cotangent, gate_weights):
    count, capacity = sel.shape[0], sel.shape[1]
    token_map = sel.reshape(count * capacity, -1).astype(jnp.bfloat16)
    feat_rows = jnp.dot(token_map, tokens, preferred_element_type=jnp.float32).astype(jnp.bfloat16)
    cotan_rows = jnp.dot(token_map, cotangent, preferred_element_type=jnp.float32).astype(
        jnp.bfloat16
    )
    per_token = jnp.sum(
        jnp.where(hit, gate_weights.T.astype(jnp.float32)[:, None, :], 0.0), axis=0
    )
    scale = jnp.sum(jnp.where(sel, per_token[:, None, :], 0.0), axis=2)
    return feat_rows, cotan_rows, scale.reshape(-1).astype(jnp.bfloat16)


def scatter_routes(hit, sel, values):
    per_token = jnp.sum(jnp.where(sel, values[:, :, None], 0.0), axis=1)
    return jnp.sum(jnp.where(hit, per_token[None, :, :], 0.0), axis=1).T


def swiglu_back(pre_gate, pre_up, grad_hidden):
    sigmoid_gate = jax.nn.sigmoid(pre_gate)
    activated = pre_gate * sigmoid_gate
    hidden = (activated * pre_up).astype(jnp.bfloat16)
    back_gate = (
        grad_hidden * pre_up * sigmoid_gate * (1.0 + pre_gate * (1.0 - sigmoid_gate))
    ).astype(jnp.bfloat16)
    back_up = (grad_hidden * activated).astype(jnp.bfloat16)
    return (hidden, back_gate, back_up)


def grp_sum_f32(x, axis_name):
    size = lax.axis_size(axis_name)
    if size & (size - 1):
        return lax.psum(x, axis_name)
    bit = 1
    while bit < size:
        partner = [(i, i ^ bit) for i in range(size)]
        x = x + lax.ppermute(x, axis_name, partner)
        bit *= 2
    return x


def grp_sum_doubling(parts, axis_name):
    size = lax.axis_size(axis_name)
    mine = [p.astype(jnp.bfloat16) for p in parts]
    if size & (size - 1):
        return [lax.psum(r, axis_name).astype(jnp.float32) for r in mine]
    sums = [r.astype(jnp.float32) for r in mine]
    bit = 1
    while bit < size:
        partner = [(i, i ^ bit) for i in range(size)]
        got = lax.ppermute(mine, axis_name, partner)
        sums = [m.astype(jnp.float32) + g.astype(jnp.float32) for m, g in zip(mine, got)]
        mine = [s.astype(jnp.bfloat16) for s in sums]
        bit *= 2
    return sums


def grp_sum_rounded(parts, axes, axis_name):
    size = lax.axis_size(axis_name)
    rounded = [p.astype(jnp.bfloat16) for p in parts]
    if size == 1:
        return [r.astype(jnp.float32) for r in rounded]
    if size & (size - 1) or any(p.shape[a] % 2 for p, a in zip(parts, axes)):
        return [lax.psum(r, axis_name).astype(jnp.float32) for r in rounded]
    first_core = lax.axis_index(axis_name) % 2 == 0
    halves = [jnp.split(r, 2, axis=a) for r, a in zip(rounded, axes)]
    keep = [jnp.where(first_core, lo, hi) for lo, hi in halves]
    send = [jnp.where(first_core, hi, lo) for lo, hi in halves]
    swap = [(i, i ^ 1) for i in range(size)]
    got = lax.ppermute(send, axis_name, swap)
    sums = [k.astype(jnp.float32) + g.astype(jnp.float32) for k, g in zip(keep, got)]
    bit = 2
    while bit < size:
        partner = [(i, i ^ bit) for i in range(size)]
        mine = [s.astype(jnp.bfloat16) for s in sums]
        got = lax.ppermute(mine, axis_name, partner)
        sums = [m.astype(jnp.float32) + g.astype(jnp.float32) for m, g in zip(mine, got)]
        bit *= 2
    other = lax.ppermute(sums, axis_name, swap)
    full = []
    for s, o, a in zip(sums, other, axes):
        first = jnp.where(first_core, s, o)
        second = jnp.where(first_core, o, s)
        full.append(jnp.concatenate([first, second], axis=a))
    return full


def body(
    tokens,
    cotangent,
    gate_weights,
    expert_ids,
    hot_ids,
    gate_cold,
    up_cold,
    down_cold,
    gate_hot,
    up_hot,
    down_hot,
):
    tok_rows, slice_width = tokens.shape
    top_count = expert_ids.shape[1]
    cold_count = lax.axis_size("ep")
    hot_count = hot_ids.shape[0]
    capacity = tok_rows // 16
    blocks = lax.axis_size("ep")
    targets = jnp.concatenate([jnp.arange(cold_count, dtype=jnp.int32), hot_ids])
    all_hit, all_sel = token_table(expert_ids, targets, capacity)
    feats_all, cotan_all, scale_all = gather_rows(all_hit, all_sel, tokens, cotangent, gate_weights)
    cold_total = cold_count * capacity
    hot_feats, hot_cotan, hot_scale = (
        feats_all[cold_total:],
        cotan_all[cold_total:],
        scale_all[cold_total:],
    )
    cold_feats, cold_cotan, cold_scale = (
        feats_all[:cold_total],
        cotan_all[:cold_total],
        scale_all[:cold_total],
    )
    hot_rows = hot_count * capacity
    scale_lines = -(-hot_rows // slice_width)
    scale_lines = -(-scale_lines // 8) * 8
    scale_block = jnp.pad(hot_scale, (0, scale_lines * slice_width - hot_rows)).reshape(
        scale_lines, slice_width
    )
    hot_outgoing = jnp.concatenate([hot_feats, hot_cotan, scale_block], axis=0)
    gathered = lax.all_gather(hot_outgoing, "ep", axis=0, tiled=False)
    cold_lines = -(-capacity // slice_width)
    cold_lines = -(-cold_lines // 8) * 8
    cold_scale_block = jnp.pad(
        cold_scale.reshape(cold_count, capacity),
        ((0, 0), (0, cold_lines * slice_width - capacity)),
    ).reshape(cold_count, cold_lines, slice_width)
    outgoing = jnp.concatenate(
        [
            cold_feats.reshape(cold_count, capacity, slice_width),
            cold_cotan.reshape(cold_count, capacity, slice_width),
            cold_scale_block,
        ],
        axis=1,
    )
    received = lax.all_to_all(outgoing, "ep", split_axis=0, concat_axis=0, tiled=True)
    recv_feats = received[:, :capacity].reshape(-1, slice_width)
    recv_cotan = received[:, capacity : 2 * capacity].reshape(-1, slice_width)
    recv_scale = received[:, 2 * capacity :].reshape(cold_count, -1)[:, :capacity]
    weighted = (
        recv_scale.reshape(-1, 1).astype(jnp.float32) * recv_cotan.astype(jnp.float32)
    ).astype(jnp.bfloat16)
    w_gate = gate_cold[0]
    w_up = up_cold[0]
    w_down = down_cold[0]
    part_gate = jnp.dot(recv_feats, w_gate, preferred_element_type=jnp.float32)
    part_up = jnp.dot(recv_feats, w_up, preferred_element_type=jnp.float32)
    part_hidden = lax.dot_general(
        weighted, w_down, (((1,), (1,)), ((), ())), preferred_element_type=jnp.float32
    )
    all_rows = gathered[:, : 2 * hot_rows].reshape(blocks, 2, hot_count, capacity, slice_width)
    all_rows = jnp.transpose(all_rows, (1, 2, 0, 3, 4)).reshape(
        2, hot_count, blocks * capacity, slice_width
    )
    all_scale = gathered[:, 2 * hot_rows :].reshape(blocks, -1)[:, :hot_rows]
    all_scale = jnp.transpose(all_scale.reshape(blocks, hot_count, capacity), (1, 0, 2))
    rows_feat, rows_cot = all_rows[0], all_rows[1]
    rows_wt = (
        all_scale.reshape(hot_count, blocks * capacity, 1).astype(jnp.float32)
        * rows_cot.astype(jnp.float32)
    ).astype(jnp.bfloat16)
    part_gate_hot = jnp.einsum(
        "jrd,jdh->jrh", rows_feat, gate_hot, preferred_element_type=jnp.float32
    )
    part_up_hot = jnp.einsum("jrd,jdh->jrh", rows_feat, up_hot, preferred_element_type=jnp.float32)
    part_hidden_hot = jnp.einsum(
        "jrd,jhd->jrh", rows_wt, down_hot, preferred_element_type=jnp.float32
    )
    part_cot_hot = jnp.einsum(
        "jrd,jhd->jrh", rows_cot, down_hot, preferred_element_type=jnp.float32
    )
    pre_gate, pre_up, grad_hidden = grp_sum_rounded(
        [part_gate, part_up, part_hidden], [0, 0, 0], "grp"
    )
    hidden, back_gate, back_up = swiglu_back(pre_gate, pre_up, grad_hidden)
    output_slice = jnp.dot(hidden, w_down, preferred_element_type=jnp.float32)
    cold_route = jnp.sum(output_slice * recv_cotan.astype(jnp.float32), axis=1)
    cold_route = grp_sum_f32(cold_route.reshape(cold_count, 1, capacity), "grp")
    contract_rows = (((0,), (0,)), ((), ()))
    late_feats, back_gate, back_up, late_hidden, late_weighted, part_gate_hot = (
        lax.optimization_barrier((recv_feats, back_gate, back_up, hidden, weighted, part_gate_hot))
    )
    pre_gate_hot, pre_up_hot, grad_hidden_hot, cot_down = grp_sum_doubling(
        [part_gate_hot, part_up_hot, part_hidden_hot, part_cot_hot], "grp"
    )
    grad_gate_cold = lax.dot_general(
        late_feats, back_gate, contract_rows, preferred_element_type=jnp.float32
    )
    grad_up_cold = lax.dot_general(
        late_feats, back_up, contract_rows, preferred_element_type=jnp.float32
    )
    grad_down_cold = lax.dot_general(
        late_hidden, late_weighted, contract_rows, preferred_element_type=jnp.float32
    )
    hidden_hot, back_gate_hot, back_up_hot = swiglu_back(pre_gate_hot, pre_up_hot, grad_hidden_hot)
    hot_route_part = jnp.sum(hidden_hot.astype(jnp.float32) * cot_down, axis=2)
    grad_gate_hot = jnp.einsum(
        "jrd,jrh->jdh", rows_feat, back_gate_hot, preferred_element_type=jnp.float32
    )
    grad_up_hot = jnp.einsum("jrd,jrh->jdh", rows_feat, back_up_hot, preferred_element_type=jnp.float32)
    grad_down_hot = jnp.einsum(
        "jrh,jrd->jhd", hidden_hot, rows_wt, preferred_element_type=jnp.float32
    )
    route_parts = jnp.concatenate(
        [
            cold_route,
            jnp.transpose(hot_route_part.reshape(hot_count, blocks, capacity), (1, 0, 2)),
        ],
        axis=1,
    )
    route_back = lax.all_to_all(route_parts, "ep", split_axis=0, concat_axis=0, tiled=True)
    cold_back = route_back[:, 0, :]
    hot_route = jnp.sum(route_back[:, 1:, :], axis=0)
    gate_weight_grad = scatter_routes(
        all_hit, all_sel, jnp.concatenate([cold_back, hot_route], axis=0)
    )
    return (
        grad_gate_cold[None].astype(jnp.bfloat16),
        grad_up_cold[None].astype(jnp.bfloat16),
        grad_down_cold[None].astype(jnp.bfloat16),
        grad_gate_hot,
        grad_up_hot,
        grad_down_hot,
        gate_weight_grad,
    )


def solution(mesh):
    in_specs = (
        P("ep", "grp"),
        P("ep", "grp"),
        P("ep", None),
        P("ep", None),
        P(),
        P("ep", "grp", None),
        P("ep", "grp", None),
        P("ep", None, "grp"),
        P(None, "grp", "ep"),
        P(None, "grp", "ep"),
        P(None, "ep", "grp"),
    )
    out_specs = (
        P("ep", "grp", None),
        P("ep", "grp", None),
        P("ep", None, "grp"),
        P(None, "grp", "ep"),
        P(None, "grp", "ep"),
        P(None, "ep", "grp"),
        P("ep", None),
    )
    return jax.shard_map(body, mesh=mesh, in_specs=in_specs, out_specs=out_specs, check_vma=False)
```

```python
import jax
import jax.numpy as jnp
from jax import lax
from jax.sharding import PartitionSpec as P


def token_table(expert_ids, targets, capacity):
    hit = expert_ids.T[:, None, :] == targets[None, :, None]
    tok_hit = jnp.any(hit, axis=0)
    rank = jnp.cumsum(tok_hit.astype(jnp.int32), axis=1) - 1
    slots = jnp.arange(capacity, dtype=jnp.int32)
    sel = (rank[:, None, :] == slots[None, :, None]) & tok_hit[:, None, :]
    return hit, sel


def gather_rows(hit, sel, tokens, cotangent, gate_weights):
    count, capacity = sel.shape[0], sel.shape[1]
    token_map = sel.reshape(count * capacity, -1).astype(jnp.bfloat16)
    feat_rows = jnp.dot(token_map, tokens, preferred_element_type=jnp.float32).astype(jnp.bfloat16)
    cotan_rows = jnp.dot(token_map, cotangent, preferred_element_type=jnp.float32).astype(
        jnp.bfloat16
    )
    per_token = jnp.sum(
        jnp.where(hit, gate_weights.T.astype(jnp.float32)[:, None, :], 0.0), axis=0
    )
    scale = jnp.sum(jnp.where(sel, per_token[:, None, :], 0.0), axis=2)
    return feat_rows, cotan_rows, scale.reshape(-1).astype(jnp.bfloat16)


def scatter_routes(hit, sel, values):
    per_token = jnp.sum(jnp.where(sel, values[:, :, None], 0.0), axis=1)
    return jnp.sum(jnp.where(hit, per_token[None, :, :], 0.0), axis=1).T


def swiglu_back(pre_gate, pre_up, grad_hidden):
    sigmoid_gate = jax.nn.sigmoid(pre_gate)
    activated = pre_gate * sigmoid_gate
    hidden = (activated * pre_up).astype(jnp.bfloat16)
    back_gate = (
        grad_hidden * pre_up * sigmoid_gate * (1.0 + pre_gate * (1.0 - sigmoid_gate))
    ).astype(jnp.bfloat16)
    back_up = (grad_hidden * activated).astype(jnp.bfloat16)
    return (hidden, back_gate, back_up)


def grp_sum_f32(x, axis_name):
    size = lax.axis_size(axis_name)
    if size & (size - 1):
        return lax.psum(x, axis_name)
    bit = 1
    while bit < size:
        partner = [(i, i ^ bit) for i in range(size)]
        x = x + lax.ppermute(x, axis_name, partner)
        bit *= 2
    return x


def grp_sum_doubling(parts, axis_name):
    size = lax.axis_size(axis_name)
    mine = [p.astype(jnp.bfloat16) for p in parts]
    if size & (size - 1):
        return [lax.psum(r, axis_name).astype(jnp.float32) for r in mine]
    sums = [r.astype(jnp.float32) for r in mine]
    bit = 1
    while bit < size:
        partner = [(i, i ^ bit) for i in range(size)]
        got = lax.ppermute(mine, axis_name, partner)
        sums = [m.astype(jnp.float32) + g.astype(jnp.float32) for m, g in zip(mine, got)]
        mine = [s.astype(jnp.bfloat16) for s in sums]
        bit *= 2
    return sums


def grp_sum_rounded(parts, axes, axis_name):
    size = lax.axis_size(axis_name)
    rounded = [p.astype(jnp.bfloat16) for p in parts]
    if size == 1:
        return [r.astype(jnp.float32) for r in rounded]
    if size & (size - 1) or any(p.shape[a] % 2 for p, a in zip(parts, axes)):
        return [lax.psum(r, axis_name).astype(jnp.float32) for r in rounded]
    first_core = lax.axis_index(axis_name) % 2 == 0
    halves = [jnp.split(r, 2, axis=a) for r, a in zip(rounded, axes)]
    keep = [jnp.where(first_core, lo, hi) for lo, hi in halves]
    send = [jnp.where(first_core, hi, lo) for lo, hi in halves]
    swap = [(i, i ^ 1) for i in range(size)]
    got = lax.ppermute(send, axis_name, swap)
    sums = [k.astype(jnp.float32) + g.astype(jnp.float32) for k, g in zip(keep, got)]
    bit = 2
    while bit < size:
        partner = [(i, i ^ bit) for i in range(size)]
        mine = [s.astype(jnp.bfloat16) for s in sums]
        got = lax.ppermute(mine, axis_name, partner)
        sums = [m.astype(jnp.float32) + g.astype(jnp.float32) for m, g in zip(mine, got)]
        bit *= 2
    other = lax.ppermute(sums, axis_name, swap)
    full = []
    for s, o, a in zip(sums, other, axes):
        first = jnp.where(first_core, s, o)
        second = jnp.where(first_core, o, s)
        full.append(jnp.concatenate([first, second], axis=a))
    return full


def body(
    tokens,
    cotangent,
    gate_weights,
    expert_ids,
    hot_ids,
    gate_cold,
    up_cold,
    down_cold,
    gate_hot,
    up_hot,
    down_hot,
):
    tok_rows, slice_width = tokens.shape
    top_count = expert_ids.shape[1]
    cold_count = lax.axis_size("ep")
    hot_count = hot_ids.shape[0]
    capacity = tok_rows // 16
    blocks = lax.axis_size("ep")
    targets = jnp.concatenate([jnp.arange(cold_count, dtype=jnp.int32), hot_ids])
    all_hit, all_sel = token_table(expert_ids, targets, capacity)
    feats_all, cotan_all, scale_all = gather_rows(all_hit, all_sel, tokens, cotangent, gate_weights)
    cold_total = cold_count * capacity
    hot_feats, hot_cotan, hot_scale = (
        feats_all[cold_total:],
        cotan_all[cold_total:],
        scale_all[cold_total:],
    )
    cold_feats, cold_cotan, cold_scale = (
        feats_all[:cold_total],
        cotan_all[:cold_total],
        scale_all[:cold_total],
    )
    hot_rows = hot_count * capacity
    scale_lines = -(-hot_rows // slice_width)
    scale_lines = -(-scale_lines // 8) * 8
    scale_block = jnp.pad(hot_scale, (0, scale_lines * slice_width - hot_rows)).reshape(
        scale_lines, slice_width
    )
    hot_outgoing = jnp.concatenate([hot_feats, hot_cotan, scale_block], axis=0)
    gathered = lax.all_gather(hot_outgoing, "ep", axis=1, tiled=False)
    cold_lines = -(-capacity // slice_width)
    cold_lines = -(-cold_lines // 8) * 8
    cold_scale_block = jnp.pad(
        cold_scale.reshape(cold_count, capacity),
        ((0, 0), (0, cold_lines * slice_width - capacity)),
    ).reshape(cold_count, cold_lines, slice_width)
    outgoing = jnp.concatenate(
        [
            cold_feats.reshape(cold_count, capacity, slice_width),
            cold_cotan.reshape(cold_count, capacity, slice_width),
            cold_scale_block,
        ],
        axis=1,
    )
    received = lax.all_to_all(outgoing, "ep", split_axis=0, concat_axis=0, tiled=True)
    recv_feats = received[:, :capacity].reshape(-1, slice_width)
    recv_cotan = received[:, capacity : 2 * capacity].reshape(-1, slice_width)
    recv_scale = received[:, 2 * capacity :].reshape(cold_count, -1)[:, :capacity]
    weighted = (
        recv_scale.reshape(-1, 1).astype(jnp.float32) * recv_cotan.astype(jnp.float32)
    ).astype(jnp.bfloat16)
    w_gate = gate_cold[0]
    w_up = up_cold[0]
    w_down = down_cold[0]
    part_gate = jnp.dot(recv_feats, w_gate, preferred_element_type=jnp.float32)
    part_up = jnp.dot(recv_feats, w_up, preferred_element_type=jnp.float32)
    part_hidden = lax.dot_general(
        weighted, w_down, (((1,), (1,)), ((), ())), preferred_element_type=jnp.float32
    )
    rows_feat = gathered[:hot_rows].reshape(hot_count, capacity * blocks, slice_width)
    rows_cot = gathered[hot_rows : 2 * hot_rows].reshape(hot_count, capacity * blocks, slice_width)
    all_scale = jnp.transpose(gathered[2 * hot_rows :], (1, 0, 2)).reshape(blocks, -1)[:, :hot_rows]
    all_scale = jnp.transpose(all_scale.reshape(blocks, hot_count, capacity), (1, 2, 0))
    rows_wt = (
        all_scale.reshape(hot_count, blocks * capacity, 1).astype(jnp.float32)
        * rows_cot.astype(jnp.float32)
    ).astype(jnp.bfloat16)
    part_gate_hot = jnp.einsum(
        "jrd,jdh->jrh", rows_feat, gate_hot, preferred_element_type=jnp.float32
    )
    part_up_hot = jnp.einsum("jrd,jdh->jrh", rows_feat, up_hot, preferred_element_type=jnp.float32)
    part_hidden_hot = jnp.einsum(
        "jrd,jhd->jrh", rows_wt, down_hot, preferred_element_type=jnp.float32
    )
    part_cot_hot = jnp.einsum(
        "jrd,jhd->jrh", rows_cot, down_hot, preferred_element_type=jnp.float32
    )
    pre_gate, pre_up, grad_hidden = grp_sum_rounded(
        [part_gate, part_up, part_hidden], [0, 0, 0], "grp"
    )
    pre_gate_hot, pre_up_hot, grad_hidden_hot, cot_down = grp_sum_doubling(
        [part_gate_hot, part_up_hot, part_hidden_hot, part_cot_hot], "grp"
    )
    hidden, back_gate, back_up = swiglu_back(pre_gate, pre_up, grad_hidden)
    output_slice = jnp.dot(hidden, w_down, preferred_element_type=jnp.float32)
    cold_route = jnp.sum(output_slice * recv_cotan.astype(jnp.float32), axis=1)
    cold_route = grp_sum_f32(cold_route.reshape(cold_count, 1, capacity), "grp")
    contract_rows = (((0,), (0,)), ((), ()))
    grad_gate_cold = lax.dot_general(
        recv_feats, back_gate, contract_rows, preferred_element_type=jnp.float32
    )
    grad_up_cold = lax.dot_general(
        recv_feats, back_up, contract_rows, preferred_element_type=jnp.float32
    )
    grad_down_cold = lax.dot_general(
        hidden, weighted, contract_rows, preferred_element_type=jnp.float32
    )
    hidden_hot, back_gate_hot, back_up_hot = swiglu_back(pre_gate_hot, pre_up_hot, grad_hidden_hot)
    hot_route_part = jnp.sum(hidden_hot.astype(jnp.float32) * cot_down, axis=2)
    grad_gate_hot = jnp.einsum(
        "jrd,jrh->jdh", rows_feat, back_gate_hot, preferred_element_type=jnp.float32
    )
    grad_up_hot = jnp.einsum("jrd,jrh->jdh", rows_feat, back_up_hot, preferred_element_type=jnp.float32)
    grad_down_hot = jnp.einsum(
        "jrh,jrd->jhd", hidden_hot, rows_wt, preferred_element_type=jnp.float32
    )
    route_parts = jnp.concatenate(
        [
            cold_route,
            jnp.transpose(hot_route_part.reshape(hot_count, capacity, blocks), (2, 0, 1)),
        ],
        axis=1,
    )
    route_back = lax.all_to_all(route_parts, "ep", split_axis=0, concat_axis=0, tiled=True)
    cold_back = route_back[:, 0, :]
    hot_route = jnp.sum(route_back[:, 1:, :], axis=0)
    gate_weight_grad = scatter_routes(
        all_hit, all_sel, jnp.concatenate([cold_back, hot_route], axis=0)
    )
    return (
        grad_gate_cold[None].astype(jnp.bfloat16),
        grad_up_cold[None].astype(jnp.bfloat16),
        grad_down_cold[None].astype(jnp.bfloat16),
        grad_gate_hot,
        grad_up_hot,
        grad_down_hot,
        gate_weight_grad,
    )


def solution(mesh):
    in_specs = (
        P("ep", "grp"),
        P("ep", "grp"),
        P("ep", None),
        P("ep", None),
        P(),
        P("ep", "grp", None),
        P("ep", "grp", None),
        P("ep", None, "grp"),
        P(None, "grp", "ep"),
        P(None, "grp", "ep"),
        P(None, "ep", "grp"),
    )
    out_specs = (
        P("ep", "grp", None),
        P("ep", "grp", None),
        P("ep", None, "grp"),
        P(None, "grp", "ep"),
        P(None, "grp", "ep"),
        P(None, "ep", "grp"),
        P("ep", None),
    )
    return jax.shard_map(body, mesh=mesh, in_specs=in_specs, out_specs=out_specs, check_vma=False)
```

```python
import jax
import jax.numpy as jnp
from jax import lax
from jax.sharding import PartitionSpec as P


def token_table(expert_ids, targets, capacity):
    hit = expert_ids.T[:, None, :] == targets[None, :, None]
    tok_hit = jnp.any(hit, axis=0)
    rank = jnp.cumsum(tok_hit.astype(jnp.int32), axis=1) - 1
    slots = jnp.arange(capacity, dtype=jnp.int32)
    sel = (rank[:, None, :] == slots[None, :, None]) & tok_hit[:, None, :]
    return hit, sel


def gather_rows(hit, sel, tokens, cotangent, gate_weights):
    count, capacity = sel.shape[0], sel.shape[1]
    token_map = sel.reshape(count * capacity, -1).astype(jnp.bfloat16)
    feat_rows = jnp.dot(token_map, tokens, preferred_element_type=jnp.float32).astype(jnp.bfloat16)
    cotan_rows = jnp.dot(token_map, cotangent, preferred_element_type=jnp.float32).astype(
        jnp.bfloat16
    )
    per_token = jnp.sum(
        jnp.where(hit, gate_weights.T.astype(jnp.float32)[:, None, :], 0.0), axis=0
    )
    scale = jnp.sum(jnp.where(sel, per_token[:, None, :], 0.0), axis=2)
    return feat_rows, cotan_rows, scale.reshape(-1).astype(jnp.bfloat16)


def scatter_routes(hit, sel, values):
    per_token = jnp.sum(jnp.where(sel, values[:, :, None], 0.0), axis=1)
    return jnp.sum(jnp.where(hit, per_token[None, :, :], 0.0), axis=1).T


def swiglu_back(pre_gate, pre_up, grad_hidden):
    sigmoid_gate = jax.nn.sigmoid(pre_gate)
    activated = pre_gate * sigmoid_gate
    hidden = (activated * pre_up).astype(jnp.bfloat16)
    back_gate = (
        grad_hidden * pre_up * sigmoid_gate * (1.0 + pre_gate * (1.0 - sigmoid_gate))
    ).astype(jnp.bfloat16)
    back_up = (grad_hidden * activated).astype(jnp.bfloat16)
    return (hidden, back_gate, back_up)


def grp_sum_f32(x, axis_name):
    size = lax.axis_size(axis_name)
    if size & (size - 1):
        return lax.psum(x, axis_name)
    bit = 1
    while bit < size:
        partner = [(i, i ^ bit) for i in range(size)]
        x = x + lax.ppermute(x, axis_name, partner)
        bit *= 2
    return x


def grp_sum_doubling(parts, axis_name):
    size = lax.axis_size(axis_name)
    mine = [p.astype(jnp.bfloat16) for p in parts]
    if size & (size - 1):
        return [lax.psum(r, axis_name).astype(jnp.float32) for r in mine]
    sums = [r.astype(jnp.float32) for r in mine]
    bit = 1
    while bit < size:
        partner = [(i, i ^ bit) for i in range(size)]
        got = lax.ppermute(mine, axis_name, partner)
        sums = [m.astype(jnp.float32) + g.astype(jnp.float32) for m, g in zip(mine, got)]
        mine = [s.astype(jnp.bfloat16) for s in sums]
        bit *= 2
    return sums


def grp_sum_rounded(parts, axes, axis_name):
    size = lax.axis_size(axis_name)
    rounded = [p.astype(jnp.bfloat16) for p in parts]
    if size == 1:
        return [r.astype(jnp.float32) for r in rounded]
    if size & (size - 1) or any(p.shape[a] % 2 for p, a in zip(parts, axes)):
        return [lax.psum(r, axis_name).astype(jnp.float32) for r in rounded]
    first_core = lax.axis_index(axis_name) % 2 == 0
    halves = [jnp.split(r, 2, axis=a) for r, a in zip(rounded, axes)]
    keep = [jnp.where(first_core, lo, hi) for lo, hi in halves]
    send = [jnp.where(first_core, hi, lo) for lo, hi in halves]
    swap = [(i, i ^ 1) for i in range(size)]
    got = lax.ppermute(send, axis_name, swap)
    sums = [k.astype(jnp.float32) + g.astype(jnp.float32) for k, g in zip(keep, got)]
    bit = 2
    while bit < size:
        partner = [(i, i ^ bit) for i in range(size)]
        mine = [s.astype(jnp.bfloat16) for s in sums]
        got = lax.ppermute(mine, axis_name, partner)
        sums = [m.astype(jnp.float32) + g.astype(jnp.float32) for m, g in zip(mine, got)]
        bit *= 2
    other = lax.ppermute(sums, axis_name, swap)
    full = []
    for s, o, a in zip(sums, other, axes):
        first = jnp.where(first_core, s, o)
        second = jnp.where(first_core, o, s)
        full.append(jnp.concatenate([first, second], axis=a))
    return full


def body(
    tokens,
    cotangent,
    gate_weights,
    expert_ids,
    hot_ids,
    gate_cold,
    up_cold,
    down_cold,
    gate_hot,
    up_hot,
    down_hot,
):
    tok_rows, slice_width = tokens.shape
    top_count = expert_ids.shape[1]
    cold_count = lax.axis_size("ep")
    hot_count = hot_ids.shape[0]
    capacity = tok_rows // 16
    blocks = lax.axis_size("ep")
    targets = jnp.concatenate([jnp.arange(cold_count, dtype=jnp.int32), hot_ids])
    all_hit, all_sel = token_table(expert_ids, targets, capacity)
    feats_all, cotan_all, scale_all = gather_rows(all_hit, all_sel, tokens, cotangent, gate_weights)
    cold_total = cold_count * capacity
    hot_feats, hot_cotan, hot_scale = (
        feats_all[cold_total:],
        cotan_all[cold_total:],
        scale_all[cold_total:],
    )
    cold_feats, cold_cotan, cold_scale = (
        feats_all[:cold_total],
        cotan_all[:cold_total],
        scale_all[:cold_total],
    )
    hot_rows = hot_count * capacity
    scale_lines = -(-hot_rows // slice_width)
    scale_lines = -(-scale_lines // 8) * 8
    scale_block = jnp.pad(hot_scale, (0, scale_lines * slice_width - hot_rows)).reshape(
        scale_lines, slice_width
    )
    hot_outgoing = jnp.concatenate([hot_feats, hot_cotan, scale_block], axis=0)
    gathered = lax.all_gather(hot_outgoing, "ep", axis=0, tiled=False)
    cold_lines = -(-capacity // slice_width)
    cold_lines = -(-cold_lines // 8) * 8
    cold_scale_block = jnp.pad(
        cold_scale.reshape(cold_count, capacity),
        ((0, 0), (0, cold_lines * slice_width - capacity)),
    ).reshape(cold_count, cold_lines, slice_width)
    outgoing = jnp.concatenate(
        [
            cold_feats.reshape(cold_count, capacity, slice_width),
            cold_cotan.reshape(cold_count, capacity, slice_width),
            cold_scale_block,
        ],
        axis=1,
    )
    received = lax.all_to_all(outgoing, "ep", split_axis=0, concat_axis=0, tiled=True)
    recv_feats = received[:, :capacity].reshape(-1, slice_width)
    recv_cotan = received[:, capacity : 2 * capacity].reshape(-1, slice_width)
    recv_scale = received[:, 2 * capacity :].reshape(cold_count, -1)[:, :capacity]
    weighted = (
        recv_scale.reshape(-1, 1).astype(jnp.float32) * recv_cotan.astype(jnp.float32)
    ).astype(jnp.bfloat16)
    w_gate = gate_cold[0]
    w_up = up_cold[0]
    w_down = down_cold[0]
    part_gate = jnp.dot(recv_feats, w_gate, preferred_element_type=jnp.float32)
    part_up = jnp.dot(recv_feats, w_up, preferred_element_type=jnp.float32)
    part_hidden = lax.dot_general(
        weighted, w_down, (((1,), (1,)), ((), ())), preferred_element_type=jnp.float32
    )
    all_rows = gathered[:, : 2 * hot_rows].reshape(blocks, 2, hot_count, capacity, slice_width)
    all_rows = jnp.transpose(all_rows, (1, 2, 0, 3, 4)).reshape(
        2, hot_count, blocks * capacity, slice_width
    )
    all_scale = gathered[:, 2 * hot_rows :].reshape(blocks, -1)[:, :hot_rows]
    all_scale = jnp.transpose(all_scale.reshape(blocks, hot_count, capacity), (1, 0, 2))
    rows_feat, rows_cot = all_rows[0], all_rows[1]
    rows_wt = (
        all_scale.reshape(hot_count, blocks * capacity, 1).astype(jnp.float32)
        * rows_cot.astype(jnp.float32)
    ).astype(jnp.bfloat16)
    part_gate_hot = jnp.einsum(
        "jrd,jdh->jrh", rows_feat, gate_hot, preferred_element_type=jnp.float32
    )
    part_up_hot = jnp.einsum("jrd,jdh->jrh", rows_feat, up_hot, preferred_element_type=jnp.float32)
    part_hidden_hot = jnp.einsum(
        "jrd,jhd->jrh", rows_wt, down_hot, preferred_element_type=jnp.float32
    )
    part_cot_hot = jnp.einsum(
        "jrd,jhd->jrh", rows_cot, down_hot, preferred_element_type=jnp.float32
    )
    pre_gate, pre_up, grad_hidden = grp_sum_doubling([part_gate, part_up, part_hidden], "grp")
    pre_gate_hot, pre_up_hot, grad_hidden_hot, cot_down = grp_sum_doubling(
        [part_gate_hot, part_up_hot, part_hidden_hot, part_cot_hot], "grp"
    )
    hidden, back_gate, back_up = swiglu_back(pre_gate, pre_up, grad_hidden)
    output_slice = jnp.dot(hidden, w_down, preferred_element_type=jnp.float32)
    cold_route = jnp.sum(output_slice * recv_cotan.astype(jnp.float32), axis=1)
    cold_route = grp_sum_f32(cold_route.reshape(cold_count, 1, capacity), "grp")
    contract_rows = (((0,), (0,)), ((), ()))
    grad_gate_cold = lax.dot_general(
        recv_feats, back_gate, contract_rows, preferred_element_type=jnp.float32
    )
    grad_up_cold = lax.dot_general(
        recv_feats, back_up, contract_rows, preferred_element_type=jnp.float32
    )
    grad_down_cold = lax.dot_general(
        hidden, weighted, contract_rows, preferred_element_type=jnp.float32
    )
    hidden_hot, back_gate_hot, back_up_hot = swiglu_back(pre_gate_hot, pre_up_hot, grad_hidden_hot)
    hot_route_part = jnp.sum(hidden_hot.astype(jnp.float32) * cot_down, axis=2)
    grad_gate_hot = jnp.einsum(
        "jrd,jrh->jdh", rows_feat, back_gate_hot, preferred_element_type=jnp.float32
    )
    grad_up_hot = jnp.einsum("jrd,jrh->jdh", rows_feat, back_up_hot, preferred_element_type=jnp.float32)
    grad_down_hot = jnp.einsum(
        "jrh,jrd->jhd", hidden_hot, rows_wt, preferred_element_type=jnp.float32
    )
    route_parts = jnp.concatenate(
        [
            cold_route,
            jnp.transpose(hot_route_part.reshape(hot_count, blocks, capacity), (1, 0, 2)),
        ],
        axis=1,
    )
    route_back = lax.all_to_all(route_parts, "ep", split_axis=0, concat_axis=0, tiled=True)
    cold_back = route_back[:, 0, :]
    hot_route = jnp.sum(route_back[:, 1:, :], axis=0)
    gate_weight_grad = scatter_routes(
        all_hit, all_sel, jnp.concatenate([cold_back, hot_route], axis=0)
    )
    return (
        grad_gate_cold[None].astype(jnp.bfloat16),
        grad_up_cold[None].astype(jnp.bfloat16),
        grad_down_cold[None].astype(jnp.bfloat16),
        grad_gate_hot,
        grad_up_hot,
        grad_down_hot,
        gate_weight_grad,
    )


def solution(mesh):
    in_specs = (
        P("ep", "grp"),
        P("ep", "grp"),
        P("ep", None),
        P("ep", None),
        P(),
        P("ep", "grp", None),
        P("ep", "grp", None),
        P("ep", None, "grp"),
        P(None, "grp", "ep"),
        P(None, "grp", "ep"),
        P(None, "ep", "grp"),
    )
    out_specs = (
        P("ep", "grp", None),
        P("ep", "grp", None),
        P("ep", None, "grp"),
        P(None, "grp", "ep"),
        P(None, "grp", "ep"),
        P(None, "ep", "grp"),
        P("ep", None),
    )
    return jax.shard_map(body, mesh=mesh, in_specs=in_specs, out_specs=out_specs, check_vma=False)
```

```python
import jax
import jax.numpy as jnp
from jax import lax
from jax.sharding import PartitionSpec as P


def token_table(expert_ids, targets, capacity):
    hit = expert_ids.T[:, None, :] == targets[None, :, None]
    tok_hit = jnp.any(hit, axis=0)
    rank = jnp.cumsum(tok_hit.astype(jnp.int32), axis=1) - 1
    slots = jnp.arange(capacity, dtype=jnp.int32)
    sel = (rank[:, None, :] == slots[None, :, None]) & tok_hit[:, None, :]
    return hit, sel


def gather_rows(hit, sel, tokens, cotangent, gate_weights):
    count, capacity = sel.shape[0], sel.shape[1]
    token_map = sel.reshape(count * capacity, -1).astype(jnp.bfloat16)
    feat_rows = jnp.dot(token_map, tokens, preferred_element_type=jnp.float32).astype(jnp.bfloat16)
    cotan_rows = jnp.dot(token_map, cotangent, preferred_element_type=jnp.float32).astype(
        jnp.bfloat16
    )
    per_token = jnp.sum(
        jnp.where(hit, gate_weights.T.astype(jnp.float32)[:, None, :], 0.0), axis=0
    )
    scale = jnp.sum(jnp.where(sel, per_token[:, None, :], 0.0), axis=2)
    return feat_rows, cotan_rows, scale.reshape(-1).astype(jnp.bfloat16)


def scatter_routes(hit, sel, values):
    per_token = jnp.sum(jnp.where(sel, values[:, :, None], 0.0), axis=1)
    return jnp.sum(jnp.where(hit, per_token[None, :, :], 0.0), axis=1).T


def swiglu_back(pre_gate, pre_up, grad_hidden):
    sigmoid_gate = jax.nn.sigmoid(pre_gate)
    activated = pre_gate * sigmoid_gate
    hidden = (activated * pre_up).astype(jnp.bfloat16)
    back_gate = (
        grad_hidden * pre_up * sigmoid_gate * (1.0 + pre_gate * (1.0 - sigmoid_gate))
    ).astype(jnp.bfloat16)
    back_up = (grad_hidden * activated).astype(jnp.bfloat16)
    return (hidden, back_gate, back_up)


def grp_sum_f32(x, axis_name):
    size = lax.axis_size(axis_name)
    if size & (size - 1):
        return lax.psum(x, axis_name)
    bit = 1
    while bit < size:
        partner = [(i, i ^ bit) for i in range(size)]
        x = x + lax.ppermute(x, axis_name, partner)
        bit *= 2
    return x


def grp_sum_doubling(parts, axis_name):
    size = lax.axis_size(axis_name)
    mine = [p.astype(jnp.bfloat16) for p in parts]
    if size & (size - 1):
        return [lax.psum(r, axis_name).astype(jnp.float32) for r in mine]
    sums = [r.astype(jnp.float32) for r in mine]
    bit = 1
    while bit < size:
        partner = [(i, i ^ bit) for i in range(size)]
        got = lax.ppermute(mine, axis_name, partner)
        sums = [m.astype(jnp.float32) + g.astype(jnp.float32) for m, g in zip(mine, got)]
        mine = [s.astype(jnp.bfloat16) for s in sums]
        bit *= 2
    return sums


def grp_sum_rounded(parts, axes, axis_name):
    size = lax.axis_size(axis_name)
    rounded = [p.astype(jnp.bfloat16) for p in parts]
    if size == 1:
        return [r.astype(jnp.float32) for r in rounded]
    if size & (size - 1) or any(p.shape[a] % 2 for p, a in zip(parts, axes)):
        return [lax.psum(r, axis_name).astype(jnp.float32) for r in rounded]
    first_core = lax.axis_index(axis_name) % 2 == 0
    halves = [jnp.split(r, 2, axis=a) for r, a in zip(rounded, axes)]
    keep = [jnp.where(first_core, lo, hi) for lo, hi in halves]
    send = [jnp.where(first_core, hi, lo) for lo, hi in halves]
    swap = [(i, i ^ 1) for i in range(size)]
    got = lax.ppermute(send, axis_name, swap)
    sums = [k.astype(jnp.float32) + g.astype(jnp.float32) for k, g in zip(keep, got)]
    bit = 2
    while bit < size:
        partner = [(i, i ^ bit) for i in range(size)]
        mine = [s.astype(jnp.bfloat16) for s in sums]
        got = lax.ppermute(mine, axis_name, partner)
        sums = [m.astype(jnp.float32) + g.astype(jnp.float32) for m, g in zip(mine, got)]
        bit *= 2
    other = lax.ppermute(sums, axis_name, swap)
    full = []
    for s, o, a in zip(sums, other, axes):
        first = jnp.where(first_core, s, o)
        second = jnp.where(first_core, o, s)
        full.append(jnp.concatenate([first, second], axis=a))
    return full


def body(
    tokens,
    cotangent,
    gate_weights,
    expert_ids,
    hot_ids,
    gate_cold,
    up_cold,
    down_cold,
    gate_hot,
    up_hot,
    down_hot,
):
    tok_rows, slice_width = tokens.shape
    top_count = expert_ids.shape[1]
    cold_count = lax.axis_size("ep")
    hot_count = hot_ids.shape[0]
    capacity = tok_rows // 16
    blocks = lax.axis_size("ep")
    targets = jnp.concatenate([jnp.arange(cold_count, dtype=jnp.int32), hot_ids])
    all_hit, all_sel = token_table(expert_ids, targets, capacity)
    feats_all, cotan_all, scale_all = gather_rows(all_hit, all_sel, tokens, cotangent, gate_weights)
    cold_total = cold_count * capacity
    hot_feats, hot_cotan, hot_scale = (
        feats_all[cold_total:],
        cotan_all[cold_total:],
        scale_all[cold_total:],
    )
    cold_feats, cold_cotan, cold_scale = (
        feats_all[:cold_total],
        cotan_all[:cold_total],
        scale_all[:cold_total],
    )
    hot_rows = hot_count * capacity
    hot_outgoing = jnp.concatenate([hot_feats, hot_cotan], axis=0)
    gathered = lax.all_gather(hot_outgoing, "ep", axis=0, tiled=False)
    scale_width = capacity + hot_rows
    cold_lines = -(-scale_width // slice_width)
    cold_lines = -(-cold_lines // 8) * 8
    both_scales = jnp.concatenate(
        [
            cold_scale.reshape(cold_count, capacity),
            jnp.broadcast_to(hot_scale[None, :], (cold_count, hot_rows)),
        ],
        axis=1,
    )
    cold_scale_block = jnp.pad(
        both_scales, ((0, 0), (0, cold_lines * slice_width - scale_width))
    ).reshape(cold_count, cold_lines, slice_width)
    outgoing = jnp.concatenate(
        [
            cold_feats.reshape(cold_count, capacity, slice_width),
            cold_cotan.reshape(cold_count, capacity, slice_width),
            cold_scale_block,
        ],
        axis=1,
    )
    received = lax.all_to_all(outgoing, "ep", split_axis=0, concat_axis=0, tiled=True)
    recv_feats = received[:, :capacity].reshape(-1, slice_width)
    recv_cotan = received[:, capacity : 2 * capacity].reshape(-1, slice_width)
    recv_scales = received[:, 2 * capacity :].reshape(cold_count, -1)
    recv_scale = recv_scales[:, :capacity]
    weighted = (
        recv_scale.reshape(-1, 1).astype(jnp.float32) * recv_cotan.astype(jnp.float32)
    ).astype(jnp.bfloat16)
    w_gate = gate_cold[0]
    w_up = up_cold[0]
    w_down = down_cold[0]
    part_gate = jnp.dot(recv_feats, w_gate, preferred_element_type=jnp.float32)
    part_up = jnp.dot(recv_feats, w_up, preferred_element_type=jnp.float32)
    part_hidden = lax.dot_general(
        weighted, w_down, (((1,), (1,)), ((), ())), preferred_element_type=jnp.float32
    )
    all_rows = gathered[:, : 2 * hot_rows].reshape(blocks, 2, hot_count, capacity, slice_width)
    all_rows = jnp.transpose(all_rows, (1, 2, 0, 3, 4)).reshape(
        2, hot_count, blocks * capacity, slice_width
    )
    all_scale = recv_scales[:, capacity:scale_width]
    all_scale = jnp.transpose(all_scale.reshape(blocks, hot_count, capacity), (1, 0, 2))
    rows_feat, rows_cot = all_rows[0], all_rows[1]
    rows_wt = (
        all_scale.reshape(hot_count, blocks * capacity, 1).astype(jnp.float32)
        * rows_cot.astype(jnp.float32)
    ).astype(jnp.bfloat16)
    part_gate_hot = jnp.einsum(
        "jrd,jdh->jrh", rows_feat, gate_hot, preferred_element_type=jnp.float32
    )
    part_up_hot = jnp.einsum("jrd,jdh->jrh", rows_feat, up_hot, preferred_element_type=jnp.float32)
    part_hidden_hot = jnp.einsum(
        "jrd,jhd->jrh", rows_wt, down_hot, preferred_element_type=jnp.float32
    )
    part_cot_hot = jnp.einsum(
        "jrd,jhd->jrh", rows_cot, down_hot, preferred_element_type=jnp.float32
    )
    pre_gate, pre_up, grad_hidden = grp_sum_rounded(
        [part_gate, part_up, part_hidden], [0, 0, 0], "grp"
    )
    pre_gate_hot, pre_up_hot, grad_hidden_hot, cot_down = grp_sum_doubling(
        [part_gate_hot, part_up_hot, part_hidden_hot, part_cot_hot], "grp"
    )
    hidden, back_gate, back_up = swiglu_back(pre_gate, pre_up, grad_hidden)
    output_slice = jnp.dot(hidden, w_down, preferred_element_type=jnp.float32)
    cold_route = jnp.sum(output_slice * recv_cotan.astype(jnp.float32), axis=1)
    cold_route = grp_sum_f32(cold_route.reshape(cold_count, 1, capacity), "grp")
    contract_rows = (((0,), (0,)), ((), ()))
    grad_gate_cold = lax.dot_general(
        recv_feats, back_gate, contract_rows, preferred_element_type=jnp.float32
    )
    grad_up_cold = lax.dot_general(
        recv_feats, back_up, contract_rows, preferred_element_type=jnp.float32
    )
    grad_down_cold = lax.dot_general(
        hidden, weighted, contract_rows, preferred_element_type=jnp.float32
    )
    hidden_hot, back_gate_hot, back_up_hot = swiglu_back(pre_gate_hot, pre_up_hot, grad_hidden_hot)
    hot_route_part = jnp.sum(hidden_hot.astype(jnp.float32) * cot_down, axis=2)
    grad_gate_hot = jnp.einsum(
        "jrd,jrh->jdh", rows_feat, back_gate_hot, preferred_element_type=jnp.float32
    )
    grad_up_hot = jnp.einsum("jrd,jrh->jdh", rows_feat, back_up_hot, preferred_element_type=jnp.float32)
    grad_down_hot = jnp.einsum(
        "jrh,jrd->jhd", hidden_hot, rows_wt, preferred_element_type=jnp.float32
    )
    route_parts = jnp.concatenate(
        [
            cold_route,
            jnp.transpose(hot_route_part.reshape(hot_count, blocks, capacity), (1, 0, 2)),
        ],
        axis=1,
    )
    route_back = lax.all_to_all(route_parts, "ep", split_axis=0, concat_axis=0, tiled=True)
    cold_back = route_back[:, 0, :]
    hot_route = jnp.sum(route_back[:, 1:, :], axis=0)
    gate_weight_grad = scatter_routes(
        all_hit, all_sel, jnp.concatenate([cold_back, hot_route], axis=0)
    )
    return (
        grad_gate_cold[None].astype(jnp.bfloat16),
        grad_up_cold[None].astype(jnp.bfloat16),
        grad_down_cold[None].astype(jnp.bfloat16),
        grad_gate_hot,
        grad_up_hot,
        grad_down_hot,
        gate_weight_grad,
    )


def solution(mesh):
    in_specs = (
        P("ep", "grp"),
        P("ep", "grp"),
        P("ep", None),
        P("ep", None),
        P(),
        P("ep", "grp", None),
        P("ep", "grp", None),
        P("ep", None, "grp"),
        P(None, "grp", "ep"),
        P(None, "grp", "ep"),
        P(None, "ep", "grp"),
    )
    out_specs = (
        P("ep", "grp", None),
        P("ep", "grp", None),
        P("ep", None, "grp"),
        P(None, "grp", "ep"),
        P(None, "grp", "ep"),
        P(None, "ep", "grp"),
        P("ep", None),
    )
    return jax.shard_map(body, mesh=mesh, in_specs=in_specs, out_specs=out_specs, check_vma=False)
```

```python
import jax
import jax.numpy as jnp
from jax import lax
from jax.sharding import PartitionSpec as P


def token_table(expert_ids, targets, capacity):
    hit = expert_ids.T[:, None, :] == targets[None, :, None]
    tok_hit = jnp.any(hit, axis=0)
    rank = jnp.cumsum(tok_hit.astype(jnp.int32), axis=1) - 1
    slots = jnp.arange(capacity, dtype=jnp.int32)
    sel = (rank[:, None, :] == slots[None, :, None]) & tok_hit[:, None, :]
    return hit, sel


def gather_rows(hit, sel, tokens, cotangent, gate_weights):
    count, capacity = sel.shape[0], sel.shape[1]
    token_map = sel.reshape(count * capacity, -1).astype(jnp.bfloat16)
    feat_rows = jnp.dot(token_map, tokens, preferred_element_type=jnp.float32).astype(jnp.bfloat16)
    cotan_rows = jnp.dot(token_map, cotangent, preferred_element_type=jnp.float32).astype(
        jnp.bfloat16
    )
    per_token = jnp.sum(
        jnp.where(hit, gate_weights.T.astype(jnp.float32)[:, None, :], 0.0), axis=0
    )
    scale = jnp.sum(jnp.where(sel, per_token[:, None, :], 0.0), axis=2)
    return feat_rows, cotan_rows, scale.reshape(-1).astype(jnp.bfloat16)


def scatter_routes(hit, sel, values):
    per_token = jnp.sum(jnp.where(sel, values[:, :, None], 0.0), axis=1)
    return jnp.sum(jnp.where(hit, per_token[None, :, :], 0.0), axis=1).T


def swiglu_back(pre_gate, pre_up, grad_hidden):
    sigmoid_gate = jax.nn.sigmoid(pre_gate)
    activated = pre_gate * sigmoid_gate
    hidden = (activated * pre_up).astype(jnp.bfloat16)
    back_gate = (
        grad_hidden * pre_up * sigmoid_gate * (1.0 + pre_gate * (1.0 - sigmoid_gate))
    ).astype(jnp.bfloat16)
    back_up = (grad_hidden * activated).astype(jnp.bfloat16)
    return (hidden, back_gate, back_up)


def grp_sum_f32(x, axis_name):
    size = lax.axis_size(axis_name)
    if size & (size - 1):
        return lax.psum(x, axis_name)
    bit = 1
    while bit < size:
        partner = [(i, i ^ bit) for i in range(size)]
        x = x + lax.ppermute(x, axis_name, partner)
        bit *= 2
    return x


def grp_sum_doubling(parts, axis_name):
    size = lax.axis_size(axis_name)
    mine = [p.astype(jnp.bfloat16) for p in parts]
    if size & (size - 1):
        return [lax.psum(r, axis_name).astype(jnp.float32) for r in mine]
    sums = [r.astype(jnp.float32) for r in mine]
    bit = 1
    while bit < size:
        partner = [(i, i ^ bit) for i in range(size)]
        got = lax.ppermute(mine, axis_name, partner)
        sums = [m.astype(jnp.float32) + g.astype(jnp.float32) for m, g in zip(mine, got)]
        mine = [s.astype(jnp.bfloat16) for s in sums]
        bit *= 2
    return sums


def grp_sum_rounded(parts, axes, axis_name):
    size = lax.axis_size(axis_name)
    rounded = [p.astype(jnp.bfloat16) for p in parts]
    if size == 1:
        return [r.astype(jnp.float32) for r in rounded]
    if size & (size - 1) or any(p.shape[a] % 2 for p, a in zip(parts, axes)):
        return [lax.psum(r, axis_name).astype(jnp.float32) for r in rounded]
    first_core = lax.axis_index(axis_name) % 2 == 0
    halves = [jnp.split(r, 2, axis=a) for r, a in zip(rounded, axes)]
    keep = [jnp.where(first_core, lo, hi) for lo, hi in halves]
    send = [jnp.where(first_core, hi, lo) for lo, hi in halves]
    swap = [(i, i ^ 1) for i in range(size)]
    got = lax.ppermute(send, axis_name, swap)
    sums = [k.astype(jnp.float32) + g.astype(jnp.float32) for k, g in zip(keep, got)]
    bit = 2
    while bit < size:
        partner = [(i, i ^ bit) for i in range(size)]
        mine = [s.astype(jnp.bfloat16) for s in sums]
        got = lax.ppermute(mine, axis_name, partner)
        sums = [m.astype(jnp.float32) + g.astype(jnp.float32) for m, g in zip(mine, got)]
        bit *= 2
    sums = [s.astype(jnp.bfloat16) for s in sums]
    other = lax.ppermute(sums, axis_name, swap)
    sums = [s.astype(jnp.float32) for s in sums]
    other = [o.astype(jnp.float32) for o in other]
    full = []
    for s, o, a in zip(sums, other, axes):
        first = jnp.where(first_core, s, o)
        second = jnp.where(first_core, o, s)
        full.append(jnp.concatenate([first, second], axis=a))
    return full


def body(
    tokens,
    cotangent,
    gate_weights,
    expert_ids,
    hot_ids,
    gate_cold,
    up_cold,
    down_cold,
    gate_hot,
    up_hot,
    down_hot,
):
    tok_rows, slice_width = tokens.shape
    top_count = expert_ids.shape[1]
    cold_count = lax.axis_size("ep")
    hot_count = hot_ids.shape[0]
    capacity = tok_rows // 16
    blocks = lax.axis_size("ep")
    targets = jnp.concatenate([jnp.arange(cold_count, dtype=jnp.int32), hot_ids])
    all_hit, all_sel = token_table(expert_ids, targets, capacity)
    feats_all, cotan_all, scale_all = gather_rows(all_hit, all_sel, tokens, cotangent, gate_weights)
    cold_total = cold_count * capacity
    hot_feats, hot_cotan, hot_scale = (
        feats_all[cold_total:],
        cotan_all[cold_total:],
        scale_all[cold_total:],
    )
    cold_feats, cold_cotan, cold_scale = (
        feats_all[:cold_total],
        cotan_all[:cold_total],
        scale_all[:cold_total],
    )
    hot_rows = hot_count * capacity
    hot_outgoing = jnp.concatenate([hot_feats, hot_cotan], axis=0)
    gathered = lax.all_gather(hot_outgoing, "ep", axis=0, tiled=False)
    scale_width = capacity + hot_rows
    cold_lines = -(-scale_width // slice_width)
    cold_lines = -(-cold_lines // 8) * 8
    both_scales = jnp.concatenate(
        [
            cold_scale.reshape(cold_count, capacity),
            jnp.broadcast_to(hot_scale[None, :], (cold_count, hot_rows)),
        ],
        axis=1,
    )
    cold_scale_block = jnp.pad(
        both_scales, ((0, 0), (0, cold_lines * slice_width - scale_width))
    ).reshape(cold_count, cold_lines, slice_width)
    outgoing = jnp.concatenate(
        [
            cold_feats.reshape(cold_count, capacity, slice_width),
            cold_cotan.reshape(cold_count, capacity, slice_width),
            cold_scale_block,
        ],
        axis=1,
    )
    received = lax.all_to_all(outgoing, "ep", split_axis=0, concat_axis=0, tiled=True)
    recv_feats = received[:, :capacity].reshape(-1, slice_width)
    recv_cotan = received[:, capacity : 2 * capacity].reshape(-1, slice_width)
    recv_scales = received[:, 2 * capacity :].reshape(cold_count, -1)
    recv_scale = recv_scales[:, :capacity]
    weighted = (
        recv_scale.reshape(-1, 1).astype(jnp.float32) * recv_cotan.astype(jnp.float32)
    ).astype(jnp.bfloat16)
    w_gate = gate_cold[0]
    w_up = up_cold[0]
    w_down = down_cold[0]
    part_gate = jnp.dot(recv_feats, w_gate, preferred_element_type=jnp.float32)
    part_up = jnp.dot(recv_feats, w_up, preferred_element_type=jnp.float32)
    part_hidden = lax.dot_general(
        weighted, w_down, (((1,), (1,)), ((), ())), preferred_element_type=jnp.float32
    )
    all_rows = gathered[:, : 2 * hot_rows].reshape(blocks, 2, hot_count, capacity, slice_width)
    all_rows = jnp.transpose(all_rows, (1, 2, 0, 3, 4)).reshape(
        2, hot_count, blocks * capacity, slice_width
    )
    all_scale = recv_scales[:, capacity:scale_width]
    all_scale = jnp.transpose(all_scale.reshape(blocks, hot_count, capacity), (1, 0, 2))
    rows_feat, rows_cot = all_rows[0], all_rows[1]
    rows_wt = (
        all_scale.reshape(hot_count, blocks * capacity, 1).astype(jnp.float32)
        * rows_cot.astype(jnp.float32)
    ).astype(jnp.bfloat16)
    part_gate_hot = jnp.einsum(
        "jrd,jdh->jrh", rows_feat, gate_hot, preferred_element_type=jnp.float32
    )
    part_up_hot = jnp.einsum("jrd,jdh->jrh", rows_feat, up_hot, preferred_element_type=jnp.float32)
    part_hidden_hot = jnp.einsum(
        "jrd,jhd->jrh", rows_wt, down_hot, preferred_element_type=jnp.float32
    )
    part_cot_hot = jnp.einsum(
        "jrd,jhd->jrh", rows_cot, down_hot, preferred_element_type=jnp.float32
    )
    pre_gate, pre_up, grad_hidden = grp_sum_rounded(
        [part_gate, part_up, part_hidden], [0, 0, 0], "grp"
    )
    pre_gate_hot, pre_up_hot, grad_hidden_hot, cot_down = grp_sum_doubling(
        [part_gate_hot, part_up_hot, part_hidden_hot, part_cot_hot], "grp"
    )
    hidden, back_gate, back_up = swiglu_back(pre_gate, pre_up, grad_hidden)
    output_slice = jnp.dot(hidden, w_down, preferred_element_type=jnp.float32)
    cold_route = jnp.sum(output_slice * recv_cotan.astype(jnp.float32), axis=1)
    cold_route = grp_sum_f32(cold_route.reshape(cold_count, 1, capacity), "grp")
    contract_rows = (((0,), (0,)), ((), ()))
    grad_gate_cold = lax.dot_general(
        recv_feats, back_gate, contract_rows, preferred_element_type=jnp.float32
    )
    grad_up_cold = lax.dot_general(
        recv_feats, back_up, contract_rows, preferred_element_type=jnp.float32
    )
    grad_down_cold = lax.dot_general(
        hidden, weighted, contract_rows, preferred_element_type=jnp.float32
    )
    hidden_hot, back_gate_hot, back_up_hot = swiglu_back(pre_gate_hot, pre_up_hot, grad_hidden_hot)
    hot_route_part = jnp.sum(hidden_hot.astype(jnp.float32) * cot_down, axis=2)
    grad_gate_hot = jnp.einsum(
        "jrd,jrh->jdh", rows_feat, back_gate_hot, preferred_element_type=jnp.float32
    )
    grad_up_hot = jnp.einsum("jrd,jrh->jdh", rows_feat, back_up_hot, preferred_element_type=jnp.float32)
    grad_down_hot = jnp.einsum(
        "jrh,jrd->jhd", hidden_hot, rows_wt, preferred_element_type=jnp.float32
    )
    route_parts = jnp.concatenate(
        [
            cold_route,
            jnp.transpose(hot_route_part.reshape(hot_count, blocks, capacity), (1, 0, 2)),
        ],
        axis=1,
    )
    route_back = lax.all_to_all(route_parts, "ep", split_axis=0, concat_axis=0, tiled=True)
    cold_back = route_back[:, 0, :]
    hot_route = jnp.sum(route_back[:, 1:, :], axis=0)
    gate_weight_grad = scatter_routes(
        all_hit, all_sel, jnp.concatenate([cold_back, hot_route], axis=0)
    )
    return (
        grad_gate_cold[None].astype(jnp.bfloat16),
        grad_up_cold[None].astype(jnp.bfloat16),
        grad_down_cold[None].astype(jnp.bfloat16),
        grad_gate_hot,
        grad_up_hot,
        grad_down_hot,
        gate_weight_grad,
    )


def solution(mesh):
    in_specs = (
        P("ep", "grp"),
        P("ep", "grp"),
        P("ep", None),
        P("ep", None),
        P(),
        P("ep", "grp", None),
        P("ep", "grp", None),
        P("ep", None, "grp"),
        P(None, "grp", "ep"),
        P(None, "grp", "ep"),
        P(None, "ep", "grp"),
    )
    out_specs = (
        P("ep", "grp", None),
        P("ep", "grp", None),
        P("ep", None, "grp"),
        P(None, "grp", "ep"),
        P(None, "grp", "ep"),
        P(None, "ep", "grp"),
        P("ep", None),
    )
    return jax.shard_map(body, mesh=mesh, in_specs=in_specs, out_specs=out_specs, check_vma=False)
```

```python
import jax
import jax.numpy as jnp
from jax import lax
from jax.sharding import PartitionSpec as P


def token_table(expert_ids, targets, capacity):
    hit = expert_ids.T[:, None, :] == targets[None, :, None]
    tok_hit = jnp.any(hit, axis=0)
    rank = jnp.cumsum(tok_hit.astype(jnp.int32), axis=1) - 1
    slots = jnp.arange(capacity, dtype=jnp.int32)
    sel = (rank[:, None, :] == slots[None, :, None]) & tok_hit[:, None, :]
    return hit, sel


def gather_rows(hit, sel, tokens, cotangent, gate_weights):
    count, capacity = sel.shape[0], sel.shape[1]
    token_map = sel.reshape(count * capacity, -1).astype(jnp.bfloat16)
    feat_rows = jnp.dot(token_map, tokens, preferred_element_type=jnp.float32).astype(jnp.bfloat16)
    cotan_rows = jnp.dot(token_map, cotangent, preferred_element_type=jnp.float32).astype(
        jnp.bfloat16
    )
    per_token = jnp.sum(
        jnp.where(hit, gate_weights.T.astype(jnp.float32)[:, None, :], 0.0), axis=0
    )
    scale = jnp.sum(jnp.where(sel, per_token[:, None, :], 0.0), axis=2)
    return feat_rows, cotan_rows, scale.reshape(-1).astype(jnp.bfloat16)


def scatter_routes(hit, sel, values):
    per_token = jnp.sum(jnp.where(sel, values[:, :, None], 0.0), axis=1)
    return jnp.sum(jnp.where(hit, per_token[None, :, :], 0.0), axis=1).T


def swiglu_back(pre_gate, pre_up, grad_hidden):
    sigmoid_gate = jax.nn.sigmoid(pre_gate)
    activated = pre_gate * sigmoid_gate
    hidden = (activated * pre_up).astype(jnp.bfloat16)
    back_gate = (
        grad_hidden * pre_up * sigmoid_gate * (1.0 + pre_gate * (1.0 - sigmoid_gate))
    ).astype(jnp.bfloat16)
    back_up = (grad_hidden * activated).astype(jnp.bfloat16)
    return (hidden, back_gate, back_up)


def grp_sum_f32(x, axis_name):
    size = lax.axis_size(axis_name)
    if size & (size - 1):
        return lax.psum(x, axis_name)
    bit = 1
    while bit < size:
        partner = [(i, i ^ bit) for i in range(size)]
        x = x + lax.ppermute(x, axis_name, partner)
        bit *= 2
    return x


def grp_sum_doubling(parts, axis_name):
    size = lax.axis_size(axis_name)
    mine = [p.astype(jnp.bfloat16) for p in parts]
    if size & (size - 1):
        return [lax.psum(r, axis_name).astype(jnp.float32) for r in mine]
    sums = [r.astype(jnp.float32) for r in mine]
    bit = 1
    while bit < size:
        partner = [(i, i ^ bit) for i in range(size)]
        got = lax.ppermute(mine, axis_name, partner)
        sums = [m.astype(jnp.float32) + g.astype(jnp.float32) for m, g in zip(mine, got)]
        mine = [s.astype(jnp.bfloat16) for s in sums]
        bit *= 2
    return sums


def grp_sum_rounded(parts, axes, axis_name):
    size = lax.axis_size(axis_name)
    rounded = [p.astype(jnp.bfloat16) for p in parts]
    if size == 1:
        return [r.astype(jnp.float32) for r in rounded]
    if size & (size - 1) or any(p.shape[a] % 2 for p, a in zip(parts, axes)):
        return [lax.psum(r, axis_name).astype(jnp.float32) for r in rounded]
    first_core = lax.axis_index(axis_name) % 2 == 0
    halves = [jnp.split(r, 2, axis=a) for r, a in zip(rounded, axes)]
    keep = [jnp.where(first_core, lo, hi) for lo, hi in halves]
    send = [jnp.where(first_core, hi, lo) for lo, hi in halves]
    swap = [(i, i ^ 1) for i in range(size)]
    got = lax.ppermute(send, axis_name, swap)
    sums = [k.astype(jnp.float32) + g.astype(jnp.float32) for k, g in zip(keep, got)]
    bit = 2
    while bit < size:
        partner = [(i, i ^ bit) for i in range(size)]
        mine = [s.astype(jnp.bfloat16) for s in sums]
        got = lax.ppermute(mine, axis_name, partner)
        sums = [m.astype(jnp.float32) + g.astype(jnp.float32) for m, g in zip(mine, got)]
        bit *= 2
    other = lax.ppermute(sums, axis_name, swap)
    full = []
    for s, o, a in zip(sums, other, axes):
        first = jnp.where(first_core, s, o)
        second = jnp.where(first_core, o, s)
        full.append(jnp.concatenate([first, second], axis=a))
    return full


def body(
    tokens,
    cotangent,
    gate_weights,
    expert_ids,
    hot_ids,
    gate_cold,
    up_cold,
    down_cold,
    gate_hot,
    up_hot,
    down_hot,
):
    tok_rows, slice_width = tokens.shape
    top_count = expert_ids.shape[1]
    cold_count = lax.axis_size("ep")
    hot_count = hot_ids.shape[0]
    capacity = tok_rows // 16
    blocks = lax.axis_size("ep")
    targets = jnp.concatenate([jnp.arange(cold_count, dtype=jnp.int32), hot_ids])
    all_hit, all_sel = token_table(expert_ids, targets, capacity)
    feats_all, cotan_all, scale_all = gather_rows(all_hit, all_sel, tokens, cotangent, gate_weights)
    cold_total = cold_count * capacity
    hot_feats, hot_cotan, hot_scale = (
        feats_all[cold_total:],
        cotan_all[cold_total:],
        scale_all[cold_total:],
    )
    cold_feats, cold_cotan, cold_scale = (
        feats_all[:cold_total],
        cotan_all[:cold_total],
        scale_all[:cold_total],
    )
    hot_rows = hot_count * capacity
    hot_outgoing = jnp.concatenate([hot_feats, hot_cotan], axis=0)
    gathered = lax.all_gather(hot_outgoing, "ep", axis=0, tiled=False)
    scale_width = capacity + hot_rows
    cold_lines = -(-scale_width // slice_width)
    both_scales = jnp.concatenate(
        [
            cold_scale.reshape(cold_count, capacity),
            jnp.broadcast_to(hot_scale[None, :], (cold_count, hot_rows)),
        ],
        axis=1,
    )
    cold_scale_block = jnp.pad(
        both_scales, ((0, 0), (0, cold_lines * slice_width - scale_width))
    ).reshape(cold_count, cold_lines, slice_width)
    outgoing = jnp.concatenate(
        [
            cold_feats.reshape(cold_count, capacity, slice_width),
            cold_cotan.reshape(cold_count, capacity, slice_width),
            cold_scale_block,
        ],
        axis=1,
    )
    received = lax.all_to_all(outgoing, "ep", split_axis=0, concat_axis=0, tiled=True)
    recv_feats = received[:, :capacity].reshape(-1, slice_width)
    recv_cotan = received[:, capacity : 2 * capacity].reshape(-1, slice_width)
    recv_scales = received[:, 2 * capacity :].reshape(cold_count, -1)
    recv_scale = recv_scales[:, :capacity]
    weighted = (
        recv_scale.reshape(-1, 1).astype(jnp.float32) * recv_cotan.astype(jnp.float32)
    ).astype(jnp.bfloat16)
    w_gate = gate_cold[0]
    w_up = up_cold[0]
    w_down = down_cold[0]
    part_gate = jnp.dot(recv_feats, w_gate, preferred_element_type=jnp.float32)
    part_up = jnp.dot(recv_feats, w_up, preferred_element_type=jnp.float32)
    part_hidden = lax.dot_general(
        weighted, w_down, (((1,), (1,)), ((), ())), preferred_element_type=jnp.float32
    )
    all_rows = gathered[:, : 2 * hot_rows].reshape(blocks, 2, hot_count, capacity, slice_width)
    all_rows = jnp.transpose(all_rows, (1, 2, 0, 3, 4)).reshape(
        2, hot_count, blocks * capacity, slice_width
    )
    all_scale = recv_scales[:, capacity:scale_width]
    all_scale = jnp.transpose(all_scale.reshape(blocks, hot_count, capacity), (1, 0, 2))
    rows_feat, rows_cot = all_rows[0], all_rows[1]
    rows_wt = (
        all_scale.reshape(hot_count, blocks * capacity, 1).astype(jnp.float32)
        * rows_cot.astype(jnp.float32)
    ).astype(jnp.bfloat16)
    part_gate_hot = jnp.einsum(
        "jrd,jdh->jrh", rows_feat, gate_hot, preferred_element_type=jnp.float32
    )
    part_up_hot = jnp.einsum("jrd,jdh->jrh", rows_feat, up_hot, preferred_element_type=jnp.float32)
    part_hidden_hot = jnp.einsum(
        "jrd,jhd->jrh", rows_wt, down_hot, preferred_element_type=jnp.float32
    )
    part_cot_hot = jnp.einsum(
        "jrd,jhd->jrh", rows_cot, down_hot, preferred_element_type=jnp.float32
    )
    pre_gate, pre_up, grad_hidden = grp_sum_rounded(
        [part_gate, part_up, part_hidden], [0, 0, 0], "grp"
    )
    pre_gate_hot, pre_up_hot, grad_hidden_hot, cot_down = grp_sum_doubling(
        [part_gate_hot, part_up_hot, part_hidden_hot, part_cot_hot], "grp"
    )
    hidden, back_gate, back_up = swiglu_back(pre_gate, pre_up, grad_hidden)
    output_slice = jnp.dot(hidden, w_down, preferred_element_type=jnp.float32)
    cold_route = jnp.sum(output_slice * recv_cotan.astype(jnp.float32), axis=1)
    cold_route = grp_sum_f32(cold_route.reshape(cold_count, 1, capacity), "grp")
    contract_rows = (((0,), (0,)), ((), ()))
    grad_gate_cold = lax.dot_general(
        recv_feats, back_gate, contract_rows, preferred_element_type=jnp.float32
    )
    grad_up_cold = lax.dot_general(
        recv_feats, back_up, contract_rows, preferred_element_type=jnp.float32
    )
    grad_down_cold = lax.dot_general(
        hidden, weighted, contract_rows, preferred_element_type=jnp.float32
    )
    hidden_hot, back_gate_hot, back_up_hot = swiglu_back(pre_gate_hot, pre_up_hot, grad_hidden_hot)
    hot_route_part = jnp.sum(hidden_hot.astype(jnp.float32) * cot_down, axis=2)
    grad_gate_hot = jnp.einsum(
        "jrd,jrh->jdh", rows_feat, back_gate_hot, preferred_element_type=jnp.float32
    )
    grad_up_hot = jnp.einsum("jrd,jrh->jdh", rows_feat, back_up_hot, preferred_element_type=jnp.float32)
    grad_down_hot = jnp.einsum(
        "jrh,jrd->jhd", hidden_hot, rows_wt, preferred_element_type=jnp.float32
    )
    route_parts = jnp.concatenate(
        [
            cold_route,
            jnp.transpose(hot_route_part.reshape(hot_count, blocks, capacity), (1, 0, 2)),
        ],
        axis=1,
    )
    route_back = lax.all_to_all(route_parts, "ep", split_axis=0, concat_axis=0, tiled=True)
    cold_back = route_back[:, 0, :]
    hot_route = jnp.sum(route_back[:, 1:, :], axis=0)
    gate_weight_grad = scatter_routes(
        all_hit, all_sel, jnp.concatenate([cold_back, hot_route], axis=0)
    )
    return (
        grad_gate_cold[None].astype(jnp.bfloat16),
        grad_up_cold[None].astype(jnp.bfloat16),
        grad_down_cold[None].astype(jnp.bfloat16),
        grad_gate_hot,
        grad_up_hot,
        grad_down_hot,
        gate_weight_grad,
    )


def solution(mesh):
    in_specs = (
        P("ep", "grp"),
        P("ep", "grp"),
        P("ep", None),
        P("ep", None),
        P(),
        P("ep", "grp", None),
        P("ep", "grp", None),
        P("ep", None, "grp"),
        P(None, "grp", "ep"),
        P(None, "grp", "ep"),
        P(None, "ep", "grp"),
    )
    out_specs = (
        P("ep", "grp", None),
        P("ep", "grp", None),
        P("ep", None, "grp"),
        P(None, "grp", "ep"),
        P(None, "grp", "ep"),
        P(None, "ep", "grp"),
        P("ep", None),
    )
    return jax.shard_map(body, mesh=mesh, in_specs=in_specs, out_specs=out_specs, check_vma=False)
```

```python
import jax
import jax.numpy as jnp
from jax import lax
from jax.sharding import PartitionSpec as P


def token_table(expert_ids, targets, capacity):
    hit = expert_ids.T[:, None, :] == targets[None, :, None]
    tok_hit = jnp.any(hit, axis=0)
    rank = jnp.cumsum(tok_hit.astype(jnp.int32), axis=1) - 1
    slots = jnp.arange(capacity, dtype=jnp.int32)
    sel = (rank[:, None, :] == slots[None, :, None]) & tok_hit[:, None, :]
    return hit, sel


def gather_rows(hit, sel, tokens, cotangent, gate_weights):
    count, capacity = sel.shape[0], sel.shape[1]
    token_map = sel.reshape(count * capacity, -1).astype(jnp.bfloat16)
    feat_rows = jnp.dot(token_map, tokens, preferred_element_type=jnp.float32).astype(jnp.bfloat16)
    cotan_rows = jnp.dot(token_map, cotangent, preferred_element_type=jnp.float32).astype(
        jnp.bfloat16
    )
    per_token = jnp.sum(
        jnp.where(hit, gate_weights.T.astype(jnp.float32)[:, None, :], 0.0), axis=0
    )
    scale = jnp.sum(jnp.where(sel, per_token[:, None, :], 0.0), axis=2)
    return feat_rows, cotan_rows, scale.reshape(-1).astype(jnp.bfloat16)


def scatter_routes(hit, sel, values):
    per_token = jnp.sum(jnp.where(sel, values[:, :, None], 0.0), axis=1)
    return jnp.sum(jnp.where(hit, per_token[None, :, :], 0.0), axis=1).T


def swiglu_back(pre_gate, pre_up, grad_hidden):
    sigmoid_gate = jax.nn.sigmoid(pre_gate)
    activated = pre_gate * sigmoid_gate
    hidden = (activated * pre_up).astype(jnp.bfloat16)
    back_gate = (
        grad_hidden * pre_up * sigmoid_gate * (1.0 + pre_gate * (1.0 - sigmoid_gate))
    ).astype(jnp.bfloat16)
    back_up = (grad_hidden * activated).astype(jnp.bfloat16)
    return (hidden, back_gate, back_up)


def grp_sum_f32(x, axis_name):
    size = lax.axis_size(axis_name)
    if size & (size - 1):
        return lax.psum(x, axis_name)
    bit = 1
    while bit < size:
        partner = [(i, i ^ bit) for i in range(size)]
        x = x + lax.ppermute(x, axis_name, partner)
        bit *= 2
    return x


def grp_sum_doubling(parts, axis_name):
    size = lax.axis_size(axis_name)
    mine = [p.astype(jnp.bfloat16) for p in parts]
    if size & (size - 1):
        return [lax.psum(r, axis_name).astype(jnp.float32) for r in mine]
    sums = [r.astype(jnp.float32) for r in mine]
    bit = 1
    while bit < size:
        partner = [(i, i ^ bit) for i in range(size)]
        got = lax.ppermute(mine, axis_name, partner)
        sums = [m.astype(jnp.float32) + g.astype(jnp.float32) for m, g in zip(mine, got)]
        mine = [s.astype(jnp.bfloat16) for s in sums]
        bit *= 2
    return sums


def grp_sum_rounded(parts, axes, axis_name):
    size = lax.axis_size(axis_name)
    rounded = [p.astype(jnp.bfloat16) for p in parts]
    if size == 1:
        return [r.astype(jnp.float32) for r in rounded]
    if size & (size - 1) or any(p.shape[a] % 2 for p, a in zip(parts, axes)):
        return [lax.psum(r, axis_name).astype(jnp.float32) for r in rounded]
    first_core = lax.axis_index(axis_name) % 2 == 0
    halves = [jnp.split(r, 2, axis=a) for r, a in zip(rounded, axes)]
    keep = [jnp.where(first_core, lo, hi) for lo, hi in halves]
    send = [jnp.where(first_core, hi, lo) for lo, hi in halves]
    swap = [(i, i ^ 1) for i in range(size)]
    got = lax.ppermute(send, axis_name, swap)
    sums = [k.astype(jnp.float32) + g.astype(jnp.float32) for k, g in zip(keep, got)]
    bit = 2
    while bit < size:
        partner = [(i, i ^ bit) for i in range(size)]
        mine = [s.astype(jnp.bfloat16) for s in sums]
        got = lax.ppermute(mine, axis_name, partner)
        sums = [m.astype(jnp.float32) + g.astype(jnp.float32) for m, g in zip(mine, got)]
        bit *= 2
    sums = [s.astype(jnp.bfloat16) for s in sums]
    other = lax.ppermute(sums, axis_name, swap)
    sums = [s.astype(jnp.float32) for s in sums]
    other = [o.astype(jnp.float32) for o in other]
    full = []
    for s, o, a in zip(sums, other, axes):
        first = jnp.where(first_core, s, o)
        second = jnp.where(first_core, o, s)
        full.append(jnp.concatenate([first, second], axis=a))
    return full


def body(
    tokens,
    cotangent,
    gate_weights,
    expert_ids,
    hot_ids,
    gate_cold,
    up_cold,
    down_cold,
    gate_hot,
    up_hot,
    down_hot,
):
    tok_rows, slice_width = tokens.shape
    top_count = expert_ids.shape[1]
    cold_count = lax.axis_size("ep")
    hot_count = hot_ids.shape[0]
    capacity = tok_rows // 16
    blocks = lax.axis_size("ep")
    targets = jnp.concatenate([jnp.arange(cold_count, dtype=jnp.int32), hot_ids])
    all_hit, all_sel = token_table(expert_ids, targets, capacity)
    feats_all, cotan_all, scale_all = gather_rows(all_hit, all_sel, tokens, cotangent, gate_weights)
    cold_total = cold_count * capacity
    hot_feats, hot_cotan, hot_scale = (
        feats_all[cold_total:],
        cotan_all[cold_total:],
        scale_all[cold_total:],
    )
    cold_feats, cold_cotan, cold_scale = (
        feats_all[:cold_total],
        cotan_all[:cold_total],
        scale_all[:cold_total],
    )
    hot_rows = hot_count * capacity
    hot_outgoing = jnp.concatenate([hot_feats, hot_cotan], axis=0)
    gathered = lax.all_gather(hot_outgoing, "ep", axis=0, tiled=False)
    scale_width = capacity + hot_rows
    cold_lines = -(-scale_width // slice_width)
    both_scales = jnp.concatenate(
        [
            cold_scale.reshape(cold_count, capacity),
            jnp.broadcast_to(hot_scale[None, :], (cold_count, hot_rows)),
        ],
        axis=1,
    )
    cold_scale_block = jnp.pad(
        both_scales, ((0, 0), (0, cold_lines * slice_width - scale_width))
    ).reshape(cold_count, cold_lines, slice_width)
    outgoing = jnp.concatenate(
        [
            cold_feats.reshape(cold_count, capacity, slice_width),
            cold_cotan.reshape(cold_count, capacity, slice_width),
            cold_scale_block,
        ],
        axis=1,
    )
    received = lax.all_to_all(outgoing, "ep", split_axis=0, concat_axis=0, tiled=True)
    recv_feats = received[:, :capacity].reshape(-1, slice_width)
    recv_cotan = received[:, capacity : 2 * capacity].reshape(-1, slice_width)
    recv_scales = received[:, 2 * capacity :].reshape(cold_count, -1)
    recv_scale = recv_scales[:, :capacity]
    weighted = (
        recv_scale.reshape(-1, 1).astype(jnp.float32) * recv_cotan.astype(jnp.float32)
    ).astype(jnp.bfloat16)
    w_gate = gate_cold[0]
    w_up = up_cold[0]
    w_down = down_cold[0]
    part_gate = jnp.dot(recv_feats, w_gate, preferred_element_type=jnp.float32)
    part_up = jnp.dot(recv_feats, w_up, preferred_element_type=jnp.float32)
    part_hidden = lax.dot_general(
        weighted, w_down, (((1,), (1,)), ((), ())), preferred_element_type=jnp.float32
    )
    all_rows = gathered[:, : 2 * hot_rows].reshape(blocks, 2, hot_count, capacity, slice_width)
    all_rows = jnp.transpose(all_rows, (1, 2, 0, 3, 4)).reshape(
        2, hot_count, blocks * capacity, slice_width
    )
    all_scale = recv_scales[:, capacity:scale_width]
    all_scale = jnp.transpose(all_scale.reshape(blocks, hot_count, capacity), (1, 0, 2))
    rows_feat, rows_cot = all_rows[0], all_rows[1]
    rows_wt = (
        all_scale.reshape(hot_count, blocks * capacity, 1).astype(jnp.float32)
        * rows_cot.astype(jnp.float32)
    ).astype(jnp.bfloat16)
    part_gate_hot = jnp.einsum(
        "jrd,jdh->jrh", rows_feat, gate_hot, preferred_element_type=jnp.float32
    )
    part_up_hot = jnp.einsum("jrd,jdh->jrh", rows_feat, up_hot, preferred_element_type=jnp.float32)
    part_hidden_hot = jnp.einsum(
        "jrd,jhd->jrh", rows_wt, down_hot, preferred_element_type=jnp.float32
    )
    part_cot_hot = jnp.einsum(
        "jrd,jhd->jrh", rows_cot, down_hot, preferred_element_type=jnp.float32
    )
    pre_gate, pre_up, grad_hidden = grp_sum_rounded(
        [part_gate, part_up, part_hidden], [0, 0, 0], "grp"
    )
    pre_gate_hot, pre_up_hot, grad_hidden_hot, cot_down = grp_sum_doubling(
        [part_gate_hot, part_up_hot, part_hidden_hot, part_cot_hot], "grp"
    )
    hidden, back_gate, back_up = swiglu_back(pre_gate, pre_up, grad_hidden)
    output_slice = jnp.dot(hidden, w_down, preferred_element_type=jnp.float32)
    cold_route = jnp.sum(output_slice * recv_cotan.astype(jnp.float32), axis=1)
    cold_route = grp_sum_f32(cold_route.reshape(cold_count, 1, capacity), "grp")
    contract_rows = (((0,), (0,)), ((), ()))
    grad_gate_cold = lax.dot_general(
        recv_feats, back_gate, contract_rows, preferred_element_type=jnp.float32
    )
    grad_up_cold = lax.dot_general(
        recv_feats, back_up, contract_rows, preferred_element_type=jnp.float32
    )
    grad_down_cold = lax.dot_general(
        hidden, weighted, contract_rows, preferred_element_type=jnp.float32
    )
    hidden_hot, back_gate_hot, back_up_hot = swiglu_back(pre_gate_hot, pre_up_hot, grad_hidden_hot)
    hot_route_part = jnp.sum(hidden_hot.astype(jnp.float32) * cot_down, axis=2)
    grad_gate_hot = jnp.einsum(
        "jrd,jrh->jdh", rows_feat, back_gate_hot, preferred_element_type=jnp.float32
    )
    grad_up_hot = jnp.einsum("jrd,jrh->jdh", rows_feat, back_up_hot, preferred_element_type=jnp.float32)
    grad_down_hot = jnp.einsum(
        "jrh,jrd->jhd", hidden_hot, rows_wt, preferred_element_type=jnp.float32
    )
    route_parts = jnp.concatenate(
        [
            cold_route,
            jnp.transpose(hot_route_part.reshape(hot_count, blocks, capacity), (1, 0, 2)),
        ],
        axis=1,
    )
    route_back = lax.all_to_all(route_parts, "ep", split_axis=0, concat_axis=0, tiled=True)
    cold_back = route_back[:, 0, :]
    hot_route = jnp.sum(route_back[:, 1:, :], axis=0)
    gate_weight_grad = scatter_routes(
        all_hit, all_sel, jnp.concatenate([cold_back, hot_route], axis=0)
    )
    return (
        grad_gate_cold[None].astype(jnp.bfloat16),
        grad_up_cold[None].astype(jnp.bfloat16),
        grad_down_cold[None].astype(jnp.bfloat16),
        grad_gate_hot,
        grad_up_hot,
        grad_down_hot,
        gate_weight_grad,
    )


def solution(mesh):
    in_specs = (
        P("ep", "grp"),
        P("ep", "grp"),
        P("ep", None),
        P("ep", None),
        P(),
        P("ep", "grp", None),
        P("ep", "grp", None),
        P("ep", None, "grp"),
        P(None, "grp", "ep"),
        P(None, "grp", "ep"),
        P(None, "ep", "grp"),
    )
    out_specs = (
        P("ep", "grp", None),
        P("ep", "grp", None),
        P("ep", None, "grp"),
        P(None, "grp", "ep"),
        P(None, "grp", "ep"),
        P(None, "ep", "grp"),
        P("ep", None),
    )
    return jax.shard_map(body, mesh=mesh, in_specs=in_specs, out_specs=out_specs, check_vma=False)
```
